256 devices in a mesh: grp: 4 (over x_lo, core), gx: 16 (over z, x_hi), gy: 4 (over y).
Axes of the slice: x: 4 (x_hi: 2, x_lo: 2; x = x_hi * 2 + x_lo), y: 4, z: 8, core: 2. Of those that a mesh axis runs over, the one named last changes fastest.
Arguments:
- conc: float32 [4, 32, 1024, 1024], P('grp', None, 'gx', 'gy'), may hold values from 0 to 1
- velocity: bfloat16 [3, 4, 32, 1024, 1024], P(None, 'grp', None, 'gx', 'gy'), may hold values from -0.119628906 to 0.119628906
- porosity: bfloat16 [4, 32, 1024, 1024], P('grp', None, 'gx', 'gy'), may hold values from 0.099609375 to 0.3984375
- saturation: bfloat16 [4, 32, 1024, 1024], P('grp', None, 'gx', 'gy'), may hold values from 0.29882812 to 1
- layer_counts: int32 [8], replicated, may hold values from 1 to 24, 96 in all
- electrodes: int32 [4, 2], replicated, may hold values from 0 to 2097151
- init_potential: float32 [4, 8, 512, 512], P(None, None, 'gx', 'gy'), may hold values from -6 to 6
Outputs:
- conc_next: float32 [4, 32, 1024, 1024], P('grp', None, 'gx', 'gy')
- conductivity: float32 [8, 512, 512], P(None, 'gx', 'gy')
- potential: float32 [4, 8, 512, 512], P('grp', None, 'gx', 'gy')
The draws below stay inside these ranges and needn't reach their ends.
Inputs may be any that keep to these rules, and one draw needn't show every extreme that they name: layer_counts sums to 96; its largest entry is exactly 24.
All inputs are finite; a program needn't handle non-finite values.
Results may differ from the reference program's by a relative error of at most 0.0014.
Values may be sent and summed in bfloat16 or wider, within the bound.
No kernel may reach another device: no remote copies, remote signals or barrier semaphores. Data moves between devices by JAX's collectives and lax.ppermute only.
A program may use at most 128 MiB of HBM per device.

```python
import math
import jax
import jax.numpy as jnp
import numpy as np
from jax import lax

ZL = 32
ZE = 8
SRC = 4
SWEEPS = 3
ZT = 96
NX = 1024
NY = 1024
EXG = 512
EYG = 512


def touch_ends(entries, rng, least, high):
    index_at = [jax.random.randint(jax.random.fold_in(rng, axis), (), 0, length) for axis, length in enumerate(entries.shape)]
    main_axis = entries.shape.index(max(entries.shape))
    next_to = index_at[:main_axis] + [(index_at[main_axis] + 1) % entries.shape[main_axis]] + index_at[main_axis + 1:]
    return entries.at[tuple(index_at)].set(least).at[tuple(next_to)].set(high)


def steps_of(rng, shape, shards, low, largest):
    gain = 1.0
    for dim, shards_of in shards:
        draws = jax.random.uniform(jax.random.fold_in(jax.random.fold_in(rng, 6), dim), (shards_of,), jnp.float32, low / len(shards), largest / len(shards))
        gain = gain * jnp.repeat(jnp.exp(draws), shape[dim] // shards_of).reshape((-1,) + (1,) * (len(shape) - 1 - dim))
    return gain


def profile(number_of, total, limit, lean):
    portions = [(1 << 20) // math.isqrt(rank ** lean) + 1 for rank in range(2, number_of + 1)]
    surplus, holding = total - limit - (number_of - 1), [1] * (number_of - 1)
    while surplus > 0:
        free = [i for i in range(number_of - 1) if holding[i] < limit]
        pool, remaining = sum([portions[i] for i in free]), surplus
        for i in free:
            more = min(limit - holding[i], max(1, remaining * portions[i] // pool), surplus)
            holding[i] = holding[i] + more
            surplus = surplus - more
    return np.array([limit] + holding)


def ragged(key, number_of, total, reach, slope):
    if number_of == 2:
        one = jax.random.randint(key, (), max(1, total - reach), min(reach, total - 1) + 1)
        return jnp.stack([one, total - one])
    sizes = jnp.asarray(profile(number_of, total, reach, slope), jnp.int32)
    couples = (number_of - 1) // 2
    source_of, taker = sizes[1:1 + 2 * couples:2], sizes[2:2 + 2 * couples:2]
    slack = jnp.minimum(source_of - 1, reach - taker)
    passed = jax.random.randint(jax.random.fold_in(key, 1), (couples,), 0, 1 << 20) % (slack + 1)
    sizes = sizes.at[1:1 + 2 * couples:2].set(source_of - passed).at[2:2 + 2 * couples:2].set(taker + passed)
    return sizes[jax.random.permutation(jax.random.fold_in(key, 2), number_of)]


def noise(key, shape, deviation, limit, cuts=(), held_as=jnp.bfloat16):
    factor_of = steps_of(key, shape, cuts, -0.22, 0.18) if cuts else 1.0
    result = jax.random.normal(key, shape, jnp.float32) * deviation * factor_of
    return jnp.minimum(jnp.maximum(result, -limit), limit).astype(held_as)


def setup_inputs(seed: int = 0) -> dict:
    streams_of = jax.random.split(jax.random.key(seed), 8)
    conc = jnp.clip(1.0 * jax.random.uniform(streams_of[0], (4, ZL, NX, NY), jnp.float32) ** steps_of(streams_of[0], (4, ZL, NX, NY), ((0, 4), (2, 16), (3, 4)), -0.2, 0.2), 0.0, 1.0)
    velocity = jnp.clip(jax.random.uniform(streams_of[1], (3, 4, ZL, NX, NY), jnp.float32, -0.119628906, 0.119628906) * steps_of(streams_of[1], (3, 4, ZL, NX, NY), ((1, 4), (3, 16), (4, 4)), -0.4, 0.0), -0.119628906, 0.119628906).astype(jnp.bfloat16)
    porosity = jnp.clip(jnp.exp(math.log(0.3984375) - 1.3862944 * jax.random.uniform(streams_of[2], (4, ZL, NX, NY), jnp.float32) ** steps_of(streams_of[2], (4, ZL, NX, NY), ((0, 4), (2, 16), (3, 4)), -0.2, 0.2)), 0.099609375, 0.3984375).astype(jnp.bfloat16)
    saturation = jnp.clip(0.29882812 + 0.7011719 * jax.random.uniform(streams_of[3], (4, ZL, NX, NY), jnp.float32) ** steps_of(streams_of[3], (4, ZL, NX, NY), ((0, 4), (2, 16), (3, 4)), -0.2, 0.2), 0.29882812, 1.0).astype(jnp.bfloat16)
    layer_counts = ragged(streams_of[4], ZE, ZT, 2 * ZT // ZE, 1).astype(jnp.int32)
    electrodes = touch_ends(jax.random.randint(streams_of[5], (SRC, 2), 0, ZE * EXG * EYG), jax.random.fold_in(streams_of[5], 1), 0, (ZE * EXG * EYG) - 1).astype(jnp.int32)
    init_potential = noise(streams_of[6], (SRC, ZE, EXG, EYG), 1.0, 6.0, ((2, 16), (3, 4)), jnp.float32)
    return {"conc": conc, "velocity": velocity, "porosity": porosity, "saturation": saturation, "layer_counts": layer_counts, "electrodes": electrodes, "init_potential": init_potential}


KAPPA = 0.06
OMEGA = 0.8
AMPLITUDE = 40.0
ARCHIE = 20.0


def neighbours(padded, direction_index):
    leading = [slice(None)] * (padded.ndim - 3)
    middle = [slice(1, -1)] * 3
    below_slices = list(middle)
    below_slices[direction_index] = slice(0, -2)
    above_slices = list(middle)
    above_slices[direction_index] = slice(2, None)
    return padded[tuple(leading + below_slices)], padded[tuple(leading + above_slices)]


def tendency(padded, speeds):
    center = padded[1:-1, 1:-1, 1:-1]
    running = -6.0 * KAPPA * center
    for direction_index in range(3):
        below_cells, above_cells = neighbours(padded, direction_index)
        speed_comp = speeds[direction_index]
        running = running + KAPPA * (below_cells + above_cells) - (jnp.maximum(speed_comp, 0.0) * (center - below_cells) + jnp.minimum(speed_comp, 0.0) * (above_cells - center))
    return running


def reference(conc, velocity, porosity, saturation, layer_counts, electrodes, init_potential):
    field = conc[:3].reshape(ZT, NX, NY)
    speeds = velocity[:, :3].reshape(3, ZT, NX, NY).astype(jnp.float32)
    section_one = field + tendency(jnp.pad(field, 1), speeds)
    advanced = 0.5 * (field + section_one + tendency(jnp.pad(section_one, 1), speeds))
    conc_next = jnp.concatenate([advanced.reshape(3, ZL, NX, NY), jnp.zeros((1, ZL, NX, NY), jnp.float32)], 0)
    poro = porosity[:3].reshape(ZT, NX, NY).astype(jnp.float32)
    water = saturation[:3].reshape(ZT, NX, NY).astype(jnp.float32)
    sigma = ARCHIE * jnp.exp(advanced) * poro * poro * water * water
    coarse = sigma.reshape(ZT, EXG, 2, EYG, 2).sum(axis=(2, 4))
    ends = jnp.cumsum(layer_counts).astype(jnp.int32)
    starts = ends - layer_counts
    layer_ids = jnp.arange(ZT, dtype=jnp.int32)
    member = ((layer_ids[None, :] >= starts[:, None]) & (layer_ids[None, :] < ends[:, None])).astype(jnp.float32)
    weights = member / (4.0 * layer_counts.astype(jnp.float32))[:, None]
    conductivity = jnp.dot(weights, coarse.reshape(ZT, EXG * EYG), precision=lax.Precision.HIGHEST).reshape(ZE, EXG, EYG)
    cond_wide = jnp.pad(conductivity, 1)
    faces = []
    diagonal = jnp.zeros_like(conductivity)
    for direction_index in range(3):
        below_cells, above_cells = neighbours(cond_wide, direction_index)
        face_below = 0.5 * (conductivity + below_cells)
        face_above = 0.5 * (conductivity + above_cells)
        faces.append((face_below, face_above))
        diagonal = diagonal + face_below + face_above
    flat_ids = jnp.arange(ZE * EXG * EYG, dtype=jnp.int32).reshape(ZE, EXG, EYG)
    source_terms = AMPLITUDE * ((flat_ids[None] == electrodes[:, 0, None, None, None]).astype(jnp.float32) - (flat_ids[None] == electrodes[:, 1, None, None, None]).astype(jnp.float32))
    potential = init_potential
    for sweep_index in range(SWEEPS):
        pot_wide = jnp.pad(potential, ((0, 0), (1, 1), (1, 1), (1, 1)))
        coupled = jnp.zeros_like(potential)
        for direction_index in range(3):
            below_cells, above_cells = neighbours(pot_wide, direction_index)
            coupled = coupled + faces[direction_index][0] * below_cells + faces[direction_index][1] * above_cells
        applied = diagonal * potential - coupled
        potential = potential + OMEGA * (source_terms - applied) / diagonal
    return conc_next, conductivity, potential
```

```python
import jax
import jax.numpy as jnp
from jax import lax
from jax.sharding import PartitionSpec as P

SWEEPS = 3


KAPPA = 0.06
OMEGA = 0.8
AMPLITUDE = 40.0
ARCHIE = 20.0


def with_halo(shard, sides, width, top=None):
    for axis, dim in sides:
        devices, length = (lax.axis_size(axis), shard.shape[dim])
        last_member = devices if (axis != "grp" or top is None) else top
        up = [(i, i + 1) for i in range(last_member - 1)]
        down = [(j, i) for i, j in up]
        last = lax.slice_in_dim(shard, length - width, length, axis=dim)
        initial = lax.slice_in_dim(shard, 0, width, axis=dim)
        before = lax.ppermute(last, axis, up)
        after = lax.ppermute(initial, axis, down)
        shard = jnp.concatenate([before, shard, after], axis=dim)
    return shard


def neighbours(padded, direction_index):
    leading = [slice(None)] * (padded.ndim - 3)
    middle = [slice(1, -1)] * 3
    below_slices = list(middle)
    below_slices[direction_index] = slice(0, -2)
    above_slices = list(middle)
    above_slices[direction_index] = slice(2, None)
    return (padded[tuple(leading + below_slices)], padded[tuple(leading + above_slices)])


def tendency(padded, speeds):
    center = padded[1:-1, 1:-1, 1:-1]
    running = -6.0 * KAPPA * center
    for direction_index in range(3):
        below_cells, above_cells = neighbours(padded, direction_index)
        speed_comp = speeds[direction_index]
        running = (
            running
            + KAPPA * (below_cells + above_cells)
            - (
                jnp.maximum(speed_comp, 0.0) * (center - below_cells)
                + jnp.minimum(speed_comp, 0.0) * (above_cells - center)
            )
        )
    return running


def inside(start, count, total):
    ids = start + jnp.arange(count, dtype=jnp.int32)
    return (ids >= 0) & (ids < total)


def grp_sum(partial):
    pair = lax.ppermute(partial, "grp", [(0, 1), (1, 0), (2, 3), (3, 2)])
    partial = partial + pair
    pair = lax.ppermute(partial, "grp", [(0, 2), (2, 0), (1, 3), (3, 1)])
    return partial + pair


def on_device(conc, velocity, porosity, saturation, layer_counts, electrodes, init_potential):
    group_index = lax.axis_index("grp")
    row_index = lax.axis_index("gx")
    column_index = lax.axis_index("gy")
    groups = lax.axis_size("grp")
    rows = lax.axis_size("gx")
    columns = lax.axis_size("gy")
    active = group_index < 3
    field = conc[0]
    layers, tile_x, tile_y = field.shape
    slabs = 3
    speeds = velocity[:, 0]

    field_wide = with_halo(field, (("grp", 0), ("gx", 1), ("gy", 2)), 2, top=slabs)
    speeds_wide = with_halo(speeds, (("grp", 1), ("gx", 2), ("gy", 3)), 1, top=slabs).astype(
        jnp.float32
    )

    section_wide = field_wide[1:-1, 1:-1, 1:-1] + tendency(field_wide, speeds_wide)
    keep = (
        inside(group_index * layers - 1, layers + 2, slabs * layers)[:, None, None]
        & inside(row_index * tile_x - 1, tile_x + 2, rows * tile_x)[None, :, None]
        & inside(column_index * tile_y - 1, tile_y + 2, columns * tile_y)[None, None, :]
    )
    section_wide = jnp.where(keep, section_wide, 0.0)
    advanced = 0.5 * (
        field
        + section_wide[1:-1, 1:-1, 1:-1]
        + tendency(section_wide, speeds_wide[:, 1:-1, 1:-1, 1:-1])
    )
    advanced = jnp.where(active, advanced, 0.0)

    poro = porosity[0].astype(jnp.float32)
    water = saturation[0].astype(jnp.float32)
    sigma = ARCHIE * jnp.exp(advanced) * poro * poro * water * water
    coarse_x = tile_x // 2
    coarse_y = tile_y // 2
    pool_y = (
        jnp.arange(tile_y, dtype=jnp.int32)[:, None] // 2
        == jnp.arange(coarse_y, dtype=jnp.int32)[None, :]
    ).astype(jnp.float32)
    half = jnp.einsum("zxy,yc->zxc", sigma, pool_y, precision=lax.Precision.HIGHEST)
    coarse = half.reshape(layers, coarse_x, 2, coarse_y).sum(axis=2)

    ends = jnp.cumsum(layer_counts)
    starts = ends - layer_counts
    layer_ids = group_index * layers + jnp.arange(layers, dtype=jnp.int32)
    member = (
        (layer_ids[None, :] >= starts[:, None]) & (layer_ids[None, :] < ends[:, None]) & active
    ).astype(jnp.float32)
    weights = member / (4.0 * layer_counts.astype(jnp.float32))[:, None]
    resist_layers = layer_counts.shape[0]
    partial_cond = jnp.dot(
        weights, coarse.reshape(layers, coarse_x * coarse_y), precision=lax.Precision.HIGHEST
    ).reshape(resist_layers, coarse_x, coarse_y)
    conductivity = grp_sum(partial_cond)

    grid_x = coarse_x * rows
    grid_y = coarse_y * columns
    depth = SWEEPS
    potential = lax.dynamic_slice_in_dim(init_potential, group_index, 1, 0)
    potential = with_halo(potential, (("gx", 2), ("gy", 3)), depth)
    poles = lax.dynamic_slice_in_dim(electrodes, group_index, 1, 0)

    cond_wide = with_halo(conductivity, (("gx", 1), ("gy", 2)), depth)
    cond_wide = jnp.pad(cond_wide, ((1, 1), (0, 0), (0, 0)))
    wide_x = coarse_x + 2 * depth
    wide_y = coarse_y + 2 * depth
    gx_ids = row_index * coarse_x - depth + jnp.arange(wide_x, dtype=jnp.int32)
    gy_ids = column_index * coarse_y - depth + jnp.arange(wide_y, dtype=jnp.int32)
    flat_ids = (
        jnp.arange(resist_layers, dtype=jnp.int32)[:, None, None] * (grid_x * grid_y)
        + gx_ids[None, :, None] * grid_y
        + gy_ids[None, None, :]
    )
    source_terms = AMPLITUDE * (
        (flat_ids[None] == poles[:, 0, None, None, None]).astype(jnp.float32)
        - (flat_ids[None] == poles[:, 1, None, None, None]).astype(jnp.float32)
    )
    on_grid = (
        ((gx_ids >= 0) & (gx_ids < grid_x))[:, None] & ((gy_ids >= 0) & (gy_ids < grid_y))[None, :]
    )

    for sweep_index in range(SWEEPS):
        m = sweep_index + 1
        nx, ny = wide_x - 2 * m, wide_y - 2 * m
        center_c = cond_wide[1:-1, m : m + nx, m : m + ny]
        faces = []
        diagonal = jnp.zeros_like(center_c)
        for d in range(3):
            if d == 0:
                lo = cond_wide[0:-2, m : m + nx, m : m + ny]
                hi = cond_wide[2:, m : m + nx, m : m + ny]
            elif d == 1:
                lo = cond_wide[1:-1, m - 1 : m - 1 + nx, m : m + ny]
                hi = cond_wide[1:-1, m + 1 : m + 1 + nx, m : m + ny]
            else:
                lo = cond_wide[1:-1, m : m + nx, m - 1 : m - 1 + ny]
                hi = cond_wide[1:-1, m : m + nx, m + 1 : m + 1 + ny]
            face_below = 0.5 * (center_c + lo)
            face_above = 0.5 * (center_c + hi)
            faces.append((face_below, face_above))
            diagonal = diagonal + face_below + face_above
        pot_z = jnp.pad(potential, ((0, 0), (1, 1), (0, 0), (0, 0)))
        pot_c = potential[:, :, 1:-1, 1:-1]
        coupled = jnp.zeros_like(pot_c)
        for d in range(3):
            if d == 0:
                lo = pot_z[:, 0:-2, 1:-1, 1:-1]
                hi = pot_z[:, 2:, 1:-1, 1:-1]
            elif d == 1:
                lo = potential[:, :, 0:-2, 1:-1]
                hi = potential[:, :, 2:, 1:-1]
            else:
                lo = potential[:, :, 1:-1, 0:-2]
                hi = potential[:, :, 1:-1, 2:]
            coupled = coupled + faces[d][0] * lo + faces[d][1] * hi
        applied = diagonal * pot_c - coupled
        rhs = source_terms[:, :, m : m + nx, m : m + ny]
        updated = pot_c + OMEGA * (rhs - applied) / diagonal
        potential = jnp.where(on_grid[m : m + nx, m : m + ny], updated, 0.0)

    return (advanced[None], conductivity, potential)


def solution(mesh):
    in_specs = (
        P("grp", None, "gx", "gy"),
        P(None, "grp", None, "gx", "gy"),
        P("grp", None, "gx", "gy"),
        P("grp", None, "gx", "gy"),
        P(),
        P(),
        P(None, None, "gx", "gy"),
    )
    out_specs = (P("grp", None, "gx", "gy"), P(None, "gx", "gy"), P("grp", None, "gx", "gy"))
    return jax.shard_map(
        on_device, mesh=mesh, in_specs=in_specs, out_specs=out_specs, check_vma=False
    )
```

```python
import functools

import jax
import jax.numpy as jnp
from jax.experimental import pallas as pl
from jax.experimental.pallas import tpu as pltpu
from jax import lax
from jax.sharding import PartitionSpec as P

SWEEPS = 3


KAPPA = 0.06
OMEGA = 0.8
AMPLITUDE = 40.0
ARCHIE = 20.0


def with_halo(shard, sides, width, top=None):
    for axis, dim in sides:
        devices, length = (lax.axis_size(axis), shard.shape[dim])
        last_member = devices if (axis != "grp" or top is None) else top
        up = [(i, i + 1) for i in range(last_member - 1)]
        down = [(j, i) for i, j in up]
        last = lax.slice_in_dim(shard, length - width, length, axis=dim)
        initial = lax.slice_in_dim(shard, 0, width, axis=dim)
        before = lax.ppermute(last, axis, up)
        after = lax.ppermute(initial, axis, down)
        shard = jnp.concatenate([before, shard, after], axis=dim)
    return shard


def transport_halo(c, u, slabs):
    f32 = jnp.float32
    u = u.astype(f32)
    nz, nx, ny = c.shape

    def chain(axis, members):
        up = [(i, i + 1) for i in range(members - 1)]
        return up, [(j, i) for i, j in up]

    up, down = chain("grp", slabs)
    below = lax.ppermute(jnp.concatenate([c[nz - 2 :], u[:, nz - 1]], 0), "grp", up)
    above = lax.ppermute(jnp.concatenate([c[:2], u[:, 0]], 0), "grp", down)
    zlo_c, zlo_u = below[:2], below[2:]
    zhi_c, zhi_u = above[:2], above[2:]

    def zext_c(rows):
        return jnp.concatenate([zlo_c[:, rows], c[:, rows], zhi_c[:, rows]], 0)

    def zext_u(row):
        core = jnp.concatenate([zlo_u[:, None, row], u[:, :, row], zhi_u[:, None, row]], 1)
        return jnp.pad(core, ((0, 0), (1, 1), (0, 0)))

    rows = lax.axis_size("gx")
    up, down = chain("gx", rows)
    send_up = jnp.concatenate([zext_c(slice(nx - 2, nx)), jnp.swapaxes(zext_u(nx - 1), 0, 1)], 1)
    send_dn = jnp.concatenate([zext_c(slice(0, 2)), jnp.swapaxes(zext_u(0), 0, 1)], 1)
    bx = lax.ppermute(send_up, "gx", up)
    ax = lax.ppermute(send_dn, "gx", down)

    def xz_c(lanes):
        core = jnp.concatenate([zlo_c[..., lanes], c[..., lanes], zhi_c[..., lanes]], 0)
        return jnp.concatenate([bx[:, 0:2, lanes], core, ax[:, 0:2, lanes]], 1)

    def xz_u(lane):
        core = jnp.pad(
            jnp.concatenate([zlo_u[:, None, :, lane], u[..., lane], zhi_u[:, None, :, lane]], 1),
            ((0, 0), (1, 1), (0, 0)),
        )
        lo = jnp.swapaxes(bx[:, 2:5, lane], 0, 1)[:, :, None]
        hi = jnp.swapaxes(ax[:, 2:5, lane], 0, 1)[:, :, None]
        zero = jnp.zeros_like(lo)
        return jnp.moveaxis(jnp.concatenate([zero, lo, core, hi, zero], 2), 0, 2)

    columns = lax.axis_size("gy")
    up, down = chain("gy", columns)
    by = lax.ppermute(jnp.concatenate([xz_c(slice(ny - 2, ny)), xz_u(ny - 1)], 2), "gy", up)
    ay = lax.ppermute(jnp.concatenate([xz_c(slice(0, 2)), xz_u(0)], 2), "gy", down)

    xc = jnp.concatenate([ax[:, 0:2], jnp.zeros((nz + 4, 4, ny), f32), bx[:, 0:2]], 1)
    xu_hi = jnp.swapaxes(ax[1:-1, 2:5], 0, 1)[:, :, None]
    xu_lo = jnp.swapaxes(bx[1:-1, 2:5], 0, 1)[:, :, None]
    xu = jnp.concatenate([xu_hi, jnp.zeros((3, nz + 2, 6, ny), f32), xu_lo], 2)
    yc = jnp.concatenate([ay[..., 0:2], jnp.zeros((nz + 4, nx + 4, 124), f32), by[..., 0:2]], 2)
    yc = jnp.pad(yc, ((0, 0), (6, 6), (0, 0)))
    yu_hi = jnp.moveaxis(ay[1:-1, :, 2:5], 2, 0)[..., None]
    yu_lo = jnp.moveaxis(by[1:-1, :, 2:5], 2, 0)[..., None]
    yu = jnp.concatenate([yu_hi, jnp.zeros((3, nz + 2, nx + 4, 126), f32), yu_lo], 3)
    yu = jnp.pad(yu, ((0, 0), (0, 0), (6, 6), (0, 0)))
    return zlo_c, zhi_c, zlo_u, zhi_u, xc, xu, yc, yu


def roll(values, shift, axis):
    return pltpu.roll(values, shift % values.shape[axis], axis)


def stencil(c, below, above, speeds):
    running = -6.0 * KAPPA * c
    for d in range(3):
        b, a, s = below[d], above[d], speeds[d]
        running = running + KAPPA * (b + a) - (
            jnp.maximum(s, 0.0) * (c - b) + jnp.minimum(s, 0.0) * (a - c)
        )
    return running


def transport_kernel(
    grid, place, weights, c_ref, v_ref, poro_ref, sat_ref, zlo_c, zhi_c, zlo_u, zhi_u,
    xc, xu, yc, yu, pool_y, pool_x, adv_ref, part_ref, F, U, S,
):
    nz, nx, ny = c_ref.shape
    wx, wy = F.shape[1], F.shape[2]
    f32 = jnp.float32
    F[0:2, 8 : 8 + nx, 0:ny] = zlo_c[...]
    F[nz + 2 : nz + 4, 8 : 8 + nx, 0:ny] = zhi_c[...]

    def put_c(z, carry):
        F[z + 2, 8 : 8 + nx, 0:ny] = c_ref[z]
        return carry

    lax.fori_loop(0, nz, put_c, 0)
    F[:, 0:8, 0:ny] = xc[...]
    F[:, wx - 8 : wx, 0:ny] = xc[...]
    F[:, :, ny:wy] = yc[...]
    for d in range(3):
        U[d, 0, 8 : 8 + nx, 0:ny] = zlo_u[d]
        U[d, nz + 1, 8 : 8 + nx, 0:ny] = zhi_u[d]

        def put_u(z, carry, d=d):
            U[d, z + 1, 8 : 8 + nx, 0:ny] = v_ref[d, 0, z].astype(f32)
            return carry

        lax.fori_loop(0, nz, put_u, 0)
        U[d, :, 0:8, 0:ny] = xu[d]
        U[d, :, wx - 8 : wx, 0:ny] = xu[d]
        U[d, :, :, ny:wy] = yu[d]

    total_z, total_x, total_y = grid
    gz0 = place[0] * nz - 1
    gx = place[1] * nx - 8 + lax.broadcasted_iota(jnp.int32, (wx, wy), 0)
    lane = lax.broadcasted_iota(jnp.int32, (wx, wy), 1)
    gy = place[2] * ny + jnp.where(lane < ny + (wy - ny) // 2, lane, lane - wy)
    plane = (gx >= 0) & (gx < total_x) & (gy >= 0) & (gy < total_y)

    def first(k, carry):
        c0 = F[k + 1]
        below = (F[k], roll(c0, 1, 0), roll(c0, 1, 1))
        above = (F[k + 2], roll(c0, -1, 0), roll(c0, -1, 1))
        speeds = (U[0, k], U[1, k], U[2, k])
        section = c0 + stencil(c0, below, above, speeds)
        z = gz0 + k
        keep = plane & (z >= 0) & (z < total_z)
        S[k] = jnp.where(keep, section, 0.0)
        return carry

    lax.fori_loop(0, nz + 2, first, 0)

    part_ref[...] = jnp.zeros(part_ref.shape, f32)
    live = place[3] > 0

    def core(values):
        return values[8 : 8 + nx, 0:ny]

    def second(j, carry):
        s_mid = S[j + 1]
        s0 = core(s_mid)
        below = (core(S[j]), core(roll(s_mid, 1, 0)), core(roll(s_mid, 1, 1)))
        above = (core(S[j + 2]), core(roll(s_mid, -1, 0)), core(roll(s_mid, -1, 1)))
        speeds = tuple(v_ref[d, 0, j].astype(f32) for d in range(3))
        c0 = c_ref[j]
        adv = 0.5 * (c0 + s0 + stencil(s0, below, above, speeds))
        adv = jnp.where(live, adv, 0.0)
        adv_ref[0, j] = adv
        p = poro_ref[0, j].astype(f32)
        w = sat_ref[0, j].astype(f32)
        sigma = ARCHIE * jnp.exp(adv) * p * p * w * w
        half = jnp.dot(sigma, pool_y[...], precision=lax.Precision.HIGHEST, preferred_element_type=f32)
        coarse = jnp.dot(pool_x[...], half, precision=lax.Precision.HIGHEST, preferred_element_type=f32)
        for e in range(part_ref.shape[0]):
            part_ref[e] = part_ref[e] + weights[e, j] * coarse
        return carry

    lax.fori_loop(0, nz, second, 0)


def transport_call(place, weights, c, velocity, porosity, saturation, *pieces, grid):
    nz, nx, ny = c.shape
    wx, wy = nx + 16, ny + 128
    resist_layers = weights.shape[0]
    pool_y = (
        jnp.arange(ny, dtype=jnp.int32)[:, None] // 2 == jnp.arange(ny // 2, dtype=jnp.int32)[None, :]
    ).astype(jnp.float32)
    pool_x = (
        jnp.arange(nx // 2, dtype=jnp.int32)[:, None] == jnp.arange(nx, dtype=jnp.int32)[None, :] // 2
    ).astype(jnp.float32)
    vmem = pl.BlockSpec(memory_space=pltpu.VMEM)
    smem = pl.BlockSpec(memory_space=pltpu.SMEM)
    cells = nz * nx * ny
    return pl.pallas_call(
        functools.partial(transport_kernel, grid),
        out_shape=(
            jax.ShapeDtypeStruct((1, nz, nx, ny), jnp.float32),
            jax.ShapeDtypeStruct((resist_layers, nx // 2, ny // 2), jnp.float32),
        ),
        in_specs=[smem, smem] + [vmem] * 14,
        out_specs=(vmem, vmem),
        scratch_shapes=[
            pltpu.VMEM((nz + 4, wx, wy), jnp.float32),
            pltpu.VMEM((3, nz + 2, wx, wy), jnp.float32),
            pltpu.VMEM((nz + 2, wx, wy), jnp.float32),
        ],
        compiler_params=pltpu.CompilerParams(vmem_limit_bytes=60 * 1024 * 1024),
        cost_estimate=pl.CostEstimate(
            flops=200 * cells, transcendentals=cells, bytes_accessed=40 * cells
        ),
    )(place, weights, c, velocity, porosity, saturation, *pieces, pool_y, pool_x)


def neighbours(padded, direction_index):
    leading = [slice(None)] * (padded.ndim - 3)
    middle = [slice(1, -1)] * 3
    below_slices = list(middle)
    below_slices[direction_index] = slice(0, -2)
    above_slices = list(middle)
    above_slices[direction_index] = slice(2, None)
    return (padded[tuple(leading + below_slices)], padded[tuple(leading + above_slices)])


def tendency(padded, speeds):
    center = padded[1:-1, 1:-1, 1:-1]
    running = -6.0 * KAPPA * center
    for direction_index in range(3):
        below_cells, above_cells = neighbours(padded, direction_index)
        speed_comp = speeds[direction_index]
        running = (
            running
            + KAPPA * (below_cells + above_cells)
            - (
                jnp.maximum(speed_comp, 0.0) * (center - below_cells)
                + jnp.minimum(speed_comp, 0.0) * (above_cells - center)
            )
        )
    return running


def inside(start, count, total):
    ids = start + jnp.arange(count, dtype=jnp.int32)
    return (ids >= 0) & (ids < total)


def grp_sum(partial):
    pair = lax.ppermute(partial, "grp", [(0, 1), (1, 0), (2, 3), (3, 2)])
    partial = partial + pair
    pair = lax.ppermute(partial, "grp", [(0, 2), (2, 0), (1, 3), (3, 1)])
    return partial + pair


def on_device(conc, velocity, porosity, saturation, layer_counts, electrodes, init_potential):
    group_index = lax.axis_index("grp")
    row_index = lax.axis_index("gx")
    column_index = lax.axis_index("gy")
    groups = lax.axis_size("grp")
    rows = lax.axis_size("gx")
    columns = lax.axis_size("gy")
    active = group_index < 3
    field = conc[0]
    layers, tile_x, tile_y = field.shape
    slabs = 3
    speeds = velocity[:, 0]

    ends = jnp.cumsum(layer_counts)
    starts = ends - layer_counts
    layer_ids = group_index * layers + jnp.arange(layers, dtype=jnp.int32)
    member = (
        (layer_ids[None, :] >= starts[:, None]) & (layer_ids[None, :] < ends[:, None]) & active
    ).astype(jnp.float32)
    weights = member / (4.0 * layer_counts.astype(jnp.float32))[:, None]
    resist_layers = layer_counts.shape[0]
    coarse_x = tile_x // 2
    coarse_y = tile_y // 2

    pieces = transport_halo(field, speeds, slabs)
    place = jnp.stack([group_index, row_index, column_index, active.astype(jnp.int32)])
    advanced, partial_cond = transport_call(
        place, weights, field, velocity, porosity, saturation, *pieces,
        grid=(slabs * layers, rows * tile_x, columns * tile_y),
    )
    conductivity = grp_sum(partial_cond)

    grid_x = coarse_x * rows
    grid_y = coarse_y * columns
    depth = SWEEPS
    potential = lax.dynamic_slice_in_dim(init_potential, group_index, 1, 0)
    poles = lax.dynamic_slice_in_dim(electrodes, group_index, 1, 0)

    both = with_halo(jnp.concatenate([conductivity, potential[0]], axis=0), (("gx", 1), ("gy", 2)), depth)
    cond_wide = jnp.pad(both[:resist_layers], ((1, 1), (0, 0), (0, 0)))
    potential = both[None, resist_layers:]
    wide_x = coarse_x + 2 * depth
    wide_y = coarse_y + 2 * depth
    gx_ids = row_index * coarse_x - depth + jnp.arange(wide_x, dtype=jnp.int32)
    gy_ids = column_index * coarse_y - depth + jnp.arange(wide_y, dtype=jnp.int32)
    flat_ids = (
        jnp.arange(resist_layers, dtype=jnp.int32)[:, None, None] * (grid_x * grid_y)
        + gx_ids[None, :, None] * grid_y
        + gy_ids[None, None, :]
    )
    source_terms = AMPLITUDE * (
        (flat_ids[None] == poles[:, 0, None, None, None]).astype(jnp.float32)
        - (flat_ids[None] == poles[:, 1, None, None, None]).astype(jnp.float32)
    )
    on_grid = (
        ((gx_ids >= 0) & (gx_ids < grid_x))[:, None] & ((gy_ids >= 0) & (gy_ids < grid_y))[None, :]
    )

    for sweep_index in range(SWEEPS):
        m = sweep_index + 1
        nx, ny = wide_x - 2 * m, wide_y - 2 * m
        center_c = cond_wide[1:-1, m : m + nx, m : m + ny]
        faces = []
        diagonal = jnp.zeros_like(center_c)
        for d in range(3):
            if d == 0:
                lo = cond_wide[0:-2, m : m + nx, m : m + ny]
                hi = cond_wide[2:, m : m + nx, m : m + ny]
            elif d == 1:
                lo = cond_wide[1:-1, m - 1 : m - 1 + nx, m : m + ny]
                hi = cond_wide[1:-1, m + 1 : m + 1 + nx, m : m + ny]
            else:
                lo = cond_wide[1:-1, m : m + nx, m - 1 : m - 1 + ny]
                hi = cond_wide[1:-1, m : m + nx, m + 1 : m + 1 + ny]
            face_below = 0.5 * (center_c + lo)
            face_above = 0.5 * (center_c + hi)
            faces.append((face_below, face_above))
            diagonal = diagonal + face_below + face_above
        pot_z = jnp.pad(potential, ((0, 0), (1, 1), (0, 0), (0, 0)))
        pot_c = potential[:, :, 1:-1, 1:-1]
        coupled = jnp.zeros_like(pot_c)
        for d in range(3):
            if d == 0:
                lo = pot_z[:, 0:-2, 1:-1, 1:-1]
                hi = pot_z[:, 2:, 1:-1, 1:-1]
            elif d == 1:
                lo = potential[:, :, 0:-2, 1:-1]
                hi = potential[:, :, 2:, 1:-1]
            else:
                lo = potential[:, :, 1:-1, 0:-2]
                hi = potential[:, :, 1:-1, 2:]
            coupled = coupled + faces[d][0] * lo + faces[d][1] * hi
        applied = diagonal * pot_c - coupled
        rhs = source_terms[:, :, m : m + nx, m : m + ny]
        updated = pot_c + OMEGA * (rhs - applied) / diagonal
        potential = jnp.where(on_grid[m : m + nx, m : m + ny], updated, 0.0)

    return (advanced, conductivity, potential)


def solution(mesh):
    in_specs = (
        P("grp", None, "gx", "gy"),
        P(None, "grp", None, "gx", "gy"),
        P("grp", None, "gx", "gy"),
        P("grp", None, "gx", "gy"),
        P(),
        P(),
        P(None, None, "gx", "gy"),
    )
    out_specs = (P("grp", None, "gx", "gy"), P(None, "gx", "gy"), P("grp", None, "gx", "gy"))
    return jax.shard_map(
        on_device, mesh=mesh, in_specs=in_specs, out_specs=out_specs, check_vma=False
    )
```

```python
import functools

import jax
import jax.numpy as jnp
from jax.experimental import pallas as pl
from jax.experimental.pallas import tpu as pltpu
from jax import lax
from jax.sharding import PartitionSpec as P

SWEEPS = 3


KAPPA = 0.06
OMEGA = 0.8
AMPLITUDE = 40.0
ARCHIE = 20.0


def with_halo(shard, sides, width, top=None):
    for axis, dim in sides:
        devices, length = (lax.axis_size(axis), shard.shape[dim])
        last_member = devices if (axis != "grp" or top is None) else top
        up = [(i, i + 1) for i in range(last_member - 1)]
        down = [(j, i) for i, j in up]
        last = lax.slice_in_dim(shard, length - width, length, axis=dim)
        initial = lax.slice_in_dim(shard, 0, width, axis=dim)
        before = lax.ppermute(last, axis, up)
        after = lax.ppermute(initial, axis, down)
        shard = jnp.concatenate([before, shard, after], axis=dim)
    return shard


def transport_halo(c, u, slabs):
    f32 = jnp.float32
    nz, nx, ny = c.shape

    def chain(axis, members):
        up = [(i, i + 1) for i in range(members - 1)]
        return up, [(j, i) for i, j in up]

    up, down = chain("grp", slabs)
    below = lax.ppermute(jnp.concatenate([c[nz - 2 :], u[:, nz - 1].astype(f32)], 0), "grp", up)
    above = lax.ppermute(jnp.concatenate([c[:2], u[:, 0].astype(f32)], 0), "grp", down)
    zlo_c, zlo_u = below[:2], below[2:]
    zhi_c, zhi_u = above[:2], above[2:]

    def zext_c(rows):
        return jnp.concatenate([zlo_c[:, rows], c[:, rows], zhi_c[:, rows]], 0)

    def zext_u(row):
        core = jnp.concatenate(
            [zlo_u[:, None, row], u[:, :, row].astype(f32), zhi_u[:, None, row]], 1
        )
        return jnp.pad(core, ((0, 0), (1, 1), (0, 0)))

    rows = lax.axis_size("gx")
    up, down = chain("gx", rows)
    send_up = jnp.concatenate([zext_c(slice(nx - 2, nx)), jnp.swapaxes(zext_u(nx - 1), 0, 1)], 1)
    send_dn = jnp.concatenate([zext_c(slice(0, 2)), jnp.swapaxes(zext_u(0), 0, 1)], 1)
    bx = lax.ppermute(send_up, "gx", up)
    ax = lax.ppermute(send_dn, "gx", down)

    def xz_c(lanes):
        core = jnp.concatenate([zlo_c[..., lanes], c[..., lanes], zhi_c[..., lanes]], 0)
        return jnp.concatenate([bx[:, 0:2, lanes], core, ax[:, 0:2, lanes]], 1)

    def xz_u(lane):
        core = jnp.pad(
            jnp.concatenate(
                [zlo_u[:, None, :, lane], u[..., lane].astype(f32), zhi_u[:, None, :, lane]], 1
            ),
            ((0, 0), (1, 1), (0, 0)),
        )
        lo = jnp.swapaxes(bx[:, 2:5, lane], 0, 1)[:, :, None]
        hi = jnp.swapaxes(ax[:, 2:5, lane], 0, 1)[:, :, None]
        zero = jnp.zeros_like(lo)
        return jnp.moveaxis(jnp.concatenate([zero, lo, core, hi, zero], 2), 0, 2)

    columns = lax.axis_size("gy")
    up, down = chain("gy", columns)
    by = lax.ppermute(jnp.concatenate([xz_c(slice(ny - 2, ny)), xz_u(ny - 1)], 2), "gy", up)
    ay = lax.ppermute(jnp.concatenate([xz_c(slice(0, 2)), xz_u(0)], 2), "gy", down)

    xc = jnp.concatenate([ax[:, 0:2], jnp.zeros((nz + 4, 4, ny), f32), bx[:, 0:2]], 1)
    xu_hi = jnp.swapaxes(ax[1:-1, 2:5], 0, 1)[:, :, None]
    xu_lo = jnp.swapaxes(bx[1:-1, 2:5], 0, 1)[:, :, None]
    xu = jnp.concatenate([xu_hi, jnp.zeros((3, nz + 2, 6, ny), f32), xu_lo], 2)
    yc = jnp.concatenate([ay[..., 0:2], jnp.zeros((nz + 4, nx + 4, 124), f32), by[..., 0:2]], 2)
    yc = jnp.pad(yc, ((0, 0), (6, 6), (0, 0)))
    yu_hi = jnp.moveaxis(ay[1:-1, :, 2:5], 2, 0)[..., None]
    yu_lo = jnp.moveaxis(by[1:-1, :, 2:5], 2, 0)[..., None]
    yu = jnp.concatenate([yu_hi, jnp.zeros((3, nz + 2, nx + 4, 126), f32), yu_lo], 3)
    yu = jnp.pad(yu, ((0, 0), (0, 0), (6, 6), (0, 0)))
    return zlo_c, zhi_c, zlo_u, zhi_u, xc, xu, yc, yu


def roll(values, shift, axis):
    return pltpu.roll(values, shift % values.shape[axis], axis)


def stencil(c, below, above, speeds):
    running = -6.0 * KAPPA * c
    for d in range(3):
        b, a, s = below[d], above[d], speeds[d]
        running = running + KAPPA * (b + a) - (
            jnp.maximum(s, 0.0) * (c - b) + jnp.minimum(s, 0.0) * (a - c)
        )
    return running


def transport_kernel(
    grid, place, weights, c_ref, v_ref, poro_ref, sat_ref, zlo_c, zhi_c, zlo_u, zhi_u,
    xc, xu, yc, yu, adv_ref, part_ref, F, U, S,
):
    nz, nx, ny = c_ref.shape
    wx, wy = F.shape[1], F.shape[2]
    f32 = jnp.float32
    pool_y = (
        lax.broadcasted_iota(jnp.int32, (ny, ny // 2), 0) // 2
        == lax.broadcasted_iota(jnp.int32, (ny, ny // 2), 1)
    ).astype(f32)
    pool_x = (
        lax.broadcasted_iota(jnp.int32, (nx // 2, nx), 0)
        == lax.broadcasted_iota(jnp.int32, (nx // 2, nx), 1) // 2
    ).astype(f32)
    F[0:2, 8 : 8 + nx, 0:ny] = zlo_c[...]
    F[nz + 2 : nz + 4, 8 : 8 + nx, 0:ny] = zhi_c[...]

    def put_c(z, carry):
        F[z + 2, 8 : 8 + nx, 0:ny] = c_ref[z]
        return carry

    lax.fori_loop(0, nz, put_c, 0)
    F[:, 0:8, 0:ny] = xc[...]
    F[:, wx - 8 : wx, 0:ny] = xc[...]
    F[:, :, ny:wy] = yc[...]
    for d in range(3):
        U[d, 0, 8 : 8 + nx, 0:ny] = zlo_u[d]
        U[d, nz + 1, 8 : 8 + nx, 0:ny] = zhi_u[d]

        def put_u(z, carry, d=d):
            U[d, z + 1, 8 : 8 + nx, 0:ny] = v_ref[d, 0, z].astype(f32)
            return carry

        lax.fori_loop(0, nz, put_u, 0)
        U[d, :, 0:8, 0:ny] = xu[d]
        U[d, :, wx - 8 : wx, 0:ny] = xu[d]
        U[d, :, :, ny:wy] = yu[d]

    total_z, total_x, total_y = grid
    gz0 = place[0] * nz - 1
    gx = place[1] * nx - 8 + lax.broadcasted_iota(jnp.int32, (wx, wy), 0)
    lane = lax.broadcasted_iota(jnp.int32, (wx, wy), 1)
    gy = place[2] * ny + jnp.where(lane < ny + (wy - ny) // 2, lane, lane - wy)
    plane = (gx >= 0) & (gx < total_x) & (gy >= 0) & (gy < total_y)

    def first(k, carry):
        c0 = F[k + 1]
        below = (F[k], roll(c0, 1, 0), roll(c0, 1, 1))
        above = (F[k + 2], roll(c0, -1, 0), roll(c0, -1, 1))
        speeds = (U[0, k], U[1, k], U[2, k])
        section = c0 + stencil(c0, below, above, speeds)
        z = gz0 + k
        keep = plane & (z >= 0) & (z < total_z)
        S[k] = jnp.where(keep, section, 0.0)
        return carry

    lax.fori_loop(0, nz + 2, first, 0)

    part_ref[...] = jnp.zeros(part_ref.shape, f32)
    live = place[3] > 0

    def core(values):
        return values[8 : 8 + nx, 0:ny]

    def second(j, carry):
        s_mid = S[j + 1]
        s0 = core(s_mid)
        below = (core(S[j]), core(roll(s_mid, 1, 0)), core(roll(s_mid, 1, 1)))
        above = (core(S[j + 2]), core(roll(s_mid, -1, 0)), core(roll(s_mid, -1, 1)))
        speeds = tuple(v_ref[d, 0, j].astype(f32) for d in range(3))
        c0 = c_ref[j]
        adv = 0.5 * (c0 + s0 + stencil(s0, below, above, speeds))
        adv = jnp.where(live, adv, 0.0)
        adv_ref[0, j] = adv
        p = poro_ref[0, j].astype(f32)
        w = sat_ref[0, j].astype(f32)
        sigma = ARCHIE * jnp.exp(adv) * p * p * w * w
        half = jnp.dot(sigma, pool_y, precision=lax.Precision.HIGHEST, preferred_element_type=f32)
        coarse = jnp.dot(pool_x, half, precision=lax.Precision.HIGHEST, preferred_element_type=f32)
        for e in range(part_ref.shape[0]):
            part_ref[e] = part_ref[e] + weights[e, j] * coarse
        return carry

    lax.fori_loop(0, nz, second, 0)


def transport_call(place, weights, c, velocity, porosity, saturation, *pieces, grid):
    nz, nx, ny = c.shape
    wx, wy = nx + 16, ny + 128
    resist_layers = weights.shape[0]
    vmem = pl.BlockSpec(memory_space=pltpu.VMEM)
    smem = pl.BlockSpec(memory_space=pltpu.SMEM)
    cells = nz * nx * ny
    return pl.pallas_call(
        functools.partial(transport_kernel, grid),
        out_shape=(
            jax.ShapeDtypeStruct((1, nz, nx, ny), jnp.float32),
            jax.ShapeDtypeStruct((resist_layers, nx // 2, ny // 2), jnp.float32),
        ),
        in_specs=[smem, smem] + [vmem] * 12,
        out_specs=(vmem, vmem),
        scratch_shapes=[
            pltpu.VMEM((nz + 4, wx, wy), jnp.float32),
            pltpu.VMEM((3, nz + 2, wx, wy), jnp.float32),
            pltpu.VMEM((nz + 2, wx, wy), jnp.float32),
        ],
        compiler_params=pltpu.CompilerParams(vmem_limit_bytes=60 * 1024 * 1024),
        cost_estimate=pl.CostEstimate(
            flops=200 * cells, transcendentals=cells, bytes_accessed=40 * cells
        ),
    )(place, weights, c, velocity, porosity, saturation, *pieces)


def neighbours(padded, direction_index):
    leading = [slice(None)] * (padded.ndim - 3)
    middle = [slice(1, -1)] * 3
    below_slices = list(middle)
    below_slices[direction_index] = slice(0, -2)
    above_slices = list(middle)
    above_slices[direction_index] = slice(2, None)
    return (padded[tuple(leading + below_slices)], padded[tuple(leading + above_slices)])


def tendency(padded, speeds):
    center = padded[1:-1, 1:-1, 1:-1]
    running = -6.0 * KAPPA * center
    for direction_index in range(3):
        below_cells, above_cells = neighbours(padded, direction_index)
        speed_comp = speeds[direction_index]
        running = (
            running
            + KAPPA * (below_cells + above_cells)
            - (
                jnp.maximum(speed_comp, 0.0) * (center - below_cells)
                + jnp.minimum(speed_comp, 0.0) * (above_cells - center)
            )
        )
    return running


def inside(start, count, total):
    ids = start + jnp.arange(count, dtype=jnp.int32)
    return (ids >= 0) & (ids < total)


def plane_halo(values, depth):
    rows, columns = lax.axis_size("gx"), lax.axis_size("gy")
    d = depth

    def line(n, step):
        return [(i, i + step) for i in range(n) if 0 <= i + step < n]

    def flat(i, j):
        return i * columns + j

    def diagonal(di, dj):
        return [
            (flat(i, j), flat(i + di, j + dj))
            for i in range(rows)
            for j in range(columns)
            if 0 <= i + di < rows and 0 <= j + dj < columns
        ]

    both = ("gx", "gy")
    lo_x = lax.ppermute(values[:, -d:, :], "gx", line(rows, 1))
    hi_x = lax.ppermute(values[:, :d, :], "gx", line(rows, -1))
    lo_y = lax.ppermute(values[:, :, -d:], "gy", line(columns, 1))
    hi_y = lax.ppermute(values[:, :, :d], "gy", line(columns, -1))
    lo_lo = lax.ppermute(values[:, -d:, -d:], both, diagonal(1, 1))
    lo_hi = lax.ppermute(values[:, -d:, :d], both, diagonal(1, -1))
    hi_lo = lax.ppermute(values[:, :d, -d:], both, diagonal(-1, 1))
    hi_hi = lax.ppermute(values[:, :d, :d], both, diagonal(-1, -1))
    top = jnp.concatenate([lo_lo, lo_x, lo_hi], 2)
    middle = jnp.concatenate([lo_y, values, hi_y], 2)
    bottom = jnp.concatenate([hi_lo, hi_x, hi_hi], 2)
    return jnp.concatenate([top, middle, bottom], 1)


def grp_sum(partial):
    pair = lax.ppermute(partial, "grp", [(0, 1), (1, 0), (2, 3), (3, 2)])
    partial = partial + pair
    pair = lax.ppermute(partial, "grp", [(0, 2), (2, 0), (1, 3), (3, 1)])
    return partial + pair


def on_device(conc, velocity, porosity, saturation, layer_counts, electrodes, init_potential):
    group_index = lax.axis_index("grp")
    row_index = lax.axis_index("gx")
    column_index = lax.axis_index("gy")
    groups = lax.axis_size("grp")
    rows = lax.axis_size("gx")
    columns = lax.axis_size("gy")
    active = group_index < 3
    field = conc[0]
    layers, tile_x, tile_y = field.shape
    slabs = 3
    speeds = velocity[:, 0]

    ends = jnp.cumsum(layer_counts)
    starts = ends - layer_counts
    layer_ids = group_index * layers + jnp.arange(layers, dtype=jnp.int32)
    member = (
        (layer_ids[None, :] >= starts[:, None]) & (layer_ids[None, :] < ends[:, None]) & active
    ).astype(jnp.float32)
    weights = member / (4.0 * layer_counts.astype(jnp.float32))[:, None]
    resist_layers = layer_counts.shape[0]
    coarse_x = tile_x // 2
    coarse_y = tile_y // 2

    pieces = transport_halo(field, speeds, slabs)
    place = jnp.stack([group_index, row_index, column_index, active.astype(jnp.int32)])
    advanced, partial_cond = transport_call(
        place, weights, field, velocity, porosity, saturation, *pieces,
        grid=(slabs * layers, rows * tile_x, columns * tile_y),
    )
    conductivity = grp_sum(partial_cond)

    grid_x = coarse_x * rows
    grid_y = coarse_y * columns
    depth = SWEEPS
    potential = lax.dynamic_slice_in_dim(init_potential, group_index, 1, 0)
    poles = lax.dynamic_slice_in_dim(electrodes, group_index, 1, 0)

    both = plane_halo(jnp.concatenate([conductivity, potential[0]], axis=0), depth)
    cond_wide = jnp.pad(both[:resist_layers], ((1, 1), (0, 0), (0, 0)))
    potential = both[None, resist_layers:]
    wide_x = coarse_x + 2 * depth
    wide_y = coarse_y + 2 * depth
    gx_ids = row_index * coarse_x - depth + jnp.arange(wide_x, dtype=jnp.int32)
    gy_ids = column_index * coarse_y - depth + jnp.arange(wide_y, dtype=jnp.int32)
    flat_ids = (
        jnp.arange(resist_layers, dtype=jnp.int32)[:, None, None] * (grid_x * grid_y)
        + gx_ids[None, :, None] * grid_y
        + gy_ids[None, None, :]
    )
    source_terms = AMPLITUDE * (
        (flat_ids[None] == poles[:, 0, None, None, None]).astype(jnp.float32)
        - (flat_ids[None] == poles[:, 1, None, None, None]).astype(jnp.float32)
    )
    on_grid = (
        ((gx_ids >= 0) & (gx_ids < grid_x))[:, None] & ((gy_ids >= 0) & (gy_ids < grid_y))[None, :]
    )

    for sweep_index in range(SWEEPS):
        m = sweep_index + 1
        nx, ny = wide_x - 2 * m, wide_y - 2 * m
        center_c = cond_wide[1:-1, m : m + nx, m : m + ny]
        faces = []
        diagonal = jnp.zeros_like(center_c)
        for d in range(3):
            if d == 0:
                lo = cond_wide[0:-2, m : m + nx, m : m + ny]
                hi = cond_wide[2:, m : m + nx, m : m + ny]
            elif d == 1:
                lo = cond_wide[1:-1, m - 1 : m - 1 + nx, m : m + ny]
                hi = cond_wide[1:-1, m + 1 : m + 1 + nx, m : m + ny]
            else:
                lo = cond_wide[1:-1, m : m + nx, m - 1 : m - 1 + ny]
                hi = cond_wide[1:-1, m : m + nx, m + 1 : m + 1 + ny]
            face_below = 0.5 * (center_c + lo)
            face_above = 0.5 * (center_c + hi)
            faces.append((face_below, face_above))
            diagonal = diagonal + face_below + face_above
        pot_z = jnp.pad(potential, ((0, 0), (1, 1), (0, 0), (0, 0)))
        pot_c = potential[:, :, 1:-1, 1:-1]
        coupled = jnp.zeros_like(pot_c)
        for d in range(3):
            if d == 0:
                lo = pot_z[:, 0:-2, 1:-1, 1:-1]
                hi = pot_z[:, 2:, 1:-1, 1:-1]
            elif d == 1:
                lo = potential[:, :, 0:-2, 1:-1]
                hi = potential[:, :, 2:, 1:-1]
            else:
                lo = potential[:, :, 1:-1, 0:-2]
                hi = potential[:, :, 1:-1, 2:]
            coupled = coupled + faces[d][0] * lo + faces[d][1] * hi
        applied = diagonal * pot_c - coupled
        rhs = source_terms[:, :, m : m + nx, m : m + ny]
        updated = pot_c + OMEGA * (rhs - applied) / diagonal
        potential = jnp.where(on_grid[m : m + nx, m : m + ny], updated, 0.0)

    return (advanced, conductivity, potential)


def solution(mesh):
    in_specs = (
        P("grp", None, "gx", "gy"),
        P(None, "grp", None, "gx", "gy"),
        P("grp", None, "gx", "gy"),
        P("grp", None, "gx", "gy"),
        P(),
        P(),
        P(None, None, "gx", "gy"),
    )
    out_specs = (P("grp", None, "gx", "gy"), P(None, "gx", "gy"), P("grp", None, "gx", "gy"))
    return jax.shard_map(
        on_device, mesh=mesh, in_specs=in_specs, out_specs=out_specs, check_vma=False
    )
```

```python
import functools

import jax
import jax.numpy as jnp
from jax.experimental import pallas as pl
from jax.experimental.pallas import tpu as pltpu
from jax import lax
from jax.sharding import PartitionSpec as P

SWEEPS = 3


KAPPA = 0.06
OMEGA = 0.8
AMPLITUDE = 40.0
ARCHIE = 20.0


def with_halo(shard, sides, width, top=None):
    for axis, dim in sides:
        devices, length = (lax.axis_size(axis), shard.shape[dim])
        last_member = devices if (axis != "grp" or top is None) else top
        up = [(i, i + 1) for i in range(last_member - 1)]
        down = [(j, i) for i, j in up]
        last = lax.slice_in_dim(shard, length - width, length, axis=dim)
        initial = lax.slice_in_dim(shard, 0, width, axis=dim)
        before = lax.ppermute(last, axis, up)
        after = lax.ppermute(initial, axis, down)
        shard = jnp.concatenate([before, shard, after], axis=dim)
    return shard


def transport_halo(c, u, slabs):
    f32 = jnp.float32
    nz, nx, ny = c.shape

    def chain(axis, members):
        up = [(i, i + 1) for i in range(members - 1)]
        return up, [(j, i) for i, j in up]

    up, down = chain("grp", slabs)
    below = lax.ppermute(jnp.concatenate([c[nz - 2 :], u[:, nz - 1].astype(f32)], 0), "grp", up)
    above = lax.ppermute(jnp.concatenate([c[:2], u[:, 0].astype(f32)], 0), "grp", down)
    zlo_c, zlo_u = below[:2], below[2:]
    zhi_c, zhi_u = above[:2], above[2:]

    def zext_c(rows):
        return jnp.concatenate([zlo_c[:, rows], c[:, rows], zhi_c[:, rows]], 0)

    def zext_u(row):
        core = jnp.concatenate(
            [zlo_u[:, None, row], u[:, :, row].astype(f32), zhi_u[:, None, row]], 1
        )
        return jnp.pad(core, ((0, 0), (1, 1), (0, 0)))

    rows = lax.axis_size("gx")
    up, down = chain("gx", rows)
    send_up = jnp.concatenate([zext_c(slice(nx - 2, nx)), jnp.swapaxes(zext_u(nx - 1), 0, 1)], 1)
    send_dn = jnp.concatenate([zext_c(slice(0, 2)), jnp.swapaxes(zext_u(0), 0, 1)], 1)
    bx = lax.ppermute(send_up, "gx", up)
    ax = lax.ppermute(send_dn, "gx", down)

    def xz_c(lanes):
        core = jnp.concatenate([zlo_c[..., lanes], c[..., lanes], zhi_c[..., lanes]], 0)
        return jnp.concatenate([bx[:, 0:2, lanes], core, ax[:, 0:2, lanes]], 1)

    def xz_u(lane):
        core = jnp.pad(
            jnp.concatenate(
                [zlo_u[:, None, :, lane], u[..., lane].astype(f32), zhi_u[:, None, :, lane]], 1
            ),
            ((0, 0), (1, 1), (0, 0)),
        )
        lo = jnp.swapaxes(bx[:, 2:5, lane], 0, 1)[:, :, None]
        hi = jnp.swapaxes(ax[:, 2:5, lane], 0, 1)[:, :, None]
        zero = jnp.zeros_like(lo)
        return jnp.moveaxis(jnp.concatenate([zero, lo, core, hi, zero], 2), 0, 2)

    columns = lax.axis_size("gy")
    up, down = chain("gy", columns)
    by = lax.ppermute(jnp.concatenate([xz_c(slice(ny - 2, ny)), xz_u(ny - 1)], 2), "gy", up)
    ay = lax.ppermute(jnp.concatenate([xz_c(slice(0, 2)), xz_u(0)], 2), "gy", down)

    xc = jnp.concatenate([ax[:, 0:2], jnp.zeros((nz + 4, 4, ny), f32), bx[:, 0:2]], 1)
    xu_hi = jnp.swapaxes(ax[1:-1, 2:5], 0, 1)[:, :, None]
    xu_lo = jnp.swapaxes(bx[1:-1, 2:5], 0, 1)[:, :, None]
    xu = jnp.concatenate([xu_hi, jnp.zeros((3, nz + 2, 6, ny), f32), xu_lo], 2)
    yc = jnp.concatenate([ay[..., 0:2], jnp.zeros((nz + 4, nx + 4, 124), f32), by[..., 0:2]], 2)
    yc = jnp.pad(yc, ((0, 0), (6, 6), (0, 0)))
    yu_hi = jnp.moveaxis(ay[1:-1, :, 2:5], 2, 0)[..., None]
    yu_lo = jnp.moveaxis(by[1:-1, :, 2:5], 2, 0)[..., None]
    yu = jnp.concatenate([yu_hi, jnp.zeros((3, nz + 2, nx + 4, 126), f32), yu_lo], 3)
    yu = jnp.pad(yu, ((0, 0), (0, 0), (6, 6), (0, 0)))
    return zlo_c, zhi_c, zlo_u, zhi_u, xc, xu, yc, yu


def roll(values, shift, axis):
    return pltpu.roll(values, shift % values.shape[axis], axis)


def stencil(c, below, above, speeds):
    running = -6.0 * KAPPA * c
    for d in range(3):
        b, a, s = below[d], above[d], speeds[d]
        running = running + KAPPA * (b + a) - (
            jnp.maximum(s, 0.0) * (c - b) + jnp.minimum(s, 0.0) * (a - c)
        )
    return running


def transport_kernel(
    grid, place, weights, c_ref, v_ref, poro_ref, sat_ref, zlo_c, zhi_c, zlo_u, zhi_u,
    xc, xu, yc, yu, adv_ref, part_ref, F, U, S,
):
    nz, nx, ny = c_ref.shape
    wx, wy = F.shape[1], F.shape[2]
    f32 = jnp.float32
    pool_y = (
        lax.broadcasted_iota(jnp.int32, (ny, ny // 2), 0) // 2
        == lax.broadcasted_iota(jnp.int32, (ny, ny // 2), 1)
    ).astype(f32)
    pool_x = (
        lax.broadcasted_iota(jnp.int32, (nx // 2, nx), 0)
        == lax.broadcasted_iota(jnp.int32, (nx // 2, nx), 1) // 2
    ).astype(f32)
    F[0:2, 8 : 8 + nx, 0:ny] = zlo_c[...]
    F[nz + 2 : nz + 4, 8 : 8 + nx, 0:ny] = zhi_c[...]

    def put_c(z, carry):
        F[z + 2, 8 : 8 + nx, 0:ny] = c_ref[z]
        return carry

    lax.fori_loop(0, nz, put_c, 0)
    F[:, 0:8, 0:ny] = xc[...]
    F[:, wx - 8 : wx, 0:ny] = xc[...]
    F[:, :, ny:wy] = yc[...]
    for d in range(3):
        U[d, 0, 8 : 8 + nx, 0:ny] = zlo_u[d]
        U[d, nz + 1, 8 : 8 + nx, 0:ny] = zhi_u[d]

        def put_u(z, carry, d=d):
            U[d, z + 1, 8 : 8 + nx, 0:ny] = v_ref[d, 0, z].astype(f32)
            return carry

        lax.fori_loop(0, nz, put_u, 0)
        U[d, :, 0:8, 0:ny] = xu[d]
        U[d, :, wx - 8 : wx, 0:ny] = xu[d]
        U[d, :, :, ny:wy] = yu[d]

    total_z, total_x, total_y = grid
    gz0 = place[0] * nz - 1
    gx = place[1] * nx - 8 + lax.broadcasted_iota(jnp.int32, (wx, wy), 0)
    lane = lax.broadcasted_iota(jnp.int32, (wx, wy), 1)
    gy = place[2] * ny + jnp.where(lane < ny + (wy - ny) // 2, lane, lane - wy)
    plane = (gx >= 0) & (gx < total_x) & (gy >= 0) & (gy < total_y)

    def first(k, carry):
        c0 = F[k + 1]
        below = (F[k], roll(c0, 1, 0), roll(c0, 1, 1))
        above = (F[k + 2], roll(c0, -1, 0), roll(c0, -1, 1))
        speeds = (U[0, k], U[1, k], U[2, k])
        section = c0 + stencil(c0, below, above, speeds)
        z = gz0 + k
        keep = plane & (z >= 0) & (z < total_z)
        S[k] = jnp.where(keep, section, 0.0)
        return carry

    lax.fori_loop(0, nz + 2, first, 0)

    part_ref[...] = jnp.zeros(part_ref.shape, f32)
    live = place[3] > 0

    def core(values):
        return values[8 : 8 + nx, 0:ny]

    def second(j, carry):
        s_mid = S[j + 1]
        s0 = core(s_mid)
        below = (core(S[j]), core(roll(s_mid, 1, 0)), core(roll(s_mid, 1, 1)))
        above = (core(S[j + 2]), core(roll(s_mid, -1, 0)), core(roll(s_mid, -1, 1)))
        speeds = tuple(v_ref[d, 0, j].astype(f32) for d in range(3))
        c0 = c_ref[j]
        adv = 0.5 * (c0 + s0 + stencil(s0, below, above, speeds))
        adv = jnp.where(live, adv, 0.0)
        adv_ref[0, j] = adv
        p = poro_ref[0, j].astype(f32)
        w = sat_ref[0, j].astype(f32)
        sigma = ARCHIE * jnp.exp(adv) * p * p * w * w
        half = jnp.dot(sigma, pool_y, precision=lax.Precision.HIGHEST, preferred_element_type=f32)
        coarse = jnp.dot(pool_x, half, precision=lax.Precision.HIGHEST, preferred_element_type=f32)
        for e in range(part_ref.shape[0]):
            part_ref[e] = part_ref[e] + weights[e, j] * coarse
        return carry

    lax.fori_loop(0, nz, second, 0)


def transport_call(place, weights, c, velocity, porosity, saturation, *pieces, grid):
    nz, nx, ny = c.shape
    wx, wy = nx + 16, ny + 128
    resist_layers = weights.shape[0]
    vmem = pl.BlockSpec(memory_space=pltpu.VMEM)
    smem = pl.BlockSpec(memory_space=pltpu.SMEM)
    cells = nz * nx * ny
    return pl.pallas_call(
        functools.partial(transport_kernel, grid),
        out_shape=(
            jax.ShapeDtypeStruct((1, nz, nx, ny), jnp.float32),
            jax.ShapeDtypeStruct((resist_layers, nx // 2, ny // 2), jnp.float32),
        ),
        in_specs=[smem, smem] + [vmem] * 12,
        out_specs=(vmem, vmem),
        scratch_shapes=[
            pltpu.VMEM((nz + 4, wx, wy), jnp.float32),
            pltpu.VMEM((3, nz + 2, wx, wy), jnp.float32),
            pltpu.VMEM((nz + 2, wx, wy), jnp.float32),
        ],
        compiler_params=pltpu.CompilerParams(vmem_limit_bytes=60 * 1024 * 1024),
        cost_estimate=pl.CostEstimate(
            flops=200 * cells, transcendentals=cells, bytes_accessed=40 * cells
        ),
    )(place, weights, c, velocity, porosity, saturation, *pieces)


def neighbours(padded, direction_index):
    leading = [slice(None)] * (padded.ndim - 3)
    middle = [slice(1, -1)] * 3
    below_slices = list(middle)
    below_slices[direction_index] = slice(0, -2)
    above_slices = list(middle)
    above_slices[direction_index] = slice(2, None)
    return (padded[tuple(leading + below_slices)], padded[tuple(leading + above_slices)])


def tendency(padded, speeds):
    center = padded[1:-1, 1:-1, 1:-1]
    running = -6.0 * KAPPA * center
    for direction_index in range(3):
        below_cells, above_cells = neighbours(padded, direction_index)
        speed_comp = speeds[direction_index]
        running = (
            running
            + KAPPA * (below_cells + above_cells)
            - (
                jnp.maximum(speed_comp, 0.0) * (center - below_cells)
                + jnp.minimum(speed_comp, 0.0) * (above_cells - center)
            )
        )
    return running


def inside(start, count, total):
    ids = start + jnp.arange(count, dtype=jnp.int32)
    return (ids >= 0) & (ids < total)


def plane_halo(values, depth):
    rows, columns = lax.axis_size("gx"), lax.axis_size("gy")
    d = depth

    def line(n, step):
        return [(i, i + step) for i in range(n) if 0 <= i + step < n]

    def flat(i, j):
        return i * columns + j

    def diagonal(di, dj):
        return [
            (flat(i, j), flat(i + di, j + dj))
            for i in range(rows)
            for j in range(columns)
            if 0 <= i + di < rows and 0 <= j + dj < columns
        ]

    both = ("gx", "gy")
    lo_x = lax.ppermute(values[:, -d:, :], "gx", line(rows, 1))
    hi_x = lax.ppermute(values[:, :d, :], "gx", line(rows, -1))
    lo_y = lax.ppermute(values[:, :, -d:], "gy", line(columns, 1))
    hi_y = lax.ppermute(values[:, :, :d], "gy", line(columns, -1))
    lo_lo = lax.ppermute(values[:, -d:, -d:], both, diagonal(1, 1))
    lo_hi = lax.ppermute(values[:, -d:, :d], both, diagonal(1, -1))
    hi_lo = lax.ppermute(values[:, :d, -d:], both, diagonal(-1, 1))
    hi_hi = lax.ppermute(values[:, :d, :d], both, diagonal(-1, -1))
    top = jnp.concatenate([lo_lo, lo_x, lo_hi], 2)
    middle = jnp.concatenate([lo_y, values, hi_y], 2)
    bottom = jnp.concatenate([hi_lo, hi_x, hi_hi], 2)
    return jnp.concatenate([top, middle, bottom], 1)


def grp_sum(partial):
    pair = lax.ppermute(partial, "grp", [(0, 1), (1, 0), (2, 3), (3, 2)])
    partial = partial + pair
    pair = lax.ppermute(partial, "grp", [(0, 2), (2, 0), (1, 3), (3, 1)])
    return partial + pair


def on_device(conc, velocity, porosity, saturation, layer_counts, electrodes, init_potential):
    group_index = lax.axis_index("grp")
    row_index = lax.axis_index("gx")
    column_index = lax.axis_index("gy")
    groups = lax.axis_size("grp")
    rows = lax.axis_size("gx")
    columns = lax.axis_size("gy")
    active = group_index < 3
    field = conc[0]
    layers, tile_x, tile_y = field.shape
    slabs = 3
    speeds = velocity[:, 0]

    ends = jnp.cumsum(layer_counts)
    starts = ends - layer_counts
    layer_ids = group_index * layers + jnp.arange(layers, dtype=jnp.int32)
    member = (
        (layer_ids[None, :] >= starts[:, None]) & (layer_ids[None, :] < ends[:, None]) & active
    ).astype(jnp.float32)
    weights = member / (4.0 * layer_counts.astype(jnp.float32))[:, None]
    resist_layers = layer_counts.shape[0]
    coarse_x = tile_x // 2
    coarse_y = tile_y // 2

    pieces = transport_halo(field, speeds, slabs)
    place = jnp.stack([group_index, row_index, column_index, active.astype(jnp.int32)])
    advanced, partial_cond = transport_call(
        place, weights, field, velocity, porosity, saturation, *pieces,
        grid=(slabs * layers, rows * tile_x, columns * tile_y),
    )
    conductivity = grp_sum(partial_cond)

    grid_x = coarse_x * rows
    grid_y = coarse_y * columns
    depth = SWEEPS
    potential = lax.dynamic_slice_in_dim(init_potential, group_index, 1, 0)
    poles = lax.dynamic_slice_in_dim(electrodes, group_index, 1, 0)

    both = with_halo(jnp.concatenate([conductivity, potential[0]], axis=0), (("gx", 1), ("gy", 2)), depth)
    cond_wide = jnp.pad(both[:resist_layers], ((1, 1), (0, 0), (0, 0)))
    potential = both[None, resist_layers:]
    wide_x = coarse_x + 2 * depth
    wide_y = coarse_y + 2 * depth
    gx_ids = row_index * coarse_x - depth + jnp.arange(wide_x, dtype=jnp.int32)
    gy_ids = column_index * coarse_y - depth + jnp.arange(wide_y, dtype=jnp.int32)
    flat_ids = (
        jnp.arange(resist_layers, dtype=jnp.int32)[:, None, None] * (grid_x * grid_y)
        + gx_ids[None, :, None] * grid_y
        + gy_ids[None, None, :]
    )
    source_terms = AMPLITUDE * (
        (flat_ids[None] == poles[:, 0, None, None, None]).astype(jnp.float32)
        - (flat_ids[None] == poles[:, 1, None, None, None]).astype(jnp.float32)
    )
    on_grid = (
        ((gx_ids >= 0) & (gx_ids < grid_x))[:, None] & ((gy_ids >= 0) & (gy_ids < grid_y))[None, :]
    )

    for sweep_index in range(SWEEPS):
        m = sweep_index + 1
        nx, ny = wide_x - 2 * m, wide_y - 2 * m
        center_c = cond_wide[1:-1, m : m + nx, m : m + ny]
        faces = []
        diagonal = jnp.zeros_like(center_c)
        for d in range(3):
            if d == 0:
                lo = cond_wide[0:-2, m : m + nx, m : m + ny]
                hi = cond_wide[2:, m : m + nx, m : m + ny]
            elif d == 1:
                lo = cond_wide[1:-1, m - 1 : m - 1 + nx, m : m + ny]
                hi = cond_wide[1:-1, m + 1 : m + 1 + nx, m : m + ny]
            else:
                lo = cond_wide[1:-1, m : m + nx, m - 1 : m - 1 + ny]
                hi = cond_wide[1:-1, m : m + nx, m + 1 : m + 1 + ny]
            face_below = 0.5 * (center_c + lo)
            face_above = 0.5 * (center_c + hi)
            faces.append((face_below, face_above))
            diagonal = diagonal + face_below + face_above
        pot_z = jnp.pad(potential, ((0, 0), (1, 1), (0, 0), (0, 0)))
        pot_c = potential[:, :, 1:-1, 1:-1]
        coupled = jnp.zeros_like(pot_c)
        for d in range(3):
            if d == 0:
                lo = pot_z[:, 0:-2, 1:-1, 1:-1]
                hi = pot_z[:, 2:, 1:-1, 1:-1]
            elif d == 1:
                lo = potential[:, :, 0:-2, 1:-1]
                hi = potential[:, :, 2:, 1:-1]
            else:
                lo = potential[:, :, 1:-1, 0:-2]
                hi = potential[:, :, 1:-1, 2:]
            coupled = coupled + faces[d][0] * lo + faces[d][1] * hi
        applied = diagonal * pot_c - coupled
        rhs = source_terms[:, :, m : m + nx, m : m + ny]
        updated = pot_c + OMEGA * (rhs - applied) / diagonal
        potential = jnp.where(on_grid[m : m + nx, m : m + ny], updated, 0.0)

    return (advanced, conductivity, potential)


def solution(mesh):
    in_specs = (
        P("grp", None, "gx", "gy"),
        P(None, "grp", None, "gx", "gy"),
        P("grp", None, "gx", "gy"),
        P("grp", None, "gx", "gy"),
        P(),
        P(),
        P(None, None, "gx", "gy"),
    )
    out_specs = (P("grp", None, "gx", "gy"), P(None, "gx", "gy"), P("grp", None, "gx", "gy"))
    return jax.shard_map(
        on_device, mesh=mesh, in_specs=in_specs, out_specs=out_specs, check_vma=False
    )
```

```python
import functools

import jax
import jax.numpy as jnp
from jax.experimental import pallas as pl
from jax.experimental.pallas import tpu as pltpu
from jax import lax
from jax.sharding import PartitionSpec as P

SWEEPS = 3


KAPPA = 0.06
OMEGA = 0.8
AMPLITUDE = 40.0
ARCHIE = 20.0


def with_halo(shard, sides, width, top=None):
    for axis, dim in sides:
        devices, length = (lax.axis_size(axis), shard.shape[dim])
        last_member = devices if (axis != "grp" or top is None) else top
        up = [(i, i + 1) for i in range(last_member - 1)]
        down = [(j, i) for i, j in up]
        last = lax.slice_in_dim(shard, length - width, length, axis=dim)
        initial = lax.slice_in_dim(shard, 0, width, axis=dim)
        before = lax.ppermute(last, axis, up)
        after = lax.ppermute(initial, axis, down)
        shard = jnp.concatenate([before, shard, after], axis=dim)
    return shard


def transport_halo(c, u, slabs):
    f32 = jnp.float32
    nz, nx, ny = c.shape

    def chain(axis, members):
        up = [(i, i + 1) for i in range(members - 1)]
        return up, [(j, i) for i, j in up]

    up, down = chain("grp", slabs)
    below = lax.ppermute(jnp.concatenate([c[nz - 2 :], u[:, nz - 1].astype(f32)], 0), "grp", up)
    above = lax.ppermute(jnp.concatenate([c[:2], u[:, 0].astype(f32)], 0), "grp", down)
    zlo_c, zlo_u = below[:2], below[2:]
    zhi_c, zhi_u = above[:2], above[2:]

    def zext_c(rows):
        return jnp.concatenate([zlo_c[:, rows], c[:, rows], zhi_c[:, rows]], 0)

    def zext_u(row):
        core = jnp.concatenate(
            [zlo_u[:, None, row], u[:, :, row].astype(f32), zhi_u[:, None, row]], 1
        )
        return jnp.pad(core, ((0, 0), (1, 1), (0, 0)))

    rows = lax.axis_size("gx")
    up, down = chain("gx", rows)
    send_up = jnp.concatenate([zext_c(slice(nx - 2, nx)), jnp.swapaxes(zext_u(nx - 1), 0, 1)], 1)
    send_dn = jnp.concatenate([zext_c(slice(0, 2)), jnp.swapaxes(zext_u(0), 0, 1)], 1)
    bx = lax.ppermute(send_up, "gx", up)
    ax = lax.ppermute(send_dn, "gx", down)

    def xz_c(lanes):
        core = jnp.concatenate([zlo_c[..., lanes], c[..., lanes], zhi_c[..., lanes]], 0)
        return jnp.concatenate([bx[:, 0:2, lanes], core, ax[:, 0:2, lanes]], 1)

    def xz_u(lane):
        core = jnp.pad(
            jnp.concatenate(
                [zlo_u[:, None, :, lane], u[..., lane].astype(f32), zhi_u[:, None, :, lane]], 1
            ),
            ((0, 0), (1, 1), (0, 0)),
        )
        lo = jnp.swapaxes(bx[:, 2:5, lane], 0, 1)[:, :, None]
        hi = jnp.swapaxes(ax[:, 2:5, lane], 0, 1)[:, :, None]
        zero = jnp.zeros_like(lo)
        return jnp.moveaxis(jnp.concatenate([zero, lo, core, hi, zero], 2), 0, 2)

    columns = lax.axis_size("gy")
    up, down = chain("gy", columns)
    by = lax.ppermute(jnp.concatenate([xz_c(slice(ny - 2, ny)), xz_u(ny - 1)], 2), "gy", up)
    ay = lax.ppermute(jnp.concatenate([xz_c(slice(0, 2)), xz_u(0)], 2), "gy", down)

    xc = jnp.concatenate([ax[:, 0:2], jnp.zeros((nz + 4, 4, ny), f32), bx[:, 0:2]], 1)
    xu_hi = jnp.swapaxes(ax[1:-1, 2:5], 0, 1)[:, :, None]
    xu_lo = jnp.swapaxes(bx[1:-1, 2:5], 0, 1)[:, :, None]
    xu = jnp.concatenate([xu_hi, jnp.zeros((3, nz + 2, 6, ny), f32), xu_lo], 2)
    yc = jnp.concatenate([ay[..., 0:2], jnp.zeros((nz + 4, nx + 4, 124), f32), by[..., 0:2]], 2)
    yc = jnp.pad(yc, ((0, 0), (6, 6), (0, 0)))
    yu_hi = jnp.moveaxis(ay[1:-1, :, 2:5], 2, 0)[..., None]
    yu_lo = jnp.moveaxis(by[1:-1, :, 2:5], 2, 0)[..., None]
    yu = jnp.concatenate([yu_hi, jnp.zeros((3, nz + 2, nx + 4, 126), f32), yu_lo], 3)
    yu = jnp.pad(yu, ((0, 0), (0, 0), (6, 6), (0, 0)))
    return zlo_c, zhi_c, zlo_u, zhi_u, xc, xu, yc, yu


def roll(values, shift, axis):
    return pltpu.roll(values, shift % values.shape[axis], axis)


def stencil(c, below, above, speeds):
    running = -6.0 * KAPPA * c
    for d in range(3):
        b, a, s = below[d], above[d], speeds[d]
        running = running + KAPPA * (b + a) - (
            jnp.maximum(s, 0.0) * (c - b) + jnp.minimum(s, 0.0) * (a - c)
        )
    return running


def transport_kernel(
    grid, place, weights, c_ref, v_ref, poro_ref, sat_ref, zlo_c, zhi_c, zlo_u, zhi_u,
    xc, xu, yc, yu, adv_ref, part_ref, F, U, S, SG, H,
):
    nz, nx, ny = c_ref.shape
    wx, wy = F.shape[1], F.shape[2]
    f32 = jnp.float32
    pool_y = (
        lax.broadcasted_iota(jnp.int32, (ny, ny // 2), 0) // 2
        == lax.broadcasted_iota(jnp.int32, (ny, ny // 2), 1)
    ).astype(f32)
    F[0:2, 8 : 8 + nx, 0:ny] = zlo_c[...]
    F[nz + 2 : nz + 4, 8 : 8 + nx, 0:ny] = zhi_c[...]

    def put_c(z, carry):
        F[z + 2, 8 : 8 + nx, 0:ny] = c_ref[z]
        return carry

    lax.fori_loop(0, nz, put_c, 0)
    F[:, 0:8, 0:ny] = xc[...]
    F[:, wx - 8 : wx, 0:ny] = xc[...]
    F[:, :, ny:wy] = yc[...]
    for d in range(3):
        U[d, 0, 8 : 8 + nx, 0:ny] = zlo_u[d]
        U[d, nz + 1, 8 : 8 + nx, 0:ny] = zhi_u[d]

        def put_u(z, carry, d=d):
            U[d, z + 1, 8 : 8 + nx, 0:ny] = v_ref[d, 0, z].astype(f32)
            return carry

        lax.fori_loop(0, nz, put_u, 0)
        U[d, :, 0:8, 0:ny] = xu[d]
        U[d, :, wx - 8 : wx, 0:ny] = xu[d]
        U[d, :, :, ny:wy] = yu[d]

    total_z, total_x, total_y = grid
    gz0 = place[0] * nz - 1
    gx = place[1] * nx - 8 + lax.broadcasted_iota(jnp.int32, (wx, wy), 0)
    lane = lax.broadcasted_iota(jnp.int32, (wx, wy), 1)
    gy = place[2] * ny + jnp.where(lane < ny + (wy - ny) // 2, lane, lane - wy)
    plane = (gx >= 0) & (gx < total_x) & (gy >= 0) & (gy < total_y)

    def first(k, carry):
        c0 = F[k + 1]
        below = (F[k], roll(c0, 1, 0), roll(c0, 1, 1))
        above = (F[k + 2], roll(c0, -1, 0), roll(c0, -1, 1))
        speeds = (U[0, k], U[1, k], U[2, k])
        section = c0 + stencil(c0, below, above, speeds)
        z = gz0 + k
        keep = plane & (z >= 0) & (z < total_z)
        S[k] = jnp.where(keep, section, 0.0)
        return carry

    lax.fori_loop(0, nz + 2, first, 0)

    live = place[3] > 0

    def core(values):
        return values[8 : 8 + nx, 0:ny]

    def second(j, carry):
        s_mid = S[j + 1]
        s0 = core(s_mid)
        below = (core(S[j]), core(roll(s_mid, 1, 0)), core(roll(s_mid, 1, 1)))
        above = (core(S[j + 2]), core(roll(s_mid, -1, 0)), core(roll(s_mid, -1, 1)))
        speeds = tuple(v_ref[d, 0, j].astype(f32) for d in range(3))
        c0 = c_ref[j]
        adv = 0.5 * (c0 + s0 + stencil(s0, below, above, speeds))
        adv = jnp.where(live, adv, 0.0)
        adv_ref[0, j] = adv
        p = poro_ref[0, j].astype(f32)
        w = sat_ref[0, j].astype(f32)
        SG[pl.ds(pl.multiple_of(j * nx, nx), nx)] = ARCHIE * jnp.exp(adv) * p * p * w * w
        return carry

    lax.fori_loop(0, nz, second, 0)
    H[...] = jnp.dot(SG[...], pool_y, precision=lax.Precision.HIGHEST, preferred_element_type=f32)
    half_rows = nz * nx // 2
    coarse = H[pl.ds(0, half_rows, stride=2)] + H[pl.ds(1, half_rows, stride=2)]
    cx = nx // 2
    resist_layers = part_ref.shape[0]
    for e in range(resist_layers):
        total = jnp.zeros((cx, ny // 2), f32)
        for z in range(nz):
            total = total + weights[e, z] * coarse[z * cx : (z + 1) * cx]
        part_ref[e] = total


def transport_call(place, weights, c, velocity, porosity, saturation, *pieces, grid):
    nz, nx, ny = c.shape
    wx, wy = nx + 16, ny + 128
    resist_layers = weights.shape[0]
    vmem = pl.BlockSpec(memory_space=pltpu.VMEM)
    smem = pl.BlockSpec(memory_space=pltpu.SMEM)
    cells = nz * nx * ny
    return pl.pallas_call(
        functools.partial(transport_kernel, grid),
        out_shape=(
            jax.ShapeDtypeStruct((1, nz, nx, ny), jnp.float32),
            jax.ShapeDtypeStruct((resist_layers, nx // 2, ny // 2), jnp.float32),
        ),
        in_specs=[smem, smem] + [vmem] * 12,
        out_specs=(vmem, vmem),
        scratch_shapes=[
            pltpu.VMEM((nz + 4, wx, wy), jnp.float32),
            pltpu.VMEM((3, nz + 2, wx, wy), jnp.float32),
            pltpu.VMEM((nz + 2, wx, wy), jnp.float32),
            pltpu.VMEM((nz * nx, ny), jnp.float32),
            pltpu.VMEM((nz * nx, ny // 2), jnp.float32),
        ],
        compiler_params=pltpu.CompilerParams(vmem_limit_bytes=60 * 1024 * 1024),
        cost_estimate=pl.CostEstimate(
            flops=200 * cells, transcendentals=cells, bytes_accessed=40 * cells
        ),
    )(place, weights, c, velocity, porosity, saturation, *pieces)


def neighbours(padded, direction_index):
    leading = [slice(None)] * (padded.ndim - 3)
    middle = [slice(1, -1)] * 3
    below_slices = list(middle)
    below_slices[direction_index] = slice(0, -2)
    above_slices = list(middle)
    above_slices[direction_index] = slice(2, None)
    return (padded[tuple(leading + below_slices)], padded[tuple(leading + above_slices)])


def tendency(padded, speeds):
    center = padded[1:-1, 1:-1, 1:-1]
    running = -6.0 * KAPPA * center
    for direction_index in range(3):
        below_cells, above_cells = neighbours(padded, direction_index)
        speed_comp = speeds[direction_index]
        running = (
            running
            + KAPPA * (below_cells + above_cells)
            - (
                jnp.maximum(speed_comp, 0.0) * (center - below_cells)
                + jnp.minimum(speed_comp, 0.0) * (above_cells - center)
            )
        )
    return running


def inside(start, count, total):
    ids = start + jnp.arange(count, dtype=jnp.int32)
    return (ids >= 0) & (ids < total)


def plane_halo(values, depth):
    rows, columns = lax.axis_size("gx"), lax.axis_size("gy")
    d = depth

    def line(n, step):
        return [(i, i + step) for i in range(n) if 0 <= i + step < n]

    def flat(i, j):
        return i * columns + j

    def diagonal(di, dj):
        return [
            (flat(i, j), flat(i + di, j + dj))
            for i in range(rows)
            for j in range(columns)
            if 0 <= i + di < rows and 0 <= j + dj < columns
        ]

    both = ("gx", "gy")
    lo_x = lax.ppermute(values[:, -d:, :], "gx", line(rows, 1))
    hi_x = lax.ppermute(values[:, :d, :], "gx", line(rows, -1))
    lo_y = lax.ppermute(values[:, :, -d:], "gy", line(columns, 1))
    hi_y = lax.ppermute(values[:, :, :d], "gy", line(columns, -1))
    lo_lo = lax.ppermute(values[:, -d:, -d:], both, diagonal(1, 1))
    lo_hi = lax.ppermute(values[:, -d:, :d], both, diagonal(1, -1))
    hi_lo = lax.ppermute(values[:, :d, -d:], both, diagonal(-1, 1))
    hi_hi = lax.ppermute(values[:, :d, :d], both, diagonal(-1, -1))
    top = jnp.concatenate([lo_lo, lo_x, lo_hi], 2)
    middle = jnp.concatenate([lo_y, values, hi_y], 2)
    bottom = jnp.concatenate([hi_lo, hi_x, hi_hi], 2)
    return jnp.concatenate([top, middle, bottom], 1)


def grp_sum(partial):
    pair = lax.ppermute(partial, "grp", [(0, 1), (1, 0), (2, 3), (3, 2)])
    partial = partial + pair
    pair = lax.ppermute(partial, "grp", [(0, 2), (2, 0), (1, 3), (3, 1)])
    return partial + pair


def on_device(conc, velocity, porosity, saturation, layer_counts, electrodes, init_potential):
    group_index = lax.axis_index("grp")
    row_index = lax.axis_index("gx")
    column_index = lax.axis_index("gy")
    groups = lax.axis_size("grp")
    rows = lax.axis_size("gx")
    columns = lax.axis_size("gy")
    active = group_index < 3
    field = conc[0]
    layers, tile_x, tile_y = field.shape
    slabs = 3
    speeds = velocity[:, 0]

    ends = jnp.cumsum(layer_counts)
    starts = ends - layer_counts
    layer_ids = group_index * layers + jnp.arange(layers, dtype=jnp.int32)
    member = (
        (layer_ids[None, :] >= starts[:, None]) & (layer_ids[None, :] < ends[:, None]) & active
    ).astype(jnp.float32)
    weights = member / (4.0 * layer_counts.astype(jnp.float32))[:, None]
    resist_layers = layer_counts.shape[0]
    coarse_x = tile_x // 2
    coarse_y = tile_y // 2

    pieces = transport_halo(field, speeds, slabs)
    place = jnp.stack([group_index, row_index, column_index, active.astype(jnp.int32)])
    advanced, partial_cond = transport_call(
        place, weights, field, velocity, porosity, saturation, *pieces,
        grid=(slabs * layers, rows * tile_x, columns * tile_y),
    )
    conductivity = grp_sum(partial_cond)

    grid_x = coarse_x * rows
    grid_y = coarse_y * columns
    depth = SWEEPS
    potential = lax.dynamic_slice_in_dim(init_potential, group_index, 1, 0)
    poles = lax.dynamic_slice_in_dim(electrodes, group_index, 1, 0)

    both = with_halo(jnp.concatenate([conductivity, potential[0]], axis=0), (("gx", 1), ("gy", 2)), depth)
    cond_wide = jnp.pad(both[:resist_layers], ((1, 1), (0, 0), (0, 0)))
    potential = both[None, resist_layers:]
    wide_x = coarse_x + 2 * depth
    wide_y = coarse_y + 2 * depth
    gx_ids = row_index * coarse_x - depth + jnp.arange(wide_x, dtype=jnp.int32)
    gy_ids = column_index * coarse_y - depth + jnp.arange(wide_y, dtype=jnp.int32)
    flat_ids = (
        jnp.arange(resist_layers, dtype=jnp.int32)[:, None, None] * (grid_x * grid_y)
        + gx_ids[None, :, None] * grid_y
        + gy_ids[None, None, :]
    )
    source_terms = AMPLITUDE * (
        (flat_ids[None] == poles[:, 0, None, None, None]).astype(jnp.float32)
        - (flat_ids[None] == poles[:, 1, None, None, None]).astype(jnp.float32)
    )
    on_grid = (
        ((gx_ids >= 0) & (gx_ids < grid_x))[:, None] & ((gy_ids >= 0) & (gy_ids < grid_y))[None, :]
    )

    for sweep_index in range(SWEEPS):
        m = sweep_index + 1
        nx, ny = wide_x - 2 * m, wide_y - 2 * m
        center_c = cond_wide[1:-1, m : m + nx, m : m + ny]
        faces = []
        diagonal = jnp.zeros_like(center_c)
        for d in range(3):
            if d == 0:
                lo = cond_wide[0:-2, m : m + nx, m : m + ny]
                hi = cond_wide[2:, m : m + nx, m : m + ny]
            elif d == 1:
                lo = cond_wide[1:-1, m - 1 : m - 1 + nx, m : m + ny]
                hi = cond_wide[1:-1, m + 1 : m + 1 + nx, m : m + ny]
            else:
                lo = cond_wide[1:-1, m : m + nx, m - 1 : m - 1 + ny]
                hi = cond_wide[1:-1, m : m + nx, m + 1 : m + 1 + ny]
            face_below = 0.5 * (center_c + lo)
            face_above = 0.5 * (center_c + hi)
            faces.append((face_below, face_above))
            diagonal = diagonal + face_below + face_above
        pot_z = jnp.pad(potential, ((0, 0), (1, 1), (0, 0), (0, 0)))
        pot_c = potential[:, :, 1:-1, 1:-1]
        coupled = jnp.zeros_like(pot_c)
        for d in range(3):
            if d == 0:
                lo = pot_z[:, 0:-2, 1:-1, 1:-1]
                hi = pot_z[:, 2:, 1:-1, 1:-1]
            elif d == 1:
                lo = potential[:, :, 0:-2, 1:-1]
                hi = potential[:, :, 2:, 1:-1]
            else:
                lo = potential[:, :, 1:-1, 0:-2]
                hi = potential[:, :, 1:-1, 2:]
            coupled = coupled + faces[d][0] * lo + faces[d][1] * hi
        applied = diagonal * pot_c - coupled
        rhs = source_terms[:, :, m : m + nx, m : m + ny]
        updated = pot_c + OMEGA * (rhs - applied) / diagonal
        potential = jnp.where(on_grid[m : m + nx, m : m + ny], updated, 0.0)

    return (advanced, conductivity, potential)


def solution(mesh):
    in_specs = (
        P("grp", None, "gx", "gy"),
        P(None, "grp", None, "gx", "gy"),
        P("grp", None, "gx", "gy"),
        P("grp", None, "gx", "gy"),
        P(),
        P(),
        P(None, None, "gx", "gy"),
    )
    out_specs = (P("grp", None, "gx", "gy"), P(None, "gx", "gy"), P("grp", None, "gx", "gy"))
    return jax.shard_map(
        on_device, mesh=mesh, in_specs=in_specs, out_specs=out_specs, check_vma=False
    )
```

```python
import functools

import jax
import jax.numpy as jnp
from jax.experimental import pallas as pl
from jax.experimental.pallas import tpu as pltpu
from jax import lax
from jax.sharding import PartitionSpec as P

SWEEPS = 3


KAPPA = 0.06
OMEGA = 0.8
AMPLITUDE = 40.0
ARCHIE = 20.0


def with_halo(shard, sides, width, top=None):
    for axis, dim in sides:
        devices, length = (lax.axis_size(axis), shard.shape[dim])
        last_member = devices if (axis != "grp" or top is None) else top
        up = [(i, i + 1) for i in range(last_member - 1)]
        down = [(j, i) for i, j in up]
        last = lax.slice_in_dim(shard, length - width, length, axis=dim)
        initial = lax.slice_in_dim(shard, 0, width, axis=dim)
        before = lax.ppermute(last, axis, up)
        after = lax.ppermute(initial, axis, down)
        shard = jnp.concatenate([before, shard, after], axis=dim)
    return shard


def faces_kernel(c_ref, v_ref, zs_up, zs_dn, xr, yc_ref, yu_ref):
    nzx, ny = c_ref.shape
    nz = xr.shape[1]
    nx = nzx // nz
    f32 = jnp.float32
    zs_up[0:2] = c_ref[nzx - 2 * nx : nzx].reshape(2, nx, ny)
    zs_dn[0:2] = c_ref[0 : 2 * nx].reshape(2, nx, ny)
    for d in range(3):
        zs_up[2 + d] = v_ref[d, nzx - nx : nzx].astype(f32)
        zs_dn[2 + d] = v_ref[d, 0:nx].astype(f32)
    for z in range(nz):
        base = z * nx
        xr[0, z : z + 1] = c_ref[base + nx - 2 : base + nx - 1]
        xr[1, z : z + 1] = c_ref[base + nx - 1 : base + nx]
        xr[5, z : z + 1] = c_ref[base : base + 1]
        xr[6, z : z + 1] = c_ref[base + 1 : base + 2]
        for d in range(3):
            top = v_ref[d, base + nx - 16 : base + nx].astype(f32)
            bottom = v_ref[d, base : base + 16].astype(f32)
            xr[2 + d, z : z + 1] = top[15:16]
            xr[7 + d, z : z + 1] = bottom[0:1]
    lane = lax.broadcasted_iota(jnp.int32, (8, ny), 1)
    row = lax.broadcasted_iota(jnp.int32, (8, ny), 0)
    pick_c = (
        ((row == 0) & (lane == ny - 2))
        | ((row == 1) & (lane == ny - 1))
        | ((row == 2) & (lane == 0))
        | ((row == 3) & (lane == 1))
    )
    pick_u = ((row == 0) & (lane == ny - 1)) | ((row == 1) & (lane == 0))
    nt = (((1,), (1,)), ((), ()))
    yc_ref[...] = lax.dot_general(
        pick_c.astype(f32), c_ref[...], nt, precision=lax.Precision.HIGHEST,
        preferred_element_type=f32,
    )
    for d in range(3):
        yu_ref[d] = lax.dot_general(
            pick_u.astype(jnp.bfloat16), v_ref[d], nt, preferred_element_type=f32
        )


def faces_call(c, velocity):
    nz, nx, ny = c.shape
    f32 = jnp.float32
    vmem = pl.BlockSpec(memory_space=pltpu.VMEM)
    return pl.pallas_call(
        faces_kernel,
        out_shape=(
            jax.ShapeDtypeStruct((5, nx, ny), f32),
            jax.ShapeDtypeStruct((5, nx, ny), f32),
            jax.ShapeDtypeStruct((10, nz, ny), f32),
            jax.ShapeDtypeStruct((8, nz * nx), f32),
            jax.ShapeDtypeStruct((3, 8, nz * nx), f32),
        ),
        in_specs=[vmem, vmem],
        out_specs=(vmem,) * 5,
        compiler_params=pltpu.CompilerParams(vmem_limit_bytes=32 * 1024 * 1024),
        cost_estimate=pl.CostEstimate(
            flops=2 * 32 * nz * nx * ny, transcendentals=0, bytes_accessed=10 * nz * nx * ny
        ),
    )(c.reshape(nz * nx, ny), velocity.reshape(3, nz * nx, ny))


def transport_halo(c, u, slabs):
    f32 = jnp.float32
    nz, nx, ny = c.shape
    zs_up, zs_dn, xr, ycols, ucols = faces_call(c, u)
    ycols = ycols.reshape(8, nz, nx)
    ucols = ucols.reshape(3, 8, nz, nx)

    def chain(axis, members):
        up = [(i, i + 1) for i in range(members - 1)]
        return up, [(j, i) for i, j in up]

    up, down = chain("grp", slabs)
    below = lax.ppermute(zs_up, "grp", up)
    above = lax.ppermute(zs_dn, "grp", down)
    zlo_c, zlo_u = below[:2], below[2:]
    zhi_c, zhi_u = above[:2], above[2:]

    def zext_c(rows, picked):
        return jnp.concatenate([zlo_c[:, rows], jnp.swapaxes(picked, 0, 1), zhi_c[:, rows]], 0)

    def zext_u(row, picked):
        core = jnp.concatenate([zlo_u[:, None, row], picked, zhi_u[:, None, row]], 1)
        return jnp.pad(core, ((0, 0), (1, 1), (0, 0)))

    rows = lax.axis_size("gx")
    up, down = chain("gx", rows)
    send_up = jnp.concatenate(
        [zext_c(slice(nx - 2, nx), xr[0:2]), jnp.swapaxes(zext_u(nx - 1, xr[2:5]), 0, 1)], 1
    )
    send_dn = jnp.concatenate(
        [zext_c(slice(0, 2), xr[5:7]), jnp.swapaxes(zext_u(0, xr[7:10]), 0, 1)], 1
    )
    bx = lax.ppermute(send_up, "gx", up)
    ax = lax.ppermute(send_dn, "gx", down)

    def xz_c(lanes, picked):
        core = jnp.concatenate([zlo_c[..., lanes], jnp.moveaxis(picked, 0, 2), zhi_c[..., lanes]], 0)
        return jnp.concatenate([bx[:, 0:2, lanes], core, ax[:, 0:2, lanes]], 1)

    def xz_u(lane, picked):
        core = jnp.pad(
            jnp.concatenate([zlo_u[:, None, :, lane], picked, zhi_u[:, None, :, lane]], 1),
            ((0, 0), (1, 1), (0, 0)),
        )
        lo = jnp.swapaxes(bx[:, 2:5, lane], 0, 1)[:, :, None]
        hi = jnp.swapaxes(ax[:, 2:5, lane], 0, 1)[:, :, None]
        zero = jnp.zeros_like(lo)
        return jnp.moveaxis(jnp.concatenate([zero, lo, core, hi, zero], 2), 0, 2)

    columns = lax.axis_size("gy")
    up, down = chain("gy", columns)
    by = lax.ppermute(
        jnp.concatenate([xz_c(slice(ny - 2, ny), ycols[0:2]), xz_u(ny - 1, ucols[:, 0])], 2), "gy", up
    )
    ay = lax.ppermute(
        jnp.concatenate([xz_c(slice(0, 2), ycols[2:4]), xz_u(0, ucols[:, 1])], 2), "gy", down
    )

    xc = jnp.concatenate([ax[:, 0:2], jnp.zeros((nz + 4, 4, ny), f32), bx[:, 0:2]], 1)
    xu_hi = jnp.swapaxes(ax[1:-1, 2:5], 0, 1)[:, :, None]
    xu_lo = jnp.swapaxes(bx[1:-1, 2:5], 0, 1)[:, :, None]
    xu = jnp.concatenate([xu_hi, jnp.zeros((3, nz + 2, 6, ny), f32), xu_lo], 2)
    yc = jnp.concatenate([ay[..., 0:2], jnp.zeros((nz + 4, nx + 4, 124), f32), by[..., 0:2]], 2)
    yc = jnp.pad(yc, ((0, 0), (6, 6), (0, 0)))
    yu_hi = jnp.moveaxis(ay[1:-1, :, 2:5], 2, 0)[..., None]
    yu_lo = jnp.moveaxis(by[1:-1, :, 2:5], 2, 0)[..., None]
    yu = jnp.concatenate([yu_hi, jnp.zeros((3, nz + 2, nx + 4, 126), f32), yu_lo], 3)
    yu = jnp.pad(yu, ((0, 0), (0, 0), (6, 6), (0, 0)))
    return zlo_c, zhi_c, zlo_u, zhi_u, xc, xu, yc, yu


def roll(values, shift, axis):
    return pltpu.roll(values, shift % values.shape[axis], axis)


def stencil(c, below, above, speeds):
    running = -6.0 * KAPPA * c
    for d in range(3):
        b, a, s = below[d], above[d], speeds[d]
        running = running + KAPPA * (b + a) - (
            jnp.maximum(s, 0.0) * (c - b) + jnp.minimum(s, 0.0) * (a - c)
        )
    return running


def transport_kernel(
    grid, place, weights, c_ref, v_ref, poro_ref, sat_ref, zlo_c, zhi_c, zlo_u, zhi_u,
    xc, xu, yc, yu, adv_ref, part_ref, F, U, S, SG, H,
):
    nz, nx, ny = c_ref.shape
    wx, wy = F.shape[1], F.shape[2]
    f32 = jnp.float32
    pool_y = (
        lax.broadcasted_iota(jnp.int32, (ny, ny // 2), 0) // 2
        == lax.broadcasted_iota(jnp.int32, (ny, ny // 2), 1)
    ).astype(f32)
    F[0:2, 8 : 8 + nx, 0:ny] = zlo_c[...]
    F[nz + 2 : nz + 4, 8 : 8 + nx, 0:ny] = zhi_c[...]

    def put_c(z, carry):
        F[z + 2, 8 : 8 + nx, 0:ny] = c_ref[z]
        return carry

    lax.fori_loop(0, nz, put_c, 0)
    F[:, 0:8, 0:ny] = xc[...]
    F[:, wx - 8 : wx, 0:ny] = xc[...]
    F[:, :, ny:wy] = yc[...]
    for d in range(3):
        U[d, 0, 8 : 8 + nx, 0:ny] = zlo_u[d]
        U[d, nz + 1, 8 : 8 + nx, 0:ny] = zhi_u[d]

        def put_u(z, carry, d=d):
            U[d, z + 1, 8 : 8 + nx, 0:ny] = v_ref[d, 0, z].astype(f32)
            return carry

        lax.fori_loop(0, nz, put_u, 0)
        U[d, :, 0:8, 0:ny] = xu[d]
        U[d, :, wx - 8 : wx, 0:ny] = xu[d]
        U[d, :, :, ny:wy] = yu[d]

    total_z, total_x, total_y = grid
    gz0 = place[0] * nz - 1
    gx = place[1] * nx - 8 + lax.broadcasted_iota(jnp.int32, (wx, wy), 0)
    lane = lax.broadcasted_iota(jnp.int32, (wx, wy), 1)
    gy = place[2] * ny + jnp.where(lane < ny + (wy - ny) // 2, lane, lane - wy)
    plane = (gx >= 0) & (gx < total_x) & (gy >= 0) & (gy < total_y)

    def first(k, carry):
        c0 = F[k + 1]
        below = (F[k], roll(c0, 1, 0), roll(c0, 1, 1))
        above = (F[k + 2], roll(c0, -1, 0), roll(c0, -1, 1))
        speeds = (U[0, k], U[1, k], U[2, k])
        section = c0 + stencil(c0, below, above, speeds)
        z = gz0 + k
        keep = plane & (z >= 0) & (z < total_z)
        S[k] = jnp.where(keep, section, 0.0)
        return carry

    lax.fori_loop(0, nz + 2, first, 0)

    live = place[3] > 0

    def core(values):
        return values[8 : 8 + nx, 0:ny]

    def second(j, carry):
        s_mid = S[j + 1]
        s0 = core(s_mid)
        below = (core(S[j]), core(roll(s_mid, 1, 0)), core(roll(s_mid, 1, 1)))
        above = (core(S[j + 2]), core(roll(s_mid, -1, 0)), core(roll(s_mid, -1, 1)))
        speeds = tuple(v_ref[d, 0, j].astype(f32) for d in range(3))
        c0 = c_ref[j]
        adv = 0.5 * (c0 + s0 + stencil(s0, below, above, speeds))
        adv = jnp.where(live, adv, 0.0)
        adv_ref[0, j] = adv
        p = poro_ref[0, j].astype(f32)
        w = sat_ref[0, j].astype(f32)
        SG[pl.ds(pl.multiple_of(j * nx, nx), nx)] = ARCHIE * jnp.exp(adv) * p * p * w * w
        return carry

    lax.fori_loop(0, nz, second, 0)
    H[...] = jnp.dot(SG[...], pool_y, precision=lax.Precision.HIGHEST, preferred_element_type=f32)
    half_rows = nz * nx // 2
    coarse = H[pl.ds(0, half_rows, stride=2)] + H[pl.ds(1, half_rows, stride=2)]
    cx = nx // 2
    resist_layers = part_ref.shape[0]
    for e in range(resist_layers):
        total = jnp.zeros((cx, ny // 2), f32)
        for z in range(nz):
            total = total + weights[e, z] * coarse[z * cx : (z + 1) * cx]
        part_ref[e] = total


def transport_call(place, weights, c, velocity, porosity, saturation, *pieces, grid):
    nz, nx, ny = c.shape
    wx, wy = nx + 16, ny + 128
    resist_layers = weights.shape[0]
    vmem = pl.BlockSpec(memory_space=pltpu.VMEM)
    smem = pl.BlockSpec(memory_space=pltpu.SMEM)
    cells = nz * nx * ny
    return pl.pallas_call(
        functools.partial(transport_kernel, grid),
        out_shape=(
            jax.ShapeDtypeStruct((1, nz, nx, ny), jnp.float32),
            jax.ShapeDtypeStruct((resist_layers, nx // 2, ny // 2), jnp.float32),
        ),
        in_specs=[smem, smem] + [vmem] * 12,
        out_specs=(vmem, vmem),
        scratch_shapes=[
            pltpu.VMEM((nz + 4, wx, wy), jnp.float32),
            pltpu.VMEM((3, nz + 2, wx, wy), jnp.float32),
            pltpu.VMEM((nz + 2, wx, wy), jnp.float32),
            pltpu.VMEM((nz * nx, ny), jnp.float32),
            pltpu.VMEM((nz * nx, ny // 2), jnp.float32),
        ],
        compiler_params=pltpu.CompilerParams(vmem_limit_bytes=60 * 1024 * 1024),
        cost_estimate=pl.CostEstimate(
            flops=200 * cells, transcendentals=cells, bytes_accessed=40 * cells
        ),
    )(place, weights, c, velocity, porosity, saturation, *pieces)


def neighbours(padded, direction_index):
    leading = [slice(None)] * (padded.ndim - 3)
    middle = [slice(1, -1)] * 3
    below_slices = list(middle)
    below_slices[direction_index] = slice(0, -2)
    above_slices = list(middle)
    above_slices[direction_index] = slice(2, None)
    return (padded[tuple(leading + below_slices)], padded[tuple(leading + above_slices)])


def tendency(padded, speeds):
    center = padded[1:-1, 1:-1, 1:-1]
    running = -6.0 * KAPPA * center
    for direction_index in range(3):
        below_cells, above_cells = neighbours(padded, direction_index)
        speed_comp = speeds[direction_index]
        running = (
            running
            + KAPPA * (below_cells + above_cells)
            - (
                jnp.maximum(speed_comp, 0.0) * (center - below_cells)
                + jnp.minimum(speed_comp, 0.0) * (above_cells - center)
            )
        )
    return running


def inside(start, count, total):
    ids = start + jnp.arange(count, dtype=jnp.int32)
    return (ids >= 0) & (ids < total)


def plane_halo(values, depth):
    rows, columns = lax.axis_size("gx"), lax.axis_size("gy")
    d = depth

    def line(n, step):
        return [(i, i + step) for i in range(n) if 0 <= i + step < n]

    def flat(i, j):
        return i * columns + j

    def diagonal(di, dj):
        return [
            (flat(i, j), flat(i + di, j + dj))
            for i in range(rows)
            for j in range(columns)
            if 0 <= i + di < rows and 0 <= j + dj < columns
        ]

    both = ("gx", "gy")
    lo_x = lax.ppermute(values[:, -d:, :], "gx", line(rows, 1))
    hi_x = lax.ppermute(values[:, :d, :], "gx", line(rows, -1))
    lo_y = lax.ppermute(values[:, :, -d:], "gy", line(columns, 1))
    hi_y = lax.ppermute(values[:, :, :d], "gy", line(columns, -1))
    lo_lo = lax.ppermute(values[:, -d:, -d:], both, diagonal(1, 1))
    lo_hi = lax.ppermute(values[:, -d:, :d], both, diagonal(1, -1))
    hi_lo = lax.ppermute(values[:, :d, -d:], both, diagonal(-1, 1))
    hi_hi = lax.ppermute(values[:, :d, :d], both, diagonal(-1, -1))
    top = jnp.concatenate([lo_lo, lo_x, lo_hi], 2)
    middle = jnp.concatenate([lo_y, values, hi_y], 2)
    bottom = jnp.concatenate([hi_lo, hi_x, hi_hi], 2)
    return jnp.concatenate([top, middle, bottom], 1)


def grp_sum(partial):
    pair = lax.ppermute(partial, "grp", [(0, 1), (1, 0), (2, 3), (3, 2)])
    partial = partial + pair
    pair = lax.ppermute(partial, "grp", [(0, 2), (2, 0), (1, 3), (3, 1)])
    return partial + pair


def on_device(conc, velocity, porosity, saturation, layer_counts, electrodes, init_potential):
    group_index = lax.axis_index("grp")
    row_index = lax.axis_index("gx")
    column_index = lax.axis_index("gy")
    groups = lax.axis_size("grp")
    rows = lax.axis_size("gx")
    columns = lax.axis_size("gy")
    active = group_index < 3
    field = conc[0]
    layers, tile_x, tile_y = field.shape
    slabs = 3
    speeds = velocity[:, 0]

    ends = jnp.cumsum(layer_counts)
    starts = ends - layer_counts
    layer_ids = group_index * layers + jnp.arange(layers, dtype=jnp.int32)
    member = (
        (layer_ids[None, :] >= starts[:, None]) & (layer_ids[None, :] < ends[:, None]) & active
    ).astype(jnp.float32)
    weights = member / (4.0 * layer_counts.astype(jnp.float32))[:, None]
    resist_layers = layer_counts.shape[0]
    coarse_x = tile_x // 2
    coarse_y = tile_y // 2

    pieces = transport_halo(field, velocity, slabs)
    place = jnp.stack([group_index, row_index, column_index, active.astype(jnp.int32)])
    advanced, partial_cond = transport_call(
        place, weights, field, velocity, porosity, saturation, *pieces,
        grid=(slabs * layers, rows * tile_x, columns * tile_y),
    )
    conductivity = grp_sum(partial_cond)

    grid_x = coarse_x * rows
    grid_y = coarse_y * columns
    depth = SWEEPS
    potential = lax.dynamic_slice_in_dim(init_potential, group_index, 1, 0)
    poles = lax.dynamic_slice_in_dim(electrodes, group_index, 1, 0)

    both = with_halo(jnp.concatenate([conductivity, potential[0]], axis=0), (("gx", 1), ("gy", 2)), depth)
    cond_wide = jnp.pad(both[:resist_layers], ((1, 1), (0, 0), (0, 0)))
    potential = both[None, resist_layers:]
    wide_x = coarse_x + 2 * depth
    wide_y = coarse_y + 2 * depth
    gx_ids = row_index * coarse_x - depth + jnp.arange(wide_x, dtype=jnp.int32)
    gy_ids = column_index * coarse_y - depth + jnp.arange(wide_y, dtype=jnp.int32)
    flat_ids = (
        jnp.arange(resist_layers, dtype=jnp.int32)[:, None, None] * (grid_x * grid_y)
        + gx_ids[None, :, None] * grid_y
        + gy_ids[None, None, :]
    )
    source_terms = AMPLITUDE * (
        (flat_ids[None] == poles[:, 0, None, None, None]).astype(jnp.float32)
        - (flat_ids[None] == poles[:, 1, None, None, None]).astype(jnp.float32)
    )
    on_grid = (
        ((gx_ids >= 0) & (gx_ids < grid_x))[:, None] & ((gy_ids >= 0) & (gy_ids < grid_y))[None, :]
    )

    for sweep_index in range(SWEEPS):
        m = sweep_index + 1
        nx, ny = wide_x - 2 * m, wide_y - 2 * m
        center_c = cond_wide[1:-1, m : m + nx, m : m + ny]
        faces = []
        diagonal = jnp.zeros_like(center_c)
        for d in range(3):
            if d == 0:
                lo = cond_wide[0:-2, m : m + nx, m : m + ny]
                hi = cond_wide[2:, m : m + nx, m : m + ny]
            elif d == 1:
                lo = cond_wide[1:-1, m - 1 : m - 1 + nx, m : m + ny]
                hi = cond_wide[1:-1, m + 1 : m + 1 + nx, m : m + ny]
            else:
                lo = cond_wide[1:-1, m : m + nx, m - 1 : m - 1 + ny]
                hi = cond_wide[1:-1, m : m + nx, m + 1 : m + 1 + ny]
            face_below = 0.5 * (center_c + lo)
            face_above = 0.5 * (center_c + hi)
            faces.append((face_below, face_above))
            diagonal = diagonal + face_below + face_above
        pot_z = jnp.pad(potential, ((0, 0), (1, 1), (0, 0), (0, 0)))
        pot_c = potential[:, :, 1:-1, 1:-1]
        coupled = jnp.zeros_like(pot_c)
        for d in range(3):
            if d == 0:
                lo = pot_z[:, 0:-2, 1:-1, 1:-1]
                hi = pot_z[:, 2:, 1:-1, 1:-1]
            elif d == 1:
                lo = potential[:, :, 0:-2, 1:-1]
                hi = potential[:, :, 2:, 1:-1]
            else:
                lo = potential[:, :, 1:-1, 0:-2]
                hi = potential[:, :, 1:-1, 2:]
            coupled = coupled + faces[d][0] * lo + faces[d][1] * hi
        applied = diagonal * pot_c - coupled
        rhs = source_terms[:, :, m : m + nx, m : m + ny]
        updated = pot_c + OMEGA * (rhs - applied) / diagonal
        potential = jnp.where(on_grid[m : m + nx, m : m + ny], updated, 0.0)

    return (advanced, conductivity, potential)


def solution(mesh):
    in_specs = (
        P("grp", None, "gx", "gy"),
        P(None, "grp", None, "gx", "gy"),
        P("grp", None, "gx", "gy"),
        P("grp", None, "gx", "gy"),
        P(),
        P(),
        P(None, None, "gx", "gy"),
    )
    out_specs = (P("grp", None, "gx", "gy"), P(None, "gx", "gy"), P("grp", None, "gx", "gy"))
    return jax.shard_map(
        on_device, mesh=mesh, in_specs=in_specs, out_specs=out_specs, check_vma=False
    )
```

```python
import functools

import jax
import jax.numpy as jnp
from jax.experimental import pallas as pl
from jax.experimental.pallas import tpu as pltpu
from jax import lax
from jax.sharding import PartitionSpec as P

SWEEPS = 3


KAPPA = 0.06
OMEGA = 0.8
AMPLITUDE = 40.0
ARCHIE = 20.0


def with_halo(shard, sides, width, top=None):
    for axis, dim in sides:
        devices, length = (lax.axis_size(axis), shard.shape[dim])
        last_member = devices if (axis != "grp" or top is None) else top
        up = [(i, i + 1) for i in range(last_member - 1)]
        down = [(j, i) for i, j in up]
        last = lax.slice_in_dim(shard, length - width, length, axis=dim)
        initial = lax.slice_in_dim(shard, 0, width, axis=dim)
        before = lax.ppermute(last, axis, up)
        after = lax.ppermute(initial, axis, down)
        shard = jnp.concatenate([before, shard, after], axis=dim)
    return shard


def faces_kernel(c_ref, v_ref, zs_up, zs_dn, xr, yc_ref, yu_ref):
    nzx, ny = c_ref.shape
    nz = xr.shape[1]
    nx = nzx // nz
    f32 = jnp.float32
    zs_up[0:2] = c_ref[nzx - 2 * nx : nzx].reshape(2, nx, ny)
    zs_dn[0:2] = c_ref[0 : 2 * nx].reshape(2, nx, ny)
    for d in range(3):
        zs_up[2 + d] = v_ref[d, nzx - nx : nzx].astype(f32)
        zs_dn[2 + d] = v_ref[d, 0:nx].astype(f32)
    for z in range(nz):
        base = z * nx
        xr[0, z : z + 1] = c_ref[base + nx - 2 : base + nx - 1]
        xr[1, z : z + 1] = c_ref[base + nx - 1 : base + nx]
        xr[5, z : z + 1] = c_ref[base : base + 1]
        xr[6, z : z + 1] = c_ref[base + 1 : base + 2]
        for d in range(3):
            top = v_ref[d, base + nx - 16 : base + nx].astype(f32)
            bottom = v_ref[d, base : base + 16].astype(f32)
            xr[2 + d, z : z + 1] = top[15:16]
            xr[7 + d, z : z + 1] = bottom[0:1]
    lane = lax.broadcasted_iota(jnp.int32, (8, ny), 1)
    row = lax.broadcasted_iota(jnp.int32, (8, ny), 0)
    pick_c = (
        ((row == 0) & (lane == ny - 2))
        | ((row == 1) & (lane == ny - 1))
        | ((row == 2) & (lane == 0))
        | ((row == 3) & (lane == 1))
    )
    pick_u = ((row == 0) & (lane == ny - 1)) | ((row == 1) & (lane == 0))
    nt = (((1,), (1,)), ((), ()))
    yc_ref[...] = lax.dot_general(
        pick_c.astype(f32), c_ref[...], nt, precision=lax.Precision.HIGHEST,
        preferred_element_type=f32,
    )
    for d in range(3):
        yu_ref[d] = lax.dot_general(
            pick_u.astype(jnp.bfloat16), v_ref[d], nt, preferred_element_type=f32
        )


def faces_call(c, velocity):
    nz, nx, ny = c.shape
    f32 = jnp.float32
    vmem = pl.BlockSpec(memory_space=pltpu.VMEM)
    return pl.pallas_call(
        faces_kernel,
        out_shape=(
            jax.ShapeDtypeStruct((5, nx, ny), f32),
            jax.ShapeDtypeStruct((5, nx, ny), f32),
            jax.ShapeDtypeStruct((10, nz, ny), f32),
            jax.ShapeDtypeStruct((8, nz * nx), f32),
            jax.ShapeDtypeStruct((3, 8, nz * nx), f32),
        ),
        in_specs=[vmem, vmem],
        out_specs=(vmem,) * 5,
        compiler_params=pltpu.CompilerParams(vmem_limit_bytes=32 * 1024 * 1024),
        cost_estimate=pl.CostEstimate(
            flops=2 * 32 * nz * nx * ny, transcendentals=0, bytes_accessed=10 * nz * nx * ny
        ),
    )(c.reshape(nz * nx, ny), velocity.reshape(3, nz * nx, ny))


def transport_halo(c, u, slabs):
    f32 = jnp.float32
    nz, nx, ny = c.shape
    zs_up, zs_dn, xr, ycols, ucols = faces_call(c, u)
    ycols = ycols.reshape(8, nz, nx)
    ucols = ucols.reshape(3, 8, nz, nx)

    def chain(axis, members):
        up = [(i, i + 1) for i in range(members - 1)]
        return up, [(j, i) for i, j in up]

    up, down = chain("grp", slabs)
    below = lax.ppermute(zs_up, "grp", up)
    above = lax.ppermute(zs_dn, "grp", down)
    zlo_c, zlo_u = below[:2], below[2:]
    zhi_c, zhi_u = above[:2], above[2:]

    def zext_c(rows, picked):
        return jnp.concatenate([zlo_c[:, rows], jnp.swapaxes(picked, 0, 1), zhi_c[:, rows]], 0)

    def zext_u(row, picked):
        core = jnp.concatenate([zlo_u[:, None, row], picked, zhi_u[:, None, row]], 1)
        return jnp.pad(core, ((0, 0), (1, 1), (0, 0)))

    rows = lax.axis_size("gx")
    up, down = chain("gx", rows)
    send_up = jnp.concatenate(
        [zext_c(slice(nx - 2, nx), xr[0:2]), jnp.swapaxes(zext_u(nx - 1, xr[2:5]), 0, 1)], 1
    )
    send_dn = jnp.concatenate(
        [zext_c(slice(0, 2), xr[5:7]), jnp.swapaxes(zext_u(0, xr[7:10]), 0, 1)], 1
    )
    bx = lax.ppermute(send_up, "gx", up)
    ax = lax.ppermute(send_dn, "gx", down)

    def xz_c(lanes, picked):
        core = jnp.concatenate([zlo_c[..., lanes], jnp.moveaxis(picked, 0, 2), zhi_c[..., lanes]], 0)
        return jnp.concatenate([bx[:, 0:2, lanes], core, ax[:, 0:2, lanes]], 1)

    def xz_u(lane, picked):
        core = jnp.pad(
            jnp.concatenate([zlo_u[:, None, :, lane], picked, zhi_u[:, None, :, lane]], 1),
            ((0, 0), (1, 1), (0, 0)),
        )
        lo = jnp.swapaxes(bx[:, 2:5, lane], 0, 1)[:, :, None]
        hi = jnp.swapaxes(ax[:, 2:5, lane], 0, 1)[:, :, None]
        zero = jnp.zeros_like(lo)
        return jnp.moveaxis(jnp.concatenate([zero, lo, core, hi, zero], 2), 0, 2)

    columns = lax.axis_size("gy")
    up, down = chain("gy", columns)
    by = lax.ppermute(
        jnp.concatenate([xz_c(slice(ny - 2, ny), ycols[0:2]), xz_u(ny - 1, ucols[:, 0])], 2), "gy", up
    )
    ay = lax.ppermute(
        jnp.concatenate([xz_c(slice(0, 2), ycols[2:4]), xz_u(0, ucols[:, 1])], 2), "gy", down
    )

    xc = jnp.concatenate([ax[:, 0:2], jnp.zeros((nz + 4, 4, ny), f32), bx[:, 0:2]], 1)
    xu_hi = jnp.swapaxes(ax[1:-1, 2:5], 0, 1)[:, :, None]
    xu_lo = jnp.swapaxes(bx[1:-1, 2:5], 0, 1)[:, :, None]
    xu = jnp.concatenate([xu_hi, jnp.zeros((3, nz + 2, 6, ny), f32), xu_lo], 2)
    fill = jnp.zeros((nz + 4, nx + 4, 118), f32)
    yt = jnp.concatenate([ay[..., 0:2], ay[..., 2:5], fill, by[..., 2:5], by[..., 0:2]], 2)
    yt = jnp.pad(yt, ((0, 0), (6, 6), (0, 0)))
    return zlo_c, zhi_c, zlo_u, zhi_u, xc, xu, yt


def roll(values, shift, axis):
    return pltpu.roll(values, shift % values.shape[axis], axis)


def stencil(c, below, above, speeds):
    running = -6.0 * KAPPA * c
    for d in range(3):
        b, a, s = below[d], above[d], speeds[d]
        running = running + KAPPA * (b + a) - (
            jnp.maximum(s, 0.0) * (c - b) + jnp.minimum(s, 0.0) * (a - c)
        )
    return running


def transport_kernel(
    grid, place, weights, c_ref, v_ref, poro_ref, sat_ref, zlo_c, zhi_c, zlo_u, zhi_u,
    xc, xu, yt, adv_ref, part_ref, F, U, S, SG, H,
):
    nz, nx, ny = c_ref.shape
    wx, wy = F.shape[1], F.shape[2]
    f32 = jnp.float32
    pool_y = (
        lax.broadcasted_iota(jnp.int32, (ny, ny // 2), 0) // 2
        == lax.broadcasted_iota(jnp.int32, (ny, ny // 2), 1)
    ).astype(f32)
    F[0:2, 8 : 8 + nx, 0:ny] = zlo_c[...]
    F[nz + 2 : nz + 4, 8 : 8 + nx, 0:ny] = zhi_c[...]

    def put_c(z, carry):
        F[z + 2, 8 : 8 + nx, 0:ny] = c_ref[z]
        return carry

    lax.fori_loop(0, nz, put_c, 0)
    F[:, 0:8, 0:ny] = xc[...]
    F[:, wx - 8 : wx, 0:ny] = xc[...]
    F[:, :, ny:wy] = yt[...]
    tile_lane = lax.broadcasted_iota(jnp.int32, (wx, wy - ny), 1)
    for d in range(3):
        U[d, 0, 8 : 8 + nx, 0:ny] = zlo_u[d]
        U[d, nz + 1, 8 : 8 + nx, 0:ny] = zhi_u[d]

        def put_u(z, carry, d=d):
            U[d, z + 1, 8 : 8 + nx, 0:ny] = v_ref[d, 0, z].astype(f32)
            return carry

        lax.fori_loop(0, nz, put_u, 0)
        U[d, :, 0:8, 0:ny] = xu[d]
        U[d, :, wx - 8 : wx, 0:ny] = xu[d]

        def put_y(k, carry, d=d):
            tile = yt[k + 1]
            low = roll(tile, -(2 + d), 1)
            high = roll(tile, 4 - d, 1)
            U[d, k, :, ny:wy] = jnp.where(tile_lane < (wy - ny) // 2, low, high)
            return carry

        lax.fori_loop(0, nz + 2, put_y, 0)

    total_z, total_x, total_y = grid
    gz0 = place[0] * nz - 1
    gx = place[1] * nx - 8 + lax.broadcasted_iota(jnp.int32, (wx, wy), 0)
    lane = lax.broadcasted_iota(jnp.int32, (wx, wy), 1)
    gy = place[2] * ny + jnp.where(lane < ny + (wy - ny) // 2, lane, lane - wy)
    plane = (gx >= 0) & (gx < total_x) & (gy >= 0) & (gy < total_y)

    def first(k, carry):
        c0 = F[k + 1]
        below = (F[k], roll(c0, 1, 0), roll(c0, 1, 1))
        above = (F[k + 2], roll(c0, -1, 0), roll(c0, -1, 1))
        speeds = (U[0, k], U[1, k], U[2, k])
        section = c0 + stencil(c0, below, above, speeds)
        z = gz0 + k
        keep = plane & (z >= 0) & (z < total_z)
        S[k] = jnp.where(keep, section, 0.0)
        return carry

    lax.fori_loop(0, nz + 2, first, 0)

    live = place[3] > 0

    def core(values):
        return values[8 : 8 + nx, 0:ny]

    def second(j, carry):
        s_mid = S[j + 1]
        s0 = core(s_mid)
        below = (core(S[j]), core(roll(s_mid, 1, 0)), core(roll(s_mid, 1, 1)))
        above = (core(S[j + 2]), core(roll(s_mid, -1, 0)), core(roll(s_mid, -1, 1)))
        speeds = tuple(v_ref[d, 0, j].astype(f32) for d in range(3))
        c0 = c_ref[j]
        adv = 0.5 * (c0 + s0 + stencil(s0, below, above, speeds))
        adv = jnp.where(live, adv, 0.0)
        adv_ref[0, j] = adv
        p = poro_ref[0, j].astype(f32)
        w = sat_ref[0, j].astype(f32)
        SG[pl.ds(pl.multiple_of(j * nx, nx), nx)] = ARCHIE * jnp.exp(adv) * p * p * w * w
        return carry

    lax.fori_loop(0, nz, second, 0)
    H[...] = jnp.dot(SG[...], pool_y, precision=lax.Precision.HIGHEST, preferred_element_type=f32)
    half_rows = nz * nx // 2
    coarse = H[pl.ds(0, half_rows, stride=2)] + H[pl.ds(1, half_rows, stride=2)]
    cx = nx // 2
    resist_layers = part_ref.shape[0]
    for e in range(resist_layers):
        total = jnp.zeros((cx, ny // 2), f32)
        for z in range(nz):
            total = total + weights[e, z] * coarse[z * cx : (z + 1) * cx]
        part_ref[e] = total


def transport_call(place, weights, c, velocity, porosity, saturation, *pieces, grid):
    nz, nx, ny = c.shape
    wx, wy = nx + 16, ny + 128
    resist_layers = weights.shape[0]
    vmem = pl.BlockSpec(memory_space=pltpu.VMEM)
    smem = pl.BlockSpec(memory_space=pltpu.SMEM)
    cells = nz * nx * ny
    return pl.pallas_call(
        functools.partial(transport_kernel, grid),
        out_shape=(
            jax.ShapeDtypeStruct((1, nz, nx, ny), jnp.float32),
            jax.ShapeDtypeStruct((resist_layers, nx // 2, ny // 2), jnp.float32),
        ),
        in_specs=[smem, smem] + [vmem] * 11,
        out_specs=(vmem, vmem),
        scratch_shapes=[
            pltpu.VMEM((nz + 4, wx, wy), jnp.float32),
            pltpu.VMEM((3, nz + 2, wx, wy), jnp.float32),
            pltpu.VMEM((nz + 2, wx, wy), jnp.float32),
            pltpu.VMEM((nz * nx, ny), jnp.float32),
            pltpu.VMEM((nz * nx, ny // 2), jnp.float32),
        ],
        compiler_params=pltpu.CompilerParams(vmem_limit_bytes=60 * 1024 * 1024),
        cost_estimate=pl.CostEstimate(
            flops=200 * cells, transcendentals=cells, bytes_accessed=40 * cells
        ),
    )(place, weights, c, velocity, porosity, saturation, *pieces)


def neighbours(padded, direction_index):
    leading = [slice(None)] * (padded.ndim - 3)
    middle = [slice(1, -1)] * 3
    below_slices = list(middle)
    below_slices[direction_index] = slice(0, -2)
    above_slices = list(middle)
    above_slices[direction_index] = slice(2, None)
    return (padded[tuple(leading + below_slices)], padded[tuple(leading + above_slices)])


def tendency(padded, speeds):
    center = padded[1:-1, 1:-1, 1:-1]
    running = -6.0 * KAPPA * center
    for direction_index in range(3):
        below_cells, above_cells = neighbours(padded, direction_index)
        speed_comp = speeds[direction_index]
        running = (
            running
            + KAPPA * (below_cells + above_cells)
            - (
                jnp.maximum(speed_comp, 0.0) * (center - below_cells)
                + jnp.minimum(speed_comp, 0.0) * (above_cells - center)
            )
        )
    return running


def inside(start, count, total):
    ids = start + jnp.arange(count, dtype=jnp.int32)
    return (ids >= 0) & (ids < total)


def plane_halo(values, depth):
    rows, columns = lax.axis_size("gx"), lax.axis_size("gy")
    d = depth

    def line(n, step):
        return [(i, i + step) for i in range(n) if 0 <= i + step < n]

    def flat(i, j):
        return i * columns + j

    def diagonal(di, dj):
        return [
            (flat(i, j), flat(i + di, j + dj))
            for i in range(rows)
            for j in range(columns)
            if 0 <= i + di < rows and 0 <= j + dj < columns
        ]

    both = ("gx", "gy")
    lo_x = lax.ppermute(values[:, -d:, :], "gx", line(rows, 1))
    hi_x = lax.ppermute(values[:, :d, :], "gx", line(rows, -1))
    lo_y = lax.ppermute(values[:, :, -d:], "gy", line(columns, 1))
    hi_y = lax.ppermute(values[:, :, :d], "gy", line(columns, -1))
    lo_lo = lax.ppermute(values[:, -d:, -d:], both, diagonal(1, 1))
    lo_hi = lax.ppermute(values[:, -d:, :d], both, diagonal(1, -1))
    hi_lo = lax.ppermute(values[:, :d, -d:], both, diagonal(-1, 1))
    hi_hi = lax.ppermute(values[:, :d, :d], both, diagonal(-1, -1))
    top = jnp.concatenate([lo_lo, lo_x, lo_hi], 2)
    middle = jnp.concatenate([lo_y, values, hi_y], 2)
    bottom = jnp.concatenate([hi_lo, hi_x, hi_hi], 2)
    return jnp.concatenate([top, middle, bottom], 1)


def grp_sum(partial):
    pair = lax.ppermute(partial, "grp", [(0, 1), (1, 0), (2, 3), (3, 2)])
    partial = partial + pair
    pair = lax.ppermute(partial, "grp", [(0, 2), (2, 0), (1, 3), (3, 1)])
    return partial + pair


def on_device(conc, velocity, porosity, saturation, layer_counts, electrodes, init_potential):
    group_index = lax.axis_index("grp")
    row_index = lax.axis_index("gx")
    column_index = lax.axis_index("gy")
    groups = lax.axis_size("grp")
    rows = lax.axis_size("gx")
    columns = lax.axis_size("gy")
    active = group_index < 3
    field = conc[0]
    layers, tile_x, tile_y = field.shape
    slabs = 3
    speeds = velocity[:, 0]

    ends = jnp.cumsum(layer_counts)
    starts = ends - layer_counts
    layer_ids = group_index * layers + jnp.arange(layers, dtype=jnp.int32)
    member = (
        (layer_ids[None, :] >= starts[:, None]) & (layer_ids[None, :] < ends[:, None]) & active
    ).astype(jnp.float32)
    weights = member / (4.0 * layer_counts.astype(jnp.float32))[:, None]
    resist_layers = layer_counts.shape[0]
    coarse_x = tile_x // 2
    coarse_y = tile_y // 2

    pieces = transport_halo(field, velocity, slabs)
    place = jnp.stack([group_index, row_index, column_index, active.astype(jnp.int32)])
    advanced, partial_cond = transport_call(
        place, weights, field, velocity, porosity, saturation, *pieces,
        grid=(slabs * layers, rows * tile_x, columns * tile_y),
    )
    conductivity = grp_sum(partial_cond)

    grid_x = coarse_x * rows
    grid_y = coarse_y * columns
    depth = SWEEPS
    potential = lax.dynamic_slice_in_dim(init_potential, group_index, 1, 0)
    poles = lax.dynamic_slice_in_dim(electrodes, group_index, 1, 0)

    both = with_halo(jnp.concatenate([conductivity, potential[0]], axis=0), (("gx", 1), ("gy", 2)), depth)
    cond_wide = jnp.pad(both[:resist_layers], ((1, 1), (0, 0), (0, 0)))
    potential = both[None, resist_layers:]
    wide_x = coarse_x + 2 * depth
    wide_y = coarse_y + 2 * depth
    gx_ids = row_index * coarse_x - depth + jnp.arange(wide_x, dtype=jnp.int32)
    gy_ids = column_index * coarse_y - depth + jnp.arange(wide_y, dtype=jnp.int32)
    flat_ids = (
        jnp.arange(resist_layers, dtype=jnp.int32)[:, None, None] * (grid_x * grid_y)
        + gx_ids[None, :, None] * grid_y
        + gy_ids[None, None, :]
    )
    source_terms = AMPLITUDE * (
        (flat_ids[None] == poles[:, 0, None, None, None]).astype(jnp.float32)
        - (flat_ids[None] == poles[:, 1, None, None, None]).astype(jnp.float32)
    )
    on_grid = (
        ((gx_ids >= 0) & (gx_ids < grid_x))[:, None] & ((gy_ids >= 0) & (gy_ids < grid_y))[None, :]
    )

    for sweep_index in range(SWEEPS):
        m = sweep_index + 1
        nx, ny = wide_x - 2 * m, wide_y - 2 * m
        center_c = cond_wide[1:-1, m : m + nx, m : m + ny]
        faces = []
        diagonal = jnp.zeros_like(center_c)
        for d in range(3):
            if d == 0:
                lo = cond_wide[0:-2, m : m + nx, m : m + ny]
                hi = cond_wide[2:, m : m + nx, m : m + ny]
            elif d == 1:
                lo = cond_wide[1:-1, m - 1 : m - 1 + nx, m : m + ny]
                hi = cond_wide[1:-1, m + 1 : m + 1 + nx, m : m + ny]
            else:
                lo = cond_wide[1:-1, m : m + nx, m - 1 : m - 1 + ny]
                hi = cond_wide[1:-1, m : m + nx, m + 1 : m + 1 + ny]
            face_below = 0.5 * (center_c + lo)
            face_above = 0.5 * (center_c + hi)
            faces.append((face_below, face_above))
            diagonal = diagonal + face_below + face_above
        pot_z = jnp.pad(potential, ((0, 0), (1, 1), (0, 0), (0, 0)))
        pot_c = potential[:, :, 1:-1, 1:-1]
        coupled = jnp.zeros_like(pot_c)
        for d in range(3):
            if d == 0:
                lo = pot_z[:, 0:-2, 1:-1, 1:-1]
                hi = pot_z[:, 2:, 1:-1, 1:-1]
            elif d == 1:
                lo = potential[:, :, 0:-2, 1:-1]
                hi = potential[:, :, 2:, 1:-1]
            else:
                lo = potential[:, :, 1:-1, 0:-2]
                hi = potential[:, :, 1:-1, 2:]
            coupled = coupled + faces[d][0] * lo + faces[d][1] * hi
        applied = diagonal * pot_c - coupled
        rhs = source_terms[:, :, m : m + nx, m : m + ny]
        updated = pot_c + OMEGA * (rhs - applied) / diagonal
        potential = jnp.where(on_grid[m : m + nx, m : m + ny], updated, 0.0)

    return (advanced, conductivity, potential)


def solution(mesh):
    in_specs = (
        P("grp", None, "gx", "gy"),
        P(None, "grp", None, "gx", "gy"),
        P("grp", None, "gx", "gy"),
        P("grp", None, "gx", "gy"),
        P(),
        P(),
        P(None, None, "gx", "gy"),
    )
    out_specs = (P("grp", None, "gx", "gy"), P(None, "gx", "gy"), P("grp", None, "gx", "gy"))
    return jax.shard_map(
        on_device, mesh=mesh, in_specs=in_specs, out_specs=out_specs, check_vma=False
    )
```

```python
import functools

import jax
import jax.numpy as jnp
from jax.experimental import pallas as pl
from jax.experimental.pallas import tpu as pltpu
from jax import lax
from jax.sharding import PartitionSpec as P

SWEEPS = 3


KAPPA = 0.06
OMEGA = 0.8
AMPLITUDE = 40.0
ARCHIE = 20.0


def with_halo(shard, sides, width, top=None):
    for axis, dim in sides:
        devices, length = (lax.axis_size(axis), shard.shape[dim])
        last_member = devices if (axis != "grp" or top is None) else top
        up = [(i, i + 1) for i in range(last_member - 1)]
        down = [(j, i) for i, j in up]
        last = lax.slice_in_dim(shard, length - width, length, axis=dim)
        initial = lax.slice_in_dim(shard, 0, width, axis=dim)
        before = lax.ppermute(last, axis, up)
        after = lax.ppermute(initial, axis, down)
        shard = jnp.concatenate([before, shard, after], axis=dim)
    return shard


def faces_kernel(c_ref, v_ref, zs_up, zs_dn, xr, yc_ref, yu_ref):
    nzx, ny = c_ref.shape
    nz = xr.shape[1]
    nx = nzx // nz
    f32 = jnp.float32
    zs_up[0:2] = c_ref[nzx - 2 * nx : nzx].reshape(2, nx, ny)
    zs_dn[0:2] = c_ref[0 : 2 * nx].reshape(2, nx, ny)
    for d in range(3):
        zs_up[2 + d] = v_ref[d, nzx - nx : nzx].astype(f32)
        zs_dn[2 + d] = v_ref[d, 0:nx].astype(f32)
    for z in range(nz):
        base = z * nx
        xr[0, z : z + 1] = c_ref[base + nx - 2 : base + nx - 1]
        xr[1, z : z + 1] = c_ref[base + nx - 1 : base + nx]
        xr[5, z : z + 1] = c_ref[base : base + 1]
        xr[6, z : z + 1] = c_ref[base + 1 : base + 2]
        for d in range(3):
            top = v_ref[d, base + nx - 16 : base + nx].astype(f32)
            bottom = v_ref[d, base : base + 16].astype(f32)
            xr[2 + d, z : z + 1] = top[15:16]
            xr[7 + d, z : z + 1] = bottom[0:1]
    lane = lax.broadcasted_iota(jnp.int32, (8, ny), 1)
    row = lax.broadcasted_iota(jnp.int32, (8, ny), 0)
    pick_c = (
        ((row == 0) & (lane == ny - 2))
        | ((row == 1) & (lane == ny - 1))
        | ((row == 2) & (lane == 0))
        | ((row == 3) & (lane == 1))
    )
    pick_u = ((row == 0) & (lane == ny - 1)) | ((row == 1) & (lane == 0))
    nt = (((1,), (1,)), ((), ()))
    yc_ref[...] = lax.dot_general(
        pick_c.astype(f32), c_ref[...], nt, precision=lax.Precision.HIGHEST,
        preferred_element_type=f32,
    )
    for d in range(3):
        yu_ref[d] = lax.dot_general(
            pick_u.astype(jnp.bfloat16), v_ref[d], nt, preferred_element_type=f32
        )


def faces_call(c, velocity):
    nz, nx, ny = c.shape
    f32 = jnp.float32
    vmem = pl.BlockSpec(memory_space=pltpu.VMEM)
    return pl.pallas_call(
        faces_kernel,
        out_shape=(
            jax.ShapeDtypeStruct((5, nx, ny), f32),
            jax.ShapeDtypeStruct((5, nx, ny), f32),
            jax.ShapeDtypeStruct((10, nz, ny), f32),
            jax.ShapeDtypeStruct((8, nz * nx), f32),
            jax.ShapeDtypeStruct((3, 8, nz * nx), f32),
        ),
        in_specs=[vmem, vmem],
        out_specs=(vmem,) * 5,
        compiler_params=pltpu.CompilerParams(vmem_limit_bytes=32 * 1024 * 1024),
        cost_estimate=pl.CostEstimate(
            flops=2 * 32 * nz * nx * ny, transcendentals=0, bytes_accessed=10 * nz * nx * ny
        ),
    )(c.reshape(nz * nx, ny), velocity.reshape(3, nz * nx, ny))


def transport_halo(c, u, slabs):
    f32 = jnp.float32
    nz, nx, ny = c.shape
    zs_up, zs_dn, xr, ycols, ucols = faces_call(c, u)
    ycols = ycols.reshape(8, nz, nx)
    ucols = ucols.reshape(3, 8, nz, nx)

    def chain(axis, members):
        up = [(i, i + 1) for i in range(members - 1)]
        return up, [(j, i) for i, j in up]

    up, down = chain("grp", slabs)
    below = lax.ppermute(zs_up, "grp", up)
    above = lax.ppermute(zs_dn, "grp", down)
    zlo_c, zlo_u = below[:2], below[2:]
    zhi_c, zhi_u = above[:2], above[2:]

    def zext_c(rows, picked):
        return jnp.concatenate([zlo_c[:, rows], jnp.swapaxes(picked, 0, 1), zhi_c[:, rows]], 0)

    def zext_u(row, picked):
        core = jnp.concatenate([zlo_u[:, None, row], picked, zhi_u[:, None, row]], 1)
        return jnp.pad(core, ((0, 0), (1, 1), (0, 0)))

    rows = lax.axis_size("gx")
    up, down = chain("gx", rows)
    send_up = jnp.concatenate(
        [zext_c(slice(nx - 2, nx), xr[0:2]), jnp.swapaxes(zext_u(nx - 1, xr[2:5]), 0, 1)], 1
    )
    send_dn = jnp.concatenate(
        [zext_c(slice(0, 2), xr[5:7]), jnp.swapaxes(zext_u(0, xr[7:10]), 0, 1)], 1
    )
    bx = lax.ppermute(send_up, "gx", up)
    ax = lax.ppermute(send_dn, "gx", down)

    def xz_c(lanes, picked):
        core = jnp.concatenate([zlo_c[..., lanes], jnp.moveaxis(picked, 0, 2), zhi_c[..., lanes]], 0)
        return jnp.concatenate([bx[:, 0:2, lanes], core, ax[:, 0:2, lanes]], 1)

    def xz_u(lane, picked):
        core = jnp.pad(
            jnp.concatenate([zlo_u[:, None, :, lane], picked, zhi_u[:, None, :, lane]], 1),
            ((0, 0), (1, 1), (0, 0)),
        )
        lo = jnp.swapaxes(bx[:, 2:5, lane], 0, 1)[:, :, None]
        hi = jnp.swapaxes(ax[:, 2:5, lane], 0, 1)[:, :, None]
        zero = jnp.zeros_like(lo)
        return jnp.moveaxis(jnp.concatenate([zero, lo, core, hi, zero], 2), 0, 2)

    columns = lax.axis_size("gy")
    up, down = chain("gy", columns)
    by = lax.ppermute(
        jnp.concatenate([xz_c(slice(ny - 2, ny), ycols[0:2]), xz_u(ny - 1, ucols[:, 0])], 2), "gy", up
    )
    ay = lax.ppermute(
        jnp.concatenate([xz_c(slice(0, 2), ycols[2:4]), xz_u(0, ucols[:, 1])], 2), "gy", down
    )

    xc = jnp.concatenate([ax[:, 0:2], jnp.zeros((nz + 4, 4, ny), f32), bx[:, 0:2]], 1)
    xu_hi = jnp.swapaxes(ax[1:-1, 2:5], 0, 1)[:, :, None]
    xu_lo = jnp.swapaxes(bx[1:-1, 2:5], 0, 1)[:, :, None]
    xu = jnp.concatenate([xu_hi, jnp.zeros((3, nz + 2, 6, ny), f32), xu_lo], 2)
    speeds_y = jnp.stack([by[..., 2:5], ay[..., 2:5]], 3).reshape(nz + 4, nx + 4, 6)
    fill = jnp.zeros((nz + 4, nx + 4, 118), f32)
    yt = jnp.concatenate([ay[..., 0:2], speeds_y, fill, by[..., 0:2]], 2)
    yt = jnp.pad(yt, ((0, 0), (6, 6), (0, 0)))
    return zlo_c, zhi_c, zlo_u, zhi_u, xc, xu, yt


def roll(values, shift, axis):
    return pltpu.roll(values, shift % values.shape[axis], axis)


def stencil(c, below, above, speeds):
    running = -6.0 * KAPPA * c
    for d in range(3):
        b, a, s = below[d], above[d], speeds[d]
        running = running + KAPPA * (b + a) - (
            jnp.maximum(s, 0.0) * (c - b) + jnp.minimum(s, 0.0) * (a - c)
        )
    return running


def transport_kernel(
    grid, place, weights, c_ref, v_ref, poro_ref, sat_ref, zlo_c, zhi_c, zlo_u, zhi_u,
    xc, xu, yt, adv_ref, part_ref, F, U, S, SG, H,
):
    nz, nx, ny = c_ref.shape
    wx, wy = F.shape[1], F.shape[2]
    f32 = jnp.float32
    pool_y = (
        lax.broadcasted_iota(jnp.int32, (ny, ny // 2), 0) // 2
        == lax.broadcasted_iota(jnp.int32, (ny, ny // 2), 1)
    ).astype(f32)
    F[0:2, 8 : 8 + nx, 0:ny] = zlo_c[...]
    F[nz + 2 : nz + 4, 8 : 8 + nx, 0:ny] = zhi_c[...]

    def put_c(z, carry):
        F[z + 2, 8 : 8 + nx, 0:ny] = c_ref[z]
        return carry

    lax.fori_loop(0, nz, put_c, 0)
    F[:, 0:8, 0:ny] = xc[...]
    F[:, wx - 8 : wx, 0:ny] = xc[...]
    F[:, :, ny:wy] = yt[...]
    for d in range(3):
        U[d, 0, 8 : 8 + nx, 0:ny] = zlo_u[d]
        U[d, nz + 1, 8 : 8 + nx, 0:ny] = zhi_u[d]

        def put_u(z, carry, d=d):
            U[d, z + 1, 8 : 8 + nx, 0:ny] = v_ref[d, 0, z].astype(f32)
            return carry

        lax.fori_loop(0, nz, put_u, 0)
        U[d, :, 0:8, 0:ny] = xu[d]
        U[d, :, wx - 8 : wx, 0:ny] = xu[d]
        U[d, :, :, ny:wy] = roll(yt[1 : nz + 3], -(3 + 2 * d), 2)

    total_z, total_x, total_y = grid
    gz0 = place[0] * nz - 1
    gx = place[1] * nx - 8 + lax.broadcasted_iota(jnp.int32, (wx, wy), 0)
    lane = lax.broadcasted_iota(jnp.int32, (wx, wy), 1)
    gy = place[2] * ny + jnp.where(lane < ny + (wy - ny) // 2, lane, lane - wy)
    plane = (gx >= 0) & (gx < total_x) & (gy >= 0) & (gy < total_y)

    def first(k, carry):
        c0 = F[k + 1]
        below = (F[k], roll(c0, 1, 0), roll(c0, 1, 1))
        above = (F[k + 2], roll(c0, -1, 0), roll(c0, -1, 1))
        speeds = (U[0, k], U[1, k], U[2, k])
        section = c0 + stencil(c0, below, above, speeds)
        z = gz0 + k
        keep = plane & (z >= 0) & (z < total_z)
        S[k] = jnp.where(keep, section, 0.0)
        return carry

    lax.fori_loop(0, nz + 2, first, 0)

    live = place[3] > 0

    def core(values):
        return values[8 : 8 + nx, 0:ny]

    def second(j, carry):
        s_mid = S[j + 1]
        s0 = core(s_mid)
        below = (core(S[j]), core(roll(s_mid, 1, 0)), core(roll(s_mid, 1, 1)))
        above = (core(S[j + 2]), core(roll(s_mid, -1, 0)), core(roll(s_mid, -1, 1)))
        speeds = tuple(v_ref[d, 0, j].astype(f32) for d in range(3))
        c0 = c_ref[j]
        adv = 0.5 * (c0 + s0 + stencil(s0, below, above, speeds))
        adv = jnp.where(live, adv, 0.0)
        adv_ref[0, j] = adv
        p = poro_ref[0, j].astype(f32)
        w = sat_ref[0, j].astype(f32)
        SG[pl.ds(pl.multiple_of(j * nx, nx), nx)] = ARCHIE * jnp.exp(adv) * p * p * w * w
        return carry

    lax.fori_loop(0, nz, second, 0)
    H[...] = jnp.dot(SG[...], pool_y, precision=lax.Precision.HIGHEST, preferred_element_type=f32)
    half_rows = nz * nx // 2
    coarse = H[pl.ds(0, half_rows, stride=2)] + H[pl.ds(1, half_rows, stride=2)]
    cx = nx // 2
    resist_layers = part_ref.shape[0]
    for e in range(resist_layers):
        total = jnp.zeros((cx, ny // 2), f32)
        for z in range(nz):
            total = total + weights[e, z] * coarse[z * cx : (z + 1) * cx]
        part_ref[e] = total


def transport_call(place, weights, c, velocity, porosity, saturation, *pieces, grid):
    nz, nx, ny = c.shape
    wx, wy = nx + 16, ny + 128
    resist_layers = weights.shape[0]
    vmem = pl.BlockSpec(memory_space=pltpu.VMEM)
    smem = pl.BlockSpec(memory_space=pltpu.SMEM)
    cells = nz * nx * ny
    return pl.pallas_call(
        functools.partial(transport_kernel, grid),
        out_shape=(
            jax.ShapeDtypeStruct((1, nz, nx, ny), jnp.float32),
            jax.ShapeDtypeStruct((resist_layers, nx // 2, ny // 2), jnp.float32),
        ),
        in_specs=[smem, smem] + [vmem] * 11,
        out_specs=(vmem, vmem),
        scratch_shapes=[
            pltpu.VMEM((nz + 4, wx, wy), jnp.float32),
            pltpu.VMEM((3, nz + 2, wx, wy), jnp.float32),
            pltpu.VMEM((nz + 2, wx, wy), jnp.float32),
            pltpu.VMEM((nz * nx, ny), jnp.float32),
            pltpu.VMEM((nz * nx, ny // 2), jnp.float32),
        ],
        compiler_params=pltpu.CompilerParams(vmem_limit_bytes=60 * 1024 * 1024),
        cost_estimate=pl.CostEstimate(
            flops=200 * cells, transcendentals=cells, bytes_accessed=40 * cells
        ),
    )(place, weights, c, velocity, porosity, saturation, *pieces)


def neighbours(padded, direction_index):
    leading = [slice(None)] * (padded.ndim - 3)
    middle = [slice(1, -1)] * 3
    below_slices = list(middle)
    below_slices[direction_index] = slice(0, -2)
    above_slices = list(middle)
    above_slices[direction_index] = slice(2, None)
    return (padded[tuple(leading + below_slices)], padded[tuple(leading + above_slices)])


def tendency(padded, speeds):
    center = padded[1:-1, 1:-1, 1:-1]
    running = -6.0 * KAPPA * center
    for direction_index in range(3):
        below_cells, above_cells = neighbours(padded, direction_index)
        speed_comp = speeds[direction_index]
        running = (
            running
            + KAPPA * (below_cells + above_cells)
            - (
                jnp.maximum(speed_comp, 0.0) * (center - below_cells)
                + jnp.minimum(speed_comp, 0.0) * (above_cells - center)
            )
        )
    return running


def inside(start, count, total):
    ids = start + jnp.arange(count, dtype=jnp.int32)
    return (ids >= 0) & (ids < total)


def plane_halo(values, depth):
    rows, columns = lax.axis_size("gx"), lax.axis_size("gy")
    d = depth

    def line(n, step):
        return [(i, i + step) for i in range(n) if 0 <= i + step < n]

    def flat(i, j):
        return i * columns + j

    def diagonal(di, dj):
        return [
            (flat(i, j), flat(i + di, j + dj))
            for i in range(rows)
            for j in range(columns)
            if 0 <= i + di < rows and 0 <= j + dj < columns
        ]

    both = ("gx", "gy")
    lo_x = lax.ppermute(values[:, -d:, :], "gx", line(rows, 1))
    hi_x = lax.ppermute(values[:, :d, :], "gx", line(rows, -1))
    lo_y = lax.ppermute(values[:, :, -d:], "gy", line(columns, 1))
    hi_y = lax.ppermute(values[:, :, :d], "gy", line(columns, -1))
    lo_lo = lax.ppermute(values[:, -d:, -d:], both, diagonal(1, 1))
    lo_hi = lax.ppermute(values[:, -d:, :d], both, diagonal(1, -1))
    hi_lo = lax.ppermute(values[:, :d, -d:], both, diagonal(-1, 1))
    hi_hi = lax.ppermute(values[:, :d, :d], both, diagonal(-1, -1))
    top = jnp.concatenate([lo_lo, lo_x, lo_hi], 2)
    middle = jnp.concatenate([lo_y, values, hi_y], 2)
    bottom = jnp.concatenate([hi_lo, hi_x, hi_hi], 2)
    return jnp.concatenate([top, middle, bottom], 1)


def grp_sum(partial):
    pair = lax.ppermute(partial, "grp", [(0, 1), (1, 0), (2, 3), (3, 2)])
    partial = partial + pair
    pair = lax.ppermute(partial, "grp", [(0, 2), (2, 0), (1, 3), (3, 1)])
    return partial + pair


def on_device(conc, velocity, porosity, saturation, layer_counts, electrodes, init_potential):
    group_index = lax.axis_index("grp")
    row_index = lax.axis_index("gx")
    column_index = lax.axis_index("gy")
    groups = lax.axis_size("grp")
    rows = lax.axis_size("gx")
    columns = lax.axis_size("gy")
    active = group_index < 3
    field = conc[0]
    layers, tile_x, tile_y = field.shape
    slabs = 3
    speeds = velocity[:, 0]

    ends = jnp.cumsum(layer_counts)
    starts = ends - layer_counts
    layer_ids = group_index * layers + jnp.arange(layers, dtype=jnp.int32)
    member = (
        (layer_ids[None, :] >= starts[:, None]) & (layer_ids[None, :] < ends[:, None]) & active
    ).astype(jnp.float32)
    weights = member / (4.0 * layer_counts.astype(jnp.float32))[:, None]
    resist_layers = layer_counts.shape[0]
    coarse_x = tile_x // 2
    coarse_y = tile_y // 2

    pieces = transport_halo(field, velocity, slabs)
    place = jnp.stack([group_index, row_index, column_index, active.astype(jnp.int32)])
    advanced, partial_cond = transport_call(
        place, weights, field, velocity, porosity, saturation, *pieces,
        grid=(slabs * layers, rows * tile_x, columns * tile_y),
    )
    conductivity = grp_sum(partial_cond)

    grid_x = coarse_x * rows
    grid_y = coarse_y * columns
    depth = SWEEPS
    potential = lax.dynamic_slice_in_dim(init_potential, group_index, 1, 0)
    poles = lax.dynamic_slice_in_dim(electrodes, group_index, 1, 0)

    both = with_halo(jnp.concatenate([conductivity, potential[0]], axis=0), (("gx", 1), ("gy", 2)), depth)
    cond_wide = jnp.pad(both[:resist_layers], ((1, 1), (0, 0), (0, 0)))
    potential = both[None, resist_layers:]
    wide_x = coarse_x + 2 * depth
    wide_y = coarse_y + 2 * depth
    gx_ids = row_index * coarse_x - depth + jnp.arange(wide_x, dtype=jnp.int32)
    gy_ids = column_index * coarse_y - depth + jnp.arange(wide_y, dtype=jnp.int32)
    flat_ids = (
        jnp.arange(resist_layers, dtype=jnp.int32)[:, None, None] * (grid_x * grid_y)
        + gx_ids[None, :, None] * grid_y
        + gy_ids[None, None, :]
    )
    source_terms = AMPLITUDE * (
        (flat_ids[None] == poles[:, 0, None, None, None]).astype(jnp.float32)
        - (flat_ids[None] == poles[:, 1, None, None, None]).astype(jnp.float32)
    )
    on_grid = (
        ((gx_ids >= 0) & (gx_ids < grid_x))[:, None] & ((gy_ids >= 0) & (gy_ids < grid_y))[None, :]
    )

    for sweep_index in range(SWEEPS):
        m = sweep_index + 1
        nx, ny = wide_x - 2 * m, wide_y - 2 * m
        center_c = cond_wide[1:-1, m : m + nx, m : m + ny]
        faces = []
        diagonal = jnp.zeros_like(center_c)
        for d in range(3):
            if d == 0:
                lo = cond_wide[0:-2, m : m + nx, m : m + ny]
                hi = cond_wide[2:, m : m + nx, m : m + ny]
            elif d == 1:
                lo = cond_wide[1:-1, m - 1 : m - 1 + nx, m : m + ny]
                hi = cond_wide[1:-1, m + 1 : m + 1 + nx, m : m + ny]
            else:
                lo = cond_wide[1:-1, m : m + nx, m - 1 : m - 1 + ny]
                hi = cond_wide[1:-1, m : m + nx, m + 1 : m + 1 + ny]
            face_below = 0.5 * (center_c + lo)
            face_above = 0.5 * (center_c + hi)
            faces.append((face_below, face_above))
            diagonal = diagonal + face_below + face_above
        pot_z = jnp.pad(potential, ((0, 0), (1, 1), (0, 0), (0, 0)))
        pot_c = potential[:, :, 1:-1, 1:-1]
        coupled = jnp.zeros_like(pot_c)
        for d in range(3):
            if d == 0:
                lo = pot_z[:, 0:-2, 1:-1, 1:-1]
                hi = pot_z[:, 2:, 1:-1, 1:-1]
            elif d == 1:
                lo = potential[:, :, 0:-2, 1:-1]
                hi = potential[:, :, 2:, 1:-1]
            else:
                lo = potential[:, :, 1:-1, 0:-2]
                hi = potential[:, :, 1:-1, 2:]
            coupled = coupled + faces[d][0] * lo + faces[d][1] * hi
        applied = diagonal * pot_c - coupled
        rhs = source_terms[:, :, m : m + nx, m : m + ny]
        updated = pot_c + OMEGA * (rhs - applied) / diagonal
        potential = jnp.where(on_grid[m : m + nx, m : m + ny], updated, 0.0)

    return (advanced, conductivity, potential)


def solution(mesh):
    in_specs = (
        P("grp", None, "gx", "gy"),
        P(None, "grp", None, "gx", "gy"),
        P("grp", None, "gx", "gy"),
        P("grp", None, "gx", "gy"),
        P(),
        P(),
        P(None, None, "gx", "gy"),
    )
    out_specs = (P("grp", None, "gx", "gy"), P(None, "gx", "gy"), P("grp", None, "gx", "gy"))
    return jax.shard_map(
        on_device, mesh=mesh, in_specs=in_specs, out_specs=out_specs, check_vma=False
    )
```

```python
import functools

import jax
import jax.numpy as jnp
from jax.experimental import pallas as pl
from jax.experimental.pallas import tpu as pltpu
from jax import lax
from jax.sharding import PartitionSpec as P

SWEEPS = 3


KAPPA = 0.06
OMEGA = 0.8
AMPLITUDE = 40.0
ARCHIE = 20.0


def with_halo(shard, sides, width, top=None):
    for axis, dim in sides:
        devices, length = (lax.axis_size(axis), shard.shape[dim])
        last_member = devices if (axis != "grp" or top is None) else top
        up = [(i, i + 1) for i in range(last_member - 1)]
        down = [(j, i) for i, j in up]
        last = lax.slice_in_dim(shard, length - width, length, axis=dim)
        initial = lax.slice_in_dim(shard, 0, width, axis=dim)
        if dim == shard.ndim - 1:
            before = jnp.swapaxes(lax.ppermute(jnp.swapaxes(last, -1, -2), axis, up), -1, -2)
            after = jnp.swapaxes(lax.ppermute(jnp.swapaxes(initial, -1, -2), axis, down), -1, -2)
        else:
            before = lax.ppermute(last, axis, up)
            after = lax.ppermute(initial, axis, down)
        shard = jnp.concatenate([before, shard, after], axis=dim)
    return shard


def faces_kernel(c_ref, v_ref, zs_up, zs_dn, xr, yc_ref, yu_ref):
    nzx, ny = c_ref.shape
    nz = xr.shape[1]
    nx = nzx // nz
    f32 = jnp.float32
    zs_up[0:2] = c_ref[nzx - 2 * nx : nzx].reshape(2, nx, ny)
    zs_dn[0:2] = c_ref[0 : 2 * nx].reshape(2, nx, ny)
    for d in range(3):
        zs_up[2 + d] = v_ref[d, nzx - nx : nzx].astype(f32)
        zs_dn[2 + d] = v_ref[d, 0:nx].astype(f32)
    for z in range(nz):
        base = z * nx
        xr[0, z : z + 1] = c_ref[base + nx - 2 : base + nx - 1]
        xr[1, z : z + 1] = c_ref[base + nx - 1 : base + nx]
        xr[5, z : z + 1] = c_ref[base : base + 1]
        xr[6, z : z + 1] = c_ref[base + 1 : base + 2]
        for d in range(3):
            top = v_ref[d, base + nx - 16 : base + nx].astype(f32)
            bottom = v_ref[d, base : base + 16].astype(f32)
            xr[2 + d, z : z + 1] = top[15:16]
            xr[7 + d, z : z + 1] = bottom[0:1]
    lane = lax.broadcasted_iota(jnp.int32, (8, ny), 1)
    row = lax.broadcasted_iota(jnp.int32, (8, ny), 0)
    pick_c = (
        ((row == 0) & (lane == ny - 2))
        | ((row == 1) & (lane == ny - 1))
        | ((row == 2) & (lane == 0))
        | ((row == 3) & (lane == 1))
    )
    pick_u = ((row == 0) & (lane == ny - 1)) | ((row == 1) & (lane == 0))
    nt = (((1,), (1,)), ((), ()))
    yc_ref[...] = lax.dot_general(
        pick_c.astype(f32), c_ref[...], nt, precision=lax.Precision.HIGHEST,
        preferred_element_type=f32,
    )
    for d in range(3):
        yu_ref[d] = lax.dot_general(
            pick_u.astype(jnp.bfloat16), v_ref[d], nt, preferred_element_type=f32
        )


def faces_call(c, velocity):
    nz, nx, ny = c.shape
    f32 = jnp.float32
    vmem = pl.BlockSpec(memory_space=pltpu.VMEM)
    return pl.pallas_call(
        faces_kernel,
        out_shape=(
            jax.ShapeDtypeStruct((5, nx, ny), f32),
            jax.ShapeDtypeStruct((5, nx, ny), f32),
            jax.ShapeDtypeStruct((10, nz, ny), f32),
            jax.ShapeDtypeStruct((8, nz * nx), f32),
            jax.ShapeDtypeStruct((3, 8, nz * nx), f32),
        ),
        in_specs=[vmem, vmem],
        out_specs=(vmem,) * 5,
        compiler_params=pltpu.CompilerParams(vmem_limit_bytes=32 * 1024 * 1024),
        cost_estimate=pl.CostEstimate(
            flops=2 * 32 * nz * nx * ny, transcendentals=0, bytes_accessed=10 * nz * nx * ny
        ),
    )(c.reshape(nz * nx, ny), velocity.reshape(3, nz * nx, ny))


def transport_halo(c, u, slabs):
    f32 = jnp.float32
    nz, nx, ny = c.shape
    zs_up, zs_dn, xr, ycols, ucols = faces_call(c, u)
    ycols = ycols.reshape(8, nz, nx)
    ucols = ucols.reshape(3, 8, nz, nx)

    def chain(axis, members):
        up = [(i, i + 1) for i in range(members - 1)]
        return up, [(j, i) for i, j in up]

    up, down = chain("grp", slabs)
    below = lax.ppermute(zs_up, "grp", up)
    above = lax.ppermute(zs_dn, "grp", down)
    zlo_c, zlo_u = below[:2], below[2:]
    zhi_c, zhi_u = above[:2], above[2:]

    def zext_c(rows, picked):
        return jnp.concatenate([zlo_c[:, rows], jnp.swapaxes(picked, 0, 1), zhi_c[:, rows]], 0)

    def zext_u(row, picked):
        core = jnp.concatenate([zlo_u[:, None, row], picked, zhi_u[:, None, row]], 1)
        return jnp.pad(core, ((0, 0), (1, 1), (0, 0)))

    rows = lax.axis_size("gx")
    up, down = chain("gx", rows)
    send_up = jnp.concatenate(
        [zext_c(slice(nx - 2, nx), xr[0:2]), jnp.swapaxes(zext_u(nx - 1, xr[2:5]), 0, 1)], 1
    )
    send_dn = jnp.concatenate(
        [zext_c(slice(0, 2), xr[5:7]), jnp.swapaxes(zext_u(0, xr[7:10]), 0, 1)], 1
    )
    bx = lax.ppermute(send_up, "gx", up)
    ax = lax.ppermute(send_dn, "gx", down)

    def xz_c(lanes, picked):
        core = jnp.concatenate([zlo_c[..., lanes], jnp.moveaxis(picked, 0, 2), zhi_c[..., lanes]], 0)
        return jnp.concatenate([bx[:, 0:2, lanes], core, ax[:, 0:2, lanes]], 1)

    def xz_u(lane, picked):
        core = jnp.pad(
            jnp.concatenate([zlo_u[:, None, :, lane], picked, zhi_u[:, None, :, lane]], 1),
            ((0, 0), (1, 1), (0, 0)),
        )
        lo = jnp.swapaxes(bx[:, 2:5, lane], 0, 1)[:, :, None]
        hi = jnp.swapaxes(ax[:, 2:5, lane], 0, 1)[:, :, None]
        zero = jnp.zeros_like(lo)
        return jnp.moveaxis(jnp.concatenate([zero, lo, core, hi, zero], 2), 0, 2)

    columns = lax.axis_size("gy")
    up, down = chain("gy", columns)
    by = lax.ppermute(
        jnp.concatenate([xz_c(slice(ny - 2, ny), ycols[0:2]), xz_u(ny - 1, ucols[:, 0])], 2), "gy", up
    )
    ay = lax.ppermute(
        jnp.concatenate([xz_c(slice(0, 2), ycols[2:4]), xz_u(0, ucols[:, 1])], 2), "gy", down
    )

    xc = jnp.concatenate([ax[:, 0:2], jnp.zeros((nz + 4, 4, ny), f32), bx[:, 0:2]], 1)
    xu_hi = jnp.swapaxes(ax[1:-1, 2:5], 0, 1)[:, :, None]
    xu_lo = jnp.swapaxes(bx[1:-1, 2:5], 0, 1)[:, :, None]
    xu = jnp.concatenate([xu_hi, jnp.zeros((3, nz + 2, 6, ny), f32), xu_lo], 2)
    speeds_y = jnp.stack([by[..., 2:5], ay[..., 2:5]], 3).reshape(nz + 4, nx + 4, 6)
    fill = jnp.zeros((nz + 4, nx + 4, 118), f32)
    yt = jnp.concatenate([ay[..., 0:2], speeds_y, fill, by[..., 0:2]], 2)
    yt = jnp.pad(yt, ((0, 0), (6, 6), (0, 0)))
    return below, above, xc, xu, yt


def roll(values, shift, axis):
    return pltpu.roll(values, shift % values.shape[axis], axis)


def stencil(c, below, above, speeds):
    running = -6.0 * KAPPA * c
    for d in range(3):
        b, a, s = below[d], above[d], speeds[d]
        running = running + KAPPA * (b + a) - (
            jnp.maximum(s, 0.0) * (c - b) + jnp.minimum(s, 0.0) * (a - c)
        )
    return running


def transport_kernel(
    grid, place, weights, c_ref, v_ref, poro_ref, sat_ref, z_below, z_above,
    xc, xu, yt, adv_ref, part_ref, F, U, S, SG, H,
):
    nz, nx, ny = c_ref.shape
    wx, wy = F.shape[1], F.shape[2]
    f32 = jnp.float32
    pool_y = (
        lax.broadcasted_iota(jnp.int32, (ny, ny // 2), 0) // 2
        == lax.broadcasted_iota(jnp.int32, (ny, ny // 2), 1)
    ).astype(f32)
    F[0:2, 8 : 8 + nx, 0:ny] = z_below[0:2]
    F[nz + 2 : nz + 4, 8 : 8 + nx, 0:ny] = z_above[0:2]

    def put_c(z, carry):
        F[z + 2, 8 : 8 + nx, 0:ny] = c_ref[z]
        return carry

    lax.fori_loop(0, nz, put_c, 0)
    F[:, 0:8, 0:ny] = xc[...]
    F[:, wx - 8 : wx, 0:ny] = xc[...]
    F[:, :, ny:wy] = yt[...]
    for d in range(3):
        U[d, 0, 8 : 8 + nx, 0:ny] = z_below[2 + d]
        U[d, nz + 1, 8 : 8 + nx, 0:ny] = z_above[2 + d]

        def put_u(z, carry, d=d):
            U[d, z + 1, 8 : 8 + nx, 0:ny] = v_ref[d, 0, z].astype(f32)
            return carry

        lax.fori_loop(0, nz, put_u, 0)
        U[d, :, 0:8, 0:ny] = xu[d]
        U[d, :, wx - 8 : wx, 0:ny] = xu[d]
        U[d, :, :, ny:wy] = roll(yt[1 : nz + 3], -(3 + 2 * d), 2)

    total_z, total_x, total_y = grid
    gz0 = place[0] * nz - 1
    gx = place[1] * nx - 8 + lax.broadcasted_iota(jnp.int32, (wx, wy), 0)
    lane = lax.broadcasted_iota(jnp.int32, (wx, wy), 1)
    gy = place[2] * ny + jnp.where(lane < ny + (wy - ny) // 2, lane, lane - wy)
    plane = (gx >= 0) & (gx < total_x) & (gy >= 0) & (gy < total_y)

    def first(k, carry):
        c0 = F[k + 1]
        below = (F[k], roll(c0, 1, 0), roll(c0, 1, 1))
        above = (F[k + 2], roll(c0, -1, 0), roll(c0, -1, 1))
        speeds = (U[0, k], U[1, k], U[2, k])
        section = c0 + stencil(c0, below, above, speeds)
        z = gz0 + k
        keep = plane & (z >= 0) & (z < total_z)
        S[k] = jnp.where(keep, section, 0.0)
        return carry

    lax.fori_loop(0, nz + 2, first, 0)

    live = place[3] > 0

    def core(values):
        return values[8 : 8 + nx, 0:ny]

    def second(j, carry):
        s_mid = S[j + 1]
        s0 = core(s_mid)
        below = (core(S[j]), core(roll(s_mid, 1, 0)), core(roll(s_mid, 1, 1)))
        above = (core(S[j + 2]), core(roll(s_mid, -1, 0)), core(roll(s_mid, -1, 1)))
        speeds = tuple(v_ref[d, 0, j].astype(f32) for d in range(3))
        c0 = c_ref[j]
        adv = 0.5 * (c0 + s0 + stencil(s0, below, above, speeds))
        adv = jnp.where(live, adv, 0.0)
        adv_ref[0, j] = adv
        p = poro_ref[0, j].astype(f32)
        w = sat_ref[0, j].astype(f32)
        SG[pl.ds(pl.multiple_of(j * nx, nx), nx)] = ARCHIE * jnp.exp(adv) * p * p * w * w
        return carry

    lax.fori_loop(0, nz, second, 0)
    H[...] = jnp.dot(SG[...], pool_y, precision=lax.Precision.HIGHEST, preferred_element_type=f32)
    half_rows = nz * nx // 2
    coarse = H[pl.ds(0, half_rows, stride=2)] + H[pl.ds(1, half_rows, stride=2)]
    cx = nx // 2
    resist_layers = part_ref.shape[0]
    for e in range(resist_layers):
        total = jnp.zeros((cx, ny // 2), f32)
        for z in range(nz):
            total = total + weights[e, z] * coarse[z * cx : (z + 1) * cx]
        part_ref[e] = total


def transport_call(place, weights, c, velocity, porosity, saturation, *pieces, grid):
    nz, nx, ny = c.shape
    wx, wy = nx + 16, ny + 128
    resist_layers = weights.shape[0]
    vmem = pl.BlockSpec(memory_space=pltpu.VMEM)
    smem = pl.BlockSpec(memory_space=pltpu.SMEM)
    cells = nz * nx * ny
    return pl.pallas_call(
        functools.partial(transport_kernel, grid),
        out_shape=(
            jax.ShapeDtypeStruct((1, nz, nx, ny), jnp.float32),
            jax.ShapeDtypeStruct((resist_layers, nx // 2, ny // 2), jnp.float32),
        ),
        in_specs=[smem, smem] + [vmem] * 9,
        out_specs=(vmem, vmem),
        scratch_shapes=[
            pltpu.VMEM((nz + 4, wx, wy), jnp.float32),
            pltpu.VMEM((3, nz + 2, wx, wy), jnp.float32),
            pltpu.VMEM((nz + 2, wx, wy), jnp.float32),
            pltpu.VMEM((nz * nx, ny), jnp.float32),
            pltpu.VMEM((nz * nx, ny // 2), jnp.float32),
        ],
        compiler_params=pltpu.CompilerParams(vmem_limit_bytes=60 * 1024 * 1024),
        cost_estimate=pl.CostEstimate(
            flops=200 * cells, transcendentals=cells, bytes_accessed=40 * cells
        ),
    )(place, weights, c, velocity, porosity, saturation, *pieces)


def neighbours(padded, direction_index):
    leading = [slice(None)] * (padded.ndim - 3)
    middle = [slice(1, -1)] * 3
    below_slices = list(middle)
    below_slices[direction_index] = slice(0, -2)
    above_slices = list(middle)
    above_slices[direction_index] = slice(2, None)
    return (padded[tuple(leading + below_slices)], padded[tuple(leading + above_slices)])


def tendency(padded, speeds):
    center = padded[1:-1, 1:-1, 1:-1]
    running = -6.0 * KAPPA * center
    for direction_index in range(3):
        below_cells, above_cells = neighbours(padded, direction_index)
        speed_comp = speeds[direction_index]
        running = (
            running
            + KAPPA * (below_cells + above_cells)
            - (
                jnp.maximum(speed_comp, 0.0) * (center - below_cells)
                + jnp.minimum(speed_comp, 0.0) * (above_cells - center)
            )
        )
    return running


def inside(start, count, total):
    ids = start + jnp.arange(count, dtype=jnp.int32)
    return (ids >= 0) & (ids < total)


def plane_halo(values, depth):
    rows, columns = lax.axis_size("gx"), lax.axis_size("gy")
    d = depth

    def line(n, step):
        return [(i, i + step) for i in range(n) if 0 <= i + step < n]

    def flat(i, j):
        return i * columns + j

    def diagonal(di, dj):
        return [
            (flat(i, j), flat(i + di, j + dj))
            for i in range(rows)
            for j in range(columns)
            if 0 <= i + di < rows and 0 <= j + dj < columns
        ]

    both = ("gx", "gy")
    lo_x = lax.ppermute(values[:, -d:, :], "gx", line(rows, 1))
    hi_x = lax.ppermute(values[:, :d, :], "gx", line(rows, -1))
    lo_y = lax.ppermute(values[:, :, -d:], "gy", line(columns, 1))
    hi_y = lax.ppermute(values[:, :, :d], "gy", line(columns, -1))
    lo_lo = lax.ppermute(values[:, -d:, -d:], both, diagonal(1, 1))
    lo_hi = lax.ppermute(values[:, -d:, :d], both, diagonal(1, -1))
    hi_lo = lax.ppermute(values[:, :d, -d:], both, diagonal(-1, 1))
    hi_hi = lax.ppermute(values[:, :d, :d], both, diagonal(-1, -1))
    top = jnp.concatenate([lo_lo, lo_x, lo_hi], 2)
    middle = jnp.concatenate([lo_y, values, hi_y], 2)
    bottom = jnp.concatenate([hi_lo, hi_x, hi_hi], 2)
    return jnp.concatenate([top, middle, bottom], 1)


def grp_sum(partial):
    pair = lax.ppermute(partial, "grp", [(0, 1), (1, 0), (2, 3), (3, 2)])
    partial = partial + pair
    pair = lax.ppermute(partial, "grp", [(0, 2), (2, 0), (1, 3), (3, 1)])
    return partial + pair


def on_device(conc, velocity, porosity, saturation, layer_counts, electrodes, init_potential):
    group_index = lax.axis_index("grp")
    row_index = lax.axis_index("gx")
    column_index = lax.axis_index("gy")
    groups = lax.axis_size("grp")
    rows = lax.axis_size("gx")
    columns = lax.axis_size("gy")
    active = group_index < 3
    field = conc[0]
    layers, tile_x, tile_y = field.shape
    slabs = 3
    speeds = velocity[:, 0]

    ends = jnp.cumsum(layer_counts)
    starts = ends - layer_counts
    layer_ids = group_index * layers + jnp.arange(layers, dtype=jnp.int32)
    member = (
        (layer_ids[None, :] >= starts[:, None]) & (layer_ids[None, :] < ends[:, None]) & active
    ).astype(jnp.float32)
    weights = member / (4.0 * layer_counts.astype(jnp.float32))[:, None]
    resist_layers = layer_counts.shape[0]
    coarse_x = tile_x // 2
    coarse_y = tile_y // 2

    pieces = transport_halo(field, velocity, slabs)
    place = jnp.stack([group_index, row_index, column_index, active.astype(jnp.int32)])
    advanced, partial_cond = transport_call(
        place, weights, field, velocity, porosity, saturation, *pieces,
        grid=(slabs * layers, rows * tile_x, columns * tile_y),
    )
    conductivity = grp_sum(partial_cond)

    grid_x = coarse_x * rows
    grid_y = coarse_y * columns
    depth = SWEEPS
    potential = lax.dynamic_slice_in_dim(init_potential, group_index, 1, 0)
    poles = lax.dynamic_slice_in_dim(electrodes, group_index, 1, 0)

    both = with_halo(jnp.concatenate([conductivity, potential[0]], axis=0), (("gx", 1), ("gy", 2)), depth)
    cond_wide = jnp.pad(both[:resist_layers], ((1, 1), (0, 0), (0, 0)))
    potential = both[None, resist_layers:]
    wide_x = coarse_x + 2 * depth
    wide_y = coarse_y + 2 * depth
    gx_ids = row_index * coarse_x - depth + jnp.arange(wide_x, dtype=jnp.int32)
    gy_ids = column_index * coarse_y - depth + jnp.arange(wide_y, dtype=jnp.int32)
    flat_ids = (
        jnp.arange(resist_layers, dtype=jnp.int32)[:, None, None] * (grid_x * grid_y)
        + gx_ids[None, :, None] * grid_y
        + gy_ids[None, None, :]
    )
    source_terms = AMPLITUDE * (
        (flat_ids[None] == poles[:, 0, None, None, None]).astype(jnp.float32)
        - (flat_ids[None] == poles[:, 1, None, None, None]).astype(jnp.float32)
    )
    on_grid = (
        ((gx_ids >= 0) & (gx_ids < grid_x))[:, None] & ((gy_ids >= 0) & (gy_ids < grid_y))[None, :]
    )

    for sweep_index in range(SWEEPS):
        m = sweep_index + 1
        nx, ny = wide_x - 2 * m, wide_y - 2 * m
        center_c = cond_wide[1:-1, m : m + nx, m : m + ny]
        faces = []
        diagonal = jnp.zeros_like(center_c)
        for d in range(3):
            if d == 0:
                lo = cond_wide[0:-2, m : m + nx, m : m + ny]
                hi = cond_wide[2:, m : m + nx, m : m + ny]
            elif d == 1:
                lo = cond_wide[1:-1, m - 1 : m - 1 + nx, m : m + ny]
                hi = cond_wide[1:-1, m + 1 : m + 1 + nx, m : m + ny]
            else:
                lo = cond_wide[1:-1, m : m + nx, m - 1 : m - 1 + ny]
                hi = cond_wide[1:-1, m : m + nx, m + 1 : m + 1 + ny]
            face_below = 0.5 * (center_c + lo)
            face_above = 0.5 * (center_c + hi)
            faces.append((face_below, face_above))
            diagonal = diagonal + face_below + face_above
        pot_z = jnp.pad(potential, ((0, 0), (1, 1), (0, 0), (0, 0)))
        pot_c = potential[:, :, 1:-1, 1:-1]
        coupled = jnp.zeros_like(pot_c)
        for d in range(3):
            if d == 0:
                lo = pot_z[:, 0:-2, 1:-1, 1:-1]
                hi = pot_z[:, 2:, 1:-1, 1:-1]
            elif d == 1:
                lo = potential[:, :, 0:-2, 1:-1]
                hi = potential[:, :, 2:, 1:-1]
            else:
                lo = potential[:, :, 1:-1, 0:-2]
                hi = potential[:, :, 1:-1, 2:]
            coupled = coupled + faces[d][0] * lo + faces[d][1] * hi
        applied = diagonal * pot_c - coupled
        rhs = source_terms[:, :, m : m + nx, m : m + ny]
        updated = pot_c + OMEGA * (rhs - applied) / diagonal
        potential = jnp.where(on_grid[m : m + nx, m : m + ny], updated, 0.0)

    return (advanced, conductivity, potential)


def solution(mesh):
    in_specs = (
        P("grp", None, "gx", "gy"),
        P(None, "grp", None, "gx", "gy"),
        P("grp", None, "gx", "gy"),
        P("grp", None, "gx", "gy"),
        P(),
        P(),
        P(None, None, "gx", "gy"),
    )
    out_specs = (P("grp", None, "gx", "gy"), P(None, "gx", "gy"), P("grp", None, "gx", "gy"))
    return jax.shard_map(
        on_device, mesh=mesh, in_specs=in_specs, out_specs=out_specs, check_vma=False
    )
```

```python
import functools

import jax
import jax.numpy as jnp
from jax.experimental import pallas as pl
from jax.experimental.pallas import tpu as pltpu
from jax import lax
from jax.sharding import PartitionSpec as P

SWEEPS = 3


KAPPA = 0.06
OMEGA = 0.8
AMPLITUDE = 40.0
ARCHIE = 20.0


def with_halo(shard, sides, width, top=None):
    for axis, dim in sides:
        devices, length = (lax.axis_size(axis), shard.shape[dim])
        last_member = devices if (axis != "grp" or top is None) else top
        up = [(i, i + 1) for i in range(last_member - 1)]
        down = [(j, i) for i, j in up]
        last = lax.slice_in_dim(shard, length - width, length, axis=dim)
        initial = lax.slice_in_dim(shard, 0, width, axis=dim)
        before = lax.ppermute(last, axis, up)
        after = lax.ppermute(initial, axis, down)
        shard = jnp.concatenate([before, shard, after], axis=dim)
    return shard


def faces_kernel(c_ref, v_ref, zs_up, zs_dn, xr, yc_ref, yu_ref):
    nzx, ny = c_ref.shape
    nz = xr.shape[1]
    nx = nzx // nz
    f32 = jnp.float32
    zs_up[0:2] = c_ref[nzx - 2 * nx : nzx].reshape(2, nx, ny)
    zs_dn[0:2] = c_ref[0 : 2 * nx].reshape(2, nx, ny)
    for d in range(3):
        zs_up[2 + d] = v_ref[d, nzx - nx : nzx].astype(f32)
        zs_dn[2 + d] = v_ref[d, 0:nx].astype(f32)
    for z in range(nz):
        base = z * nx
        xr[0, z : z + 1] = c_ref[base + nx - 2 : base + nx - 1]
        xr[1, z : z + 1] = c_ref[base + nx - 1 : base + nx]
        xr[5, z : z + 1] = c_ref[base : base + 1]
        xr[6, z : z + 1] = c_ref[base + 1 : base + 2]
        for d in range(3):
            top = v_ref[d, base + nx - 16 : base + nx].astype(f32)
            bottom = v_ref[d, base : base + 16].astype(f32)
            xr[2 + d, z : z + 1] = top[15:16]
            xr[7 + d, z : z + 1] = bottom[0:1]
    lane = lax.broadcasted_iota(jnp.int32, (8, ny), 1)
    row = lax.broadcasted_iota(jnp.int32, (8, ny), 0)
    pick_c = (
        ((row == 0) & (lane == ny - 2))
        | ((row == 1) & (lane == ny - 1))
        | ((row == 2) & (lane == 0))
        | ((row == 3) & (lane == 1))
    )
    pick_u = ((row == 0) & (lane == ny - 1)) | ((row == 1) & (lane == 0))
    nt = (((1,), (1,)), ((), ()))
    yc_ref[...] = lax.dot_general(
        pick_c.astype(f32), c_ref[...], nt, precision=lax.Precision.HIGHEST,
        preferred_element_type=f32,
    )
    for d in range(3):
        yu_ref[d] = lax.dot_general(
            pick_u.astype(jnp.bfloat16), v_ref[d], nt, preferred_element_type=f32
        )


def faces_call(c, velocity):
    nz, nx, ny = c.shape
    f32 = jnp.float32
    vmem = pl.BlockSpec(memory_space=pltpu.VMEM)
    return pl.pallas_call(
        faces_kernel,
        out_shape=(
            jax.ShapeDtypeStruct((5, nx, ny), f32),
            jax.ShapeDtypeStruct((5, nx, ny), f32),
            jax.ShapeDtypeStruct((10, nz, ny), f32),
            jax.ShapeDtypeStruct((8, nz * nx), f32),
            jax.ShapeDtypeStruct((3, 8, nz * nx), f32),
        ),
        in_specs=[vmem, vmem],
        out_specs=(vmem,) * 5,
        compiler_params=pltpu.CompilerParams(vmem_limit_bytes=32 * 1024 * 1024),
        cost_estimate=pl.CostEstimate(
            flops=2 * 32 * nz * nx * ny, transcendentals=0, bytes_accessed=10 * nz * nx * ny
        ),
    )(c.reshape(nz * nx, ny), velocity.reshape(3, nz * nx, ny))


def transport_halo(c, u, slabs):
    f32 = jnp.float32
    nz, nx, ny = c.shape
    zs_up, zs_dn, xr, ycols, ucols = faces_call(c, u)
    ycols = ycols.reshape(8, nz, nx)
    ucols = ucols.reshape(3, 8, nz, nx)

    def chain(axis, members):
        up = [(i, i + 1) for i in range(members - 1)]
        return up, [(j, i) for i, j in up]

    up, down = chain("grp", slabs)
    below = lax.ppermute(zs_up, "grp", up)
    above = lax.ppermute(zs_dn, "grp", down)
    zlo_c, zlo_u = below[:2], below[2:]
    zhi_c, zhi_u = above[:2], above[2:]

    def zext_c(rows, picked):
        return jnp.concatenate([zlo_c[:, rows], jnp.swapaxes(picked, 0, 1), zhi_c[:, rows]], 0)

    def zext_u(row, picked):
        core = jnp.concatenate([zlo_u[:, None, row], picked, zhi_u[:, None, row]], 1)
        return jnp.pad(core, ((0, 0), (1, 1), (0, 0)))

    rows = lax.axis_size("gx")
    up, down = chain("gx", rows)
    send_up = jnp.concatenate(
        [zext_c(slice(nx - 2, nx), xr[0:2]), jnp.swapaxes(zext_u(nx - 1, xr[2:5]), 0, 1)], 1
    )
    send_dn = jnp.concatenate(
        [zext_c(slice(0, 2), xr[5:7]), jnp.swapaxes(zext_u(0, xr[7:10]), 0, 1)], 1
    )
    bx = lax.ppermute(send_up, "gx", up)
    ax = lax.ppermute(send_dn, "gx", down)

    def xz_c(lanes, picked):
        core = jnp.concatenate([zlo_c[..., lanes], jnp.moveaxis(picked, 0, 2), zhi_c[..., lanes]], 0)
        return jnp.concatenate([bx[:, 0:2, lanes], core, ax[:, 0:2, lanes]], 1)

    def xz_u(lane, picked):
        core = jnp.pad(
            jnp.concatenate([zlo_u[:, None, :, lane], picked, zhi_u[:, None, :, lane]], 1),
            ((0, 0), (1, 1), (0, 0)),
        )
        lo = jnp.swapaxes(bx[:, 2:5, lane], 0, 1)[:, :, None]
        hi = jnp.swapaxes(ax[:, 2:5, lane], 0, 1)[:, :, None]
        zero = jnp.zeros_like(lo)
        return jnp.moveaxis(jnp.concatenate([zero, lo, core, hi, zero], 2), 0, 2)

    columns = lax.axis_size("gy")
    up, down = chain("gy", columns)
    by = lax.ppermute(
        jnp.concatenate([xz_c(slice(ny - 2, ny), ycols[0:2]), xz_u(ny - 1, ucols[:, 0])], 2), "gy", up
    )
    ay = lax.ppermute(
        jnp.concatenate([xz_c(slice(0, 2), ycols[2:4]), xz_u(0, ucols[:, 1])], 2), "gy", down
    )

    xc = jnp.concatenate([ax[:, 0:2], jnp.zeros((nz + 4, 4, ny), f32), bx[:, 0:2]], 1)
    xu_hi = jnp.swapaxes(ax[1:-1, 2:5], 0, 1)[:, :, None]
    xu_lo = jnp.swapaxes(bx[1:-1, 2:5], 0, 1)[:, :, None]
    xu = jnp.concatenate([xu_hi, jnp.zeros((3, nz + 2, 6, ny), f32), xu_lo], 2)
    speeds_y = jnp.stack([by[..., 2:5], ay[..., 2:5]], 3).reshape(nz + 4, nx + 4, 6)
    fill = jnp.zeros((nz + 4, nx + 4, 118), f32)
    yt = jnp.concatenate([ay[..., 0:2], speeds_y, fill, by[..., 0:2]], 2)
    yt = jnp.pad(yt, ((0, 0), (6, 6), (0, 0)))
    return below, above, xc, xu, yt


def roll(values, shift, axis):
    return pltpu.roll(values, shift % values.shape[axis], axis)


def stencil(c, below, above, speeds):
    running = -6.0 * KAPPA * c
    for d in range(3):
        b, a, s = below[d], above[d], speeds[d]
        running = running + KAPPA * (b + a) - (
            jnp.maximum(s, 0.0) * (c - b) + jnp.minimum(s, 0.0) * (a - c)
        )
    return running


def transport_kernel(
    grid, place, weights, c_ref, v_ref, poro_ref, sat_ref, z_below, z_above,
    xc, xu, yt, adv_ref, part_ref, F, U, S, SG, H,
):
    nz, nx, ny = c_ref.shape
    wx, wy = F.shape[1], F.shape[2]
    f32 = jnp.float32
    pool_y = (
        lax.broadcasted_iota(jnp.int32, (ny, ny // 2), 0) // 2
        == lax.broadcasted_iota(jnp.int32, (ny, ny // 2), 1)
    ).astype(f32)
    F[0:2, 8 : 8 + nx, 0:ny] = z_below[0:2]
    F[nz + 2 : nz + 4, 8 : 8 + nx, 0:ny] = z_above[0:2]

    def put_c(z, carry):
        F[z + 2, 8 : 8 + nx, 0:ny] = c_ref[z]
        return carry

    lax.fori_loop(0, nz, put_c, 0)
    F[:, 0:8, 0:ny] = xc[...]
    F[:, wx - 8 : wx, 0:ny] = xc[...]
    F[:, :, ny:wy] = yt[...]
    for d in range(3):
        U[d, 0, 8 : 8 + nx, 0:ny] = z_below[2 + d]
        U[d, nz + 1, 8 : 8 + nx, 0:ny] = z_above[2 + d]

        def put_u(z, carry, d=d):
            U[d, z + 1, 8 : 8 + nx, 0:ny] = v_ref[d, 0, z].astype(f32)
            return carry

        lax.fori_loop(0, nz, put_u, 0)
        U[d, :, 0:8, 0:ny] = xu[d]
        U[d, :, wx - 8 : wx, 0:ny] = xu[d]
        U[d, :, :, ny:wy] = roll(yt[1 : nz + 3], -(3 + 2 * d), 2)

    total_z, total_x, total_y = grid
    gz0 = place[0] * nz - 1
    gx = place[1] * nx - 8 + lax.broadcasted_iota(jnp.int32, (wx, wy), 0)
    lane = lax.broadcasted_iota(jnp.int32, (wx, wy), 1)
    gy = place[2] * ny + jnp.where(lane < ny + (wy - ny) // 2, lane, lane - wy)
    plane = (gx >= 0) & (gx < total_x) & (gy >= 0) & (gy < total_y)

    def first(k, carry):
        c0 = F[k + 1]
        below = (F[k], roll(c0, 1, 0), roll(c0, 1, 1))
        above = (F[k + 2], roll(c0, -1, 0), roll(c0, -1, 1))
        speeds = (U[0, k], U[1, k], U[2, k])
        section = c0 + stencil(c0, below, above, speeds)
        z = gz0 + k
        keep = plane & (z >= 0) & (z < total_z)
        S[k] = jnp.where(keep, section, 0.0)
        return carry

    lax.fori_loop(0, nz + 2, first, 0)

    live = place[3] > 0

    def core(values):
        return values[8 : 8 + nx, 0:ny]

    def second(j, carry):
        s_mid = S[j + 1]
        s0 = core(s_mid)
        below = (core(S[j]), core(roll(s_mid, 1, 0)), core(roll(s_mid, 1, 1)))
        above = (core(S[j + 2]), core(roll(s_mid, -1, 0)), core(roll(s_mid, -1, 1)))
        speeds = tuple(v_ref[d, 0, j].astype(f32) for d in range(3))
        c0 = c_ref[j]
        adv = 0.5 * (c0 + s0 + stencil(s0, below, above, speeds))
        adv = jnp.where(live, adv, 0.0)
        adv_ref[0, j] = adv
        p = poro_ref[0, j].astype(f32)
        w = sat_ref[0, j].astype(f32)
        SG[pl.ds(pl.multiple_of(j * nx, nx), nx)] = ARCHIE * jnp.exp(adv) * p * p * w * w
        return carry

    lax.fori_loop(0, nz, second, 0)
    H[...] = jnp.dot(SG[...], pool_y, precision=lax.Precision.HIGHEST, preferred_element_type=f32)
    half_rows = nz * nx // 2
    coarse = H[pl.ds(0, half_rows, stride=2)] + H[pl.ds(1, half_rows, stride=2)]
    cx = nx // 2
    resist_layers = part_ref.shape[0]
    for e in range(resist_layers):
        total = jnp.zeros((cx, ny // 2), f32)
        for z in range(nz):
            total = total + weights[e, z] * coarse[z * cx : (z + 1) * cx]
        part_ref[e] = total


def transport_call(place, weights, c, velocity, porosity, saturation, *pieces, grid):
    nz, nx, ny = c.shape
    wx, wy = nx + 16, ny + 128
    resist_layers = weights.shape[0]
    vmem = pl.BlockSpec(memory_space=pltpu.VMEM)
    smem = pl.BlockSpec(memory_space=pltpu.SMEM)
    cells = nz * nx * ny
    return pl.pallas_call(
        functools.partial(transport_kernel, grid),
        out_shape=(
            jax.ShapeDtypeStruct((1, nz, nx, ny), jnp.float32),
            jax.ShapeDtypeStruct((resist_layers, nx // 2, ny // 2), jnp.float32),
        ),
        in_specs=[smem, smem] + [vmem] * 9,
        out_specs=(vmem, vmem),
        scratch_shapes=[
            pltpu.VMEM((nz + 4, wx, wy), jnp.float32),
            pltpu.VMEM((3, nz + 2, wx, wy), jnp.float32),
            pltpu.VMEM((nz + 2, wx, wy), jnp.float32),
            pltpu.VMEM((nz * nx, ny), jnp.float32),
            pltpu.VMEM((nz * nx, ny // 2), jnp.float32),
        ],
        compiler_params=pltpu.CompilerParams(vmem_limit_bytes=60 * 1024 * 1024),
        cost_estimate=pl.CostEstimate(
            flops=200 * cells, transcendentals=cells, bytes_accessed=40 * cells
        ),
    )(place, weights, c, velocity, porosity, saturation, *pieces)


def neighbours(padded, direction_index):
    leading = [slice(None)] * (padded.ndim - 3)
    middle = [slice(1, -1)] * 3
    below_slices = list(middle)
    below_slices[direction_index] = slice(0, -2)
    above_slices = list(middle)
    above_slices[direction_index] = slice(2, None)
    return (padded[tuple(leading + below_slices)], padded[tuple(leading + above_slices)])


def tendency(padded, speeds):
    center = padded[1:-1, 1:-1, 1:-1]
    running = -6.0 * KAPPA * center
    for direction_index in range(3):
        below_cells, above_cells = neighbours(padded, direction_index)
        speed_comp = speeds[direction_index]
        running = (
            running
            + KAPPA * (below_cells + above_cells)
            - (
                jnp.maximum(speed_comp, 0.0) * (center - below_cells)
                + jnp.minimum(speed_comp, 0.0) * (above_cells - center)
            )
        )
    return running


def inside(start, count, total):
    ids = start + jnp.arange(count, dtype=jnp.int32)
    return (ids >= 0) & (ids < total)


def plane_halo(values, depth):
    rows, columns = lax.axis_size("gx"), lax.axis_size("gy")
    d = depth

    def line(n, step):
        return [(i, i + step) for i in range(n) if 0 <= i + step < n]

    def flat(i, j):
        return i * columns + j

    def diagonal(di, dj):
        return [
            (flat(i, j), flat(i + di, j + dj))
            for i in range(rows)
            for j in range(columns)
            if 0 <= i + di < rows and 0 <= j + dj < columns
        ]

    both = ("gx", "gy")
    lo_x = lax.ppermute(values[:, -d:, :], "gx", line(rows, 1))
    hi_x = lax.ppermute(values[:, :d, :], "gx", line(rows, -1))
    lo_y = lax.ppermute(values[:, :, -d:], "gy", line(columns, 1))
    hi_y = lax.ppermute(values[:, :, :d], "gy", line(columns, -1))
    lo_lo = lax.ppermute(values[:, -d:, -d:], both, diagonal(1, 1))
    lo_hi = lax.ppermute(values[:, -d:, :d], both, diagonal(1, -1))
    hi_lo = lax.ppermute(values[:, :d, -d:], both, diagonal(-1, 1))
    hi_hi = lax.ppermute(values[:, :d, :d], both, diagonal(-1, -1))
    top = jnp.concatenate([lo_lo, lo_x, lo_hi], 2)
    middle = jnp.concatenate([lo_y, values, hi_y], 2)
    bottom = jnp.concatenate([hi_lo, hi_x, hi_hi], 2)
    return jnp.concatenate([top, middle, bottom], 1)


def grp_sum(partial):
    pair = lax.ppermute(partial, "grp", [(0, 1), (1, 0), (2, 3), (3, 2)])
    partial = partial + pair
    pair = lax.ppermute(partial, "grp", [(0, 2), (2, 0), (1, 3), (3, 1)])
    return partial + pair


def on_device(conc, velocity, porosity, saturation, layer_counts, electrodes, init_potential):
    group_index = lax.axis_index("grp")
    row_index = lax.axis_index("gx")
    column_index = lax.axis_index("gy")
    groups = lax.axis_size("grp")
    rows = lax.axis_size("gx")
    columns = lax.axis_size("gy")
    active = group_index < 3
    field = conc[0]
    layers, tile_x, tile_y = field.shape
    slabs = 3
    speeds = velocity[:, 0]

    ends = jnp.cumsum(layer_counts)
    starts = ends - layer_counts
    layer_ids = group_index * layers + jnp.arange(layers, dtype=jnp.int32)
    member = (
        (layer_ids[None, :] >= starts[:, None]) & (layer_ids[None, :] < ends[:, None]) & active
    ).astype(jnp.float32)
    weights = member / (4.0 * layer_counts.astype(jnp.float32))[:, None]
    resist_layers = layer_counts.shape[0]
    coarse_x = tile_x // 2
    coarse_y = tile_y // 2

    pieces = transport_halo(field, velocity, slabs)
    place = jnp.stack([group_index, row_index, column_index, active.astype(jnp.int32)])
    advanced, partial_cond = transport_call(
        place, weights, field, velocity, porosity, saturation, *pieces,
        grid=(slabs * layers, rows * tile_x, columns * tile_y),
    )
    conductivity = grp_sum(partial_cond)

    grid_x = coarse_x * rows
    grid_y = coarse_y * columns
    depth = SWEEPS
    potential = lax.dynamic_slice_in_dim(init_potential, group_index, 1, 0)
    poles = lax.dynamic_slice_in_dim(electrodes, group_index, 1, 0)

    both = with_halo(jnp.concatenate([conductivity, potential[0]], axis=0), (("gx", 1), ("gy", 2)), depth)
    cond_wide = jnp.pad(both[:resist_layers], ((1, 1), (0, 0), (0, 0)))
    potential = both[None, resist_layers:]
    wide_x = coarse_x + 2 * depth
    wide_y = coarse_y + 2 * depth
    gx_ids = row_index * coarse_x - depth + jnp.arange(wide_x, dtype=jnp.int32)
    gy_ids = column_index * coarse_y - depth + jnp.arange(wide_y, dtype=jnp.int32)
    flat_ids = (
        jnp.arange(resist_layers, dtype=jnp.int32)[:, None, None] * (grid_x * grid_y)
        + gx_ids[None, :, None] * grid_y
        + gy_ids[None, None, :]
    )
    source_terms = AMPLITUDE * (
        (flat_ids[None] == poles[:, 0, None, None, None]).astype(jnp.float32)
        - (flat_ids[None] == poles[:, 1, None, None, None]).astype(jnp.float32)
    )
    on_grid = (
        ((gx_ids >= 0) & (gx_ids < grid_x))[:, None] & ((gy_ids >= 0) & (gy_ids < grid_y))[None, :]
    )

    for sweep_index in range(SWEEPS):
        m = sweep_index + 1
        nx, ny = wide_x - 2 * m, wide_y - 2 * m
        center_c = cond_wide[1:-1, m : m + nx, m : m + ny]
        faces = []
        diagonal = jnp.zeros_like(center_c)
        for d in range(3):
            if d == 0:
                lo = cond_wide[0:-2, m : m + nx, m : m + ny]
                hi = cond_wide[2:, m : m + nx, m : m + ny]
            elif d == 1:
                lo = cond_wide[1:-1, m - 1 : m - 1 + nx, m : m + ny]
                hi = cond_wide[1:-1, m + 1 : m + 1 + nx, m : m + ny]
            else:
                lo = cond_wide[1:-1, m : m + nx, m - 1 : m - 1 + ny]
                hi = cond_wide[1:-1, m : m + nx, m + 1 : m + 1 + ny]
            face_below = 0.5 * (center_c + lo)
            face_above = 0.5 * (center_c + hi)
            faces.append((face_below, face_above))
            diagonal = diagonal + face_below + face_above
        pot_z = jnp.pad(potential, ((0, 0), (1, 1), (0, 0), (0, 0)))
        pot_c = potential[:, :, 1:-1, 1:-1]
        coupled = jnp.zeros_like(pot_c)
        for d in range(3):
            if d == 0:
                lo = pot_z[:, 0:-2, 1:-1, 1:-1]
                hi = pot_z[:, 2:, 1:-1, 1:-1]
            elif d == 1:
                lo = potential[:, :, 0:-2, 1:-1]
                hi = potential[:, :, 2:, 1:-1]
            else:
                lo = potential[:, :, 1:-1, 0:-2]
                hi = potential[:, :, 1:-1, 2:]
            coupled = coupled + faces[d][0] * lo + faces[d][1] * hi
        applied = diagonal * pot_c - coupled
        rhs = source_terms[:, :, m : m + nx, m : m + ny]
        updated = pot_c + OMEGA * (rhs - applied) / diagonal
        potential = jnp.where(on_grid[m : m + nx, m : m + ny], updated, 0.0)

    return (advanced, conductivity, potential)


def solution(mesh):
    in_specs = (
        P("grp", None, "gx", "gy"),
        P(None, "grp", None, "gx", "gy"),
        P("grp", None, "gx", "gy"),
        P("grp", None, "gx", "gy"),
        P(),
        P(),
        P(None, None, "gx", "gy"),
    )
    out_specs = (P("grp", None, "gx", "gy"), P(None, "gx", "gy"), P("grp", None, "gx", "gy"))
    return jax.shard_map(
        on_device, mesh=mesh, in_specs=in_specs, out_specs=out_specs, check_vma=False
    )
```

```python
import functools

import jax
import jax.numpy as jnp
from jax.experimental import pallas as pl
from jax.experimental.pallas import tpu as pltpu
from jax import lax
from jax.sharding import PartitionSpec as P

SWEEPS = 3


KAPPA = 0.06
OMEGA = 0.8
AMPLITUDE = 40.0
ARCHIE = 20.0


def with_halo(shard, sides, width, top=None):
    for axis, dim in sides:
        devices, length = (lax.axis_size(axis), shard.shape[dim])
        last_member = devices if (axis != "grp" or top is None) else top
        up = [(i, i + 1) for i in range(last_member - 1)]
        down = [(j, i) for i, j in up]
        last = lax.slice_in_dim(shard, length - width, length, axis=dim)
        initial = lax.slice_in_dim(shard, 0, width, axis=dim)
        before = lax.ppermute(last, axis, up)
        after = lax.ppermute(initial, axis, down)
        shard = jnp.concatenate([before, shard, after], axis=dim)
    return shard


def faces_kernel(c_ref, v_ref, zs_up, zs_dn, xr, yc_ref, yu_ref):
    nzx, ny = c_ref.shape
    nz = xr.shape[1]
    nx = nzx // nz
    f32 = jnp.float32
    zs_up[0:2] = c_ref[nzx - 2 * nx : nzx].reshape(2, nx, ny)
    zs_dn[0:2] = c_ref[0 : 2 * nx].reshape(2, nx, ny)
    for d in range(3):
        zs_up[2 + d] = v_ref[d, nzx - nx : nzx].astype(f32)
        zs_dn[2 + d] = v_ref[d, 0:nx].astype(f32)
    for z in range(nz):
        base = z * nx
        xr[0, z : z + 1] = c_ref[base + nx - 2 : base + nx - 1]
        xr[1, z : z + 1] = c_ref[base + nx - 1 : base + nx]
        xr[5, z : z + 1] = c_ref[base : base + 1]
        xr[6, z : z + 1] = c_ref[base + 1 : base + 2]
        for d in range(3):
            top = v_ref[d, base + nx - 16 : base + nx].astype(f32)
            bottom = v_ref[d, base : base + 16].astype(f32)
            xr[2 + d, z : z + 1] = top[15:16]
            xr[7 + d, z : z + 1] = bottom[0:1]
    lane = lax.broadcasted_iota(jnp.int32, (8, ny), 1)
    row = lax.broadcasted_iota(jnp.int32, (8, ny), 0)
    pick_c = (
        ((row == 0) & (lane == ny - 2))
        | ((row == 1) & (lane == ny - 1))
        | ((row == 2) & (lane == 0))
        | ((row == 3) & (lane == 1))
    )
    pick_u = ((row == 0) & (lane == ny - 1)) | ((row == 1) & (lane == 0))
    nt = (((1,), (1,)), ((), ()))
    yc_ref[...] = lax.dot_general(
        pick_c.astype(f32), c_ref[...], nt, precision=lax.Precision.HIGHEST,
        preferred_element_type=f32,
    )
    for d in range(3):
        yu_ref[d] = lax.dot_general(
            pick_u.astype(jnp.bfloat16), v_ref[d], nt, preferred_element_type=f32
        )


def faces_call(c, velocity):
    nz, nx, ny = c.shape
    f32 = jnp.float32
    vmem = pl.BlockSpec(memory_space=pltpu.VMEM)
    return pl.pallas_call(
        faces_kernel,
        out_shape=(
            jax.ShapeDtypeStruct((5, nx, ny), f32),
            jax.ShapeDtypeStruct((5, nx, ny), f32),
            jax.ShapeDtypeStruct((10, nz, ny), f32),
            jax.ShapeDtypeStruct((8, nz * nx), f32),
            jax.ShapeDtypeStruct((3, 8, nz * nx), f32),
        ),
        in_specs=[vmem, vmem],
        out_specs=(vmem,) * 5,
        compiler_params=pltpu.CompilerParams(vmem_limit_bytes=32 * 1024 * 1024),
        cost_estimate=pl.CostEstimate(
            flops=2 * 32 * nz * nx * ny, transcendentals=0, bytes_accessed=10 * nz * nx * ny
        ),
    )(c.reshape(nz * nx, ny), velocity.reshape(3, nz * nx, ny))


def transport_halo(c, u, slabs):
    f32 = jnp.float32
    nz, nx, ny = c.shape
    zs_up, zs_dn, xr, ycols, ucols = faces_call(c, u)
    ycols = ycols.reshape(8, nz, nx)
    ucols = ucols.reshape(3, 8, nz, nx)

    def chain(axis, members):
        up = [(i, i + 1) for i in range(members - 1)]
        return up, [(j, i) for i, j in up]

    up, down = chain("grp", slabs)
    below = lax.ppermute(zs_up, "grp", up)
    above = lax.ppermute(zs_dn, "grp", down)
    zlo_c, zlo_u = below[:2], below[2:]
    zhi_c, zhi_u = above[:2], above[2:]

    def zext_c(rows, picked):
        return jnp.concatenate([zlo_c[:, rows], jnp.swapaxes(picked, 0, 1), zhi_c[:, rows]], 0)

    def zext_u(row, picked):
        core = jnp.concatenate([zlo_u[:, None, row], picked, zhi_u[:, None, row]], 1)
        return jnp.pad(core, ((0, 0), (1, 1), (0, 0)))

    rows = lax.axis_size("gx")
    up, down = chain("gx", rows)
    send_up = jnp.concatenate(
        [zext_c(slice(nx - 2, nx), xr[0:2]), jnp.swapaxes(zext_u(nx - 1, xr[2:5]), 0, 1)], 1
    )
    send_dn = jnp.concatenate(
        [zext_c(slice(0, 2), xr[5:7]), jnp.swapaxes(zext_u(0, xr[7:10]), 0, 1)], 1
    )
    bx = lax.ppermute(send_up, "gx", up)
    ax = lax.ppermute(send_dn, "gx", down)

    def xz_c(lanes, picked):
        core = jnp.concatenate([zlo_c[..., lanes], jnp.moveaxis(picked, 0, 2), zhi_c[..., lanes]], 0)
        return jnp.concatenate([bx[:, 0:2, lanes], core, ax[:, 0:2, lanes]], 1)

    def xz_u(lane, picked):
        core = jnp.pad(
            jnp.concatenate([zlo_u[:, None, :, lane], picked, zhi_u[:, None, :, lane]], 1),
            ((0, 0), (1, 1), (0, 0)),
        )
        lo = jnp.swapaxes(bx[:, 2:5, lane], 0, 1)[:, :, None]
        hi = jnp.swapaxes(ax[:, 2:5, lane], 0, 1)[:, :, None]
        zero = jnp.zeros_like(lo)
        return jnp.moveaxis(jnp.concatenate([zero, lo, core, hi, zero], 2), 0, 2)

    columns = lax.axis_size("gy")
    up, down = chain("gy", columns)
    by = lax.ppermute(
        jnp.concatenate([xz_c(slice(ny - 2, ny), ycols[0:2]), xz_u(ny - 1, ucols[:, 0])], 2), "gy", up
    )
    ay = lax.ppermute(
        jnp.concatenate([xz_c(slice(0, 2), ycols[2:4]), xz_u(0, ucols[:, 1])], 2), "gy", down
    )

    xc = jnp.concatenate([ax[:, 0:2], jnp.zeros((nz + 4, 4, ny), f32), bx[:, 0:2]], 1)
    xu_hi = jnp.swapaxes(ax[1:-1, 2:5], 0, 1)[:, :, None]
    xu_lo = jnp.swapaxes(bx[1:-1, 2:5], 0, 1)[:, :, None]
    xu = jnp.concatenate([xu_hi, jnp.zeros((3, nz + 2, 6, ny), f32), xu_lo], 2)
    speeds_y = jnp.stack([by[..., 2:5], ay[..., 2:5]], 3).reshape(nz + 4, nx + 4, 6)
    fill = jnp.zeros((nz + 4, nx + 4, 118), f32)
    yt = jnp.concatenate([ay[..., 0:2], speeds_y, fill, by[..., 0:2]], 2)
    yt = jnp.pad(yt, ((0, 0), (6, 6), (0, 0)))
    return zlo_c, zhi_c, zlo_u, zhi_u, xc, xu, yt


def roll(values, shift, axis):
    return pltpu.roll(values, shift % values.shape[axis], axis)


def stencil(c, below, above, speeds):
    running = -6.0 * KAPPA * c
    for d in range(3):
        b, a, s = below[d], above[d], speeds[d]
        running = running + KAPPA * (b + a) - (
            jnp.maximum(s, 0.0) * (c - b) + jnp.minimum(s, 0.0) * (a - c)
        )
    return running


def transport_kernel(
    grid, place, weights, c_ref, v_ref, poro_ref, sat_ref, zlo_c, zhi_c, zlo_u, zhi_u,
    xc, xu, yt, adv_ref, part_ref, F, U, S, SG, H,
):
    nz, nx, ny = c_ref.shape
    wx, wy = F.shape[1], F.shape[2]
    f32 = jnp.float32
    pool_y = (
        lax.broadcasted_iota(jnp.int32, (ny, ny // 2), 0) // 2
        == lax.broadcasted_iota(jnp.int32, (ny, ny // 2), 1)
    ).astype(f32)
    F[0:2, 8 : 8 + nx, 0:ny] = zlo_c[...]
    F[nz + 2 : nz + 4, 8 : 8 + nx, 0:ny] = zhi_c[...]

    def put_c(z, carry):
        F[z + 2, 8 : 8 + nx, 0:ny] = c_ref[z]
        return carry

    lax.fori_loop(0, nz, put_c, 0)
    F[:, 0:8, 0:ny] = xc[...]
    F[:, wx - 8 : wx, 0:ny] = xc[...]
    F[:, :, ny:wy] = yt[...]
    for d in range(3):
        U[d, 0, 8 : 8 + nx, 0:ny] = zlo_u[d]
        U[d, nz + 1, 8 : 8 + nx, 0:ny] = zhi_u[d]

        def put_u(z, carry, d=d):
            U[d, z + 1, 8 : 8 + nx, 0:ny] = v_ref[d, 0, z].astype(f32)
            return carry

        lax.fori_loop(0, nz, put_u, 0)
        U[d, :, 0:8, 0:ny] = xu[d]
        U[d, :, wx - 8 : wx, 0:ny] = xu[d]
        U[d, :, :, ny:wy] = roll(yt[1 : nz + 3], -(3 + 2 * d), 2)

    total_z, total_x, total_y = grid
    gz0 = place[0] * nz - 1
    gx = place[1] * nx - 8 + lax.broadcasted_iota(jnp.int32, (wx, wy), 0)
    lane = lax.broadcasted_iota(jnp.int32, (wx, wy), 1)
    gy = place[2] * ny + jnp.where(lane < ny + (wy - ny) // 2, lane, lane - wy)
    plane = (gx >= 0) & (gx < total_x) & (gy >= 0) & (gy < total_y)

    def first(k, carry):
        c0 = F[k + 1]
        below = (F[k], roll(c0, 1, 0), roll(c0, 1, 1))
        above = (F[k + 2], roll(c0, -1, 0), roll(c0, -1, 1))
        speeds = (U[0, k], U[1, k], U[2, k])
        section = c0 + stencil(c0, below, above, speeds)
        z = gz0 + k
        keep = plane & (z >= 0) & (z < total_z)
        S[k] = jnp.where(keep, section, 0.0)
        return carry

    lax.fori_loop(0, nz + 2, first, 0)

    live = place[3] > 0

    def core(values):
        return values[8 : 8 + nx, 0:ny]

    def second(j, carry):
        s_mid = S[j + 1]
        s0 = core(s_mid)
        below = (core(S[j]), core(roll(s_mid, 1, 0)), core(roll(s_mid, 1, 1)))
        above = (core(S[j + 2]), core(roll(s_mid, -1, 0)), core(roll(s_mid, -1, 1)))
        speeds = tuple(v_ref[d, 0, j].astype(f32) for d in range(3))
        c0 = c_ref[j]
        adv = 0.5 * (c0 + s0 + stencil(s0, below, above, speeds))
        adv = jnp.where(live, adv, 0.0)
        adv_ref[0, j] = adv
        p = poro_ref[0, j].astype(f32)
        w = sat_ref[0, j].astype(f32)
        SG[pl.ds(pl.multiple_of(j * nx, nx), nx)] = ARCHIE * jnp.exp(adv) * p * p * w * w
        return carry

    lax.fori_loop(0, nz, second, 0)
    H[...] = jnp.dot(SG[...], pool_y, precision=lax.Precision.HIGHEST, preferred_element_type=f32)
    half_rows = nz * nx // 2
    coarse = H[pl.ds(0, half_rows, stride=2)] + H[pl.ds(1, half_rows, stride=2)]
    cx = nx // 2
    resist_layers = part_ref.shape[0]
    for e in range(resist_layers):
        total = jnp.zeros((cx, ny // 2), f32)
        for z in range(nz):
            total = total + weights[e, z] * coarse[z * cx : (z + 1) * cx]
        part_ref[e] = total


def transport_call(place, weights, c, velocity, porosity, saturation, *pieces, grid):
    nz, nx, ny = c.shape
    wx, wy = nx + 16, ny + 128
    resist_layers = weights.shape[0]
    vmem = pl.BlockSpec(memory_space=pltpu.VMEM)
    smem = pl.BlockSpec(memory_space=pltpu.SMEM)
    cells = nz * nx * ny
    return pl.pallas_call(
        functools.partial(transport_kernel, grid),
        out_shape=(
            jax.ShapeDtypeStruct((1, nz, nx, ny), jnp.float32),
            jax.ShapeDtypeStruct((resist_layers, nx // 2, ny // 2), jnp.float32),
        ),
        in_specs=[smem, smem] + [vmem] * 11,
        out_specs=(vmem, vmem),
        scratch_shapes=[
            pltpu.VMEM((nz + 4, wx, wy), jnp.float32),
            pltpu.VMEM((3, nz + 2, wx, wy), jnp.float32),
            pltpu.VMEM((nz + 2, wx, wy), jnp.float32),
            pltpu.VMEM((nz * nx, ny), jnp.float32),
            pltpu.VMEM((nz * nx, ny // 2), jnp.float32),
        ],
        compiler_params=pltpu.CompilerParams(vmem_limit_bytes=60 * 1024 * 1024),
        cost_estimate=pl.CostEstimate(
            flops=200 * cells, transcendentals=cells, bytes_accessed=40 * cells
        ),
    )(place, weights, c, velocity, porosity, saturation, *pieces)


def neighbours(padded, direction_index):
    leading = [slice(None)] * (padded.ndim - 3)
    middle = [slice(1, -1)] * 3
    below_slices = list(middle)
    below_slices[direction_index] = slice(0, -2)
    above_slices = list(middle)
    above_slices[direction_index] = slice(2, None)
    return (padded[tuple(leading + below_slices)], padded[tuple(leading + above_slices)])


def tendency(padded, speeds):
    center = padded[1:-1, 1:-1, 1:-1]
    running = -6.0 * KAPPA * center
    for direction_index in range(3):
        below_cells, above_cells = neighbours(padded, direction_index)
        speed_comp = speeds[direction_index]
        running = (
            running
            + KAPPA * (below_cells + above_cells)
            - (
                jnp.maximum(speed_comp, 0.0) * (center - below_cells)
                + jnp.minimum(speed_comp, 0.0) * (above_cells - center)
            )
        )
    return running


def inside(start, count, total):
    ids = start + jnp.arange(count, dtype=jnp.int32)
    return (ids >= 0) & (ids < total)


def plane_halo(values, depth):
    rows, columns = lax.axis_size("gx"), lax.axis_size("gy")
    d = depth

    def line(n, step):
        return [(i, i + step) for i in range(n) if 0 <= i + step < n]

    def flat(i, j):
        return i * columns + j

    def diagonal(di, dj):
        return [
            (flat(i, j), flat(i + di, j + dj))
            for i in range(rows)
            for j in range(columns)
            if 0 <= i + di < rows and 0 <= j + dj < columns
        ]

    both = ("gx", "gy")
    lo_x = lax.ppermute(values[:, -d:, :], "gx", line(rows, 1))
    hi_x = lax.ppermute(values[:, :d, :], "gx", line(rows, -1))
    lo_y = lax.ppermute(values[:, :, -d:], "gy", line(columns, 1))
    hi_y = lax.ppermute(values[:, :, :d], "gy", line(columns, -1))
    lo_lo = lax.ppermute(values[:, -d:, -d:], both, diagonal(1, 1))
    lo_hi = lax.ppermute(values[:, -d:, :d], both, diagonal(1, -1))
    hi_lo = lax.ppermute(values[:, :d, -d:], both, diagonal(-1, 1))
    hi_hi = lax.ppermute(values[:, :d, :d], both, diagonal(-1, -1))
    top = jnp.concatenate([lo_lo, lo_x, lo_hi], 2)
    middle = jnp.concatenate([lo_y, values, hi_y], 2)
    bottom = jnp.concatenate([hi_lo, hi_x, hi_hi], 2)
    return jnp.concatenate([top, middle, bottom], 1)


def grp_sum(partial, slabs):
    groups = lax.axis_size("grp")
    me = lax.axis_index("grp")
    received = {}
    for shift in range(1, groups):
        pairs = [(g, (g + shift) % groups) for g in range(slabs)]
        received[shift] = lax.ppermute(partial, "grp", pairs)
    total = None
    for owner in range(slabs):
        share = partial
        for shift in range(1, groups):
            share = jnp.where((me - shift) % groups == owner, received[shift], share)
        total = share if total is None else total + share
    return total


def on_device(conc, velocity, porosity, saturation, layer_counts, electrodes, init_potential):
    group_index = lax.axis_index("grp")
    row_index = lax.axis_index("gx")
    column_index = lax.axis_index("gy")
    groups = lax.axis_size("grp")
    rows = lax.axis_size("gx")
    columns = lax.axis_size("gy")
    active = group_index < 3
    field = conc[0]
    layers, tile_x, tile_y = field.shape
    slabs = 3
    speeds = velocity[:, 0]

    ends = jnp.cumsum(layer_counts)
    starts = ends - layer_counts
    layer_ids = group_index * layers + jnp.arange(layers, dtype=jnp.int32)
    member = (
        (layer_ids[None, :] >= starts[:, None]) & (layer_ids[None, :] < ends[:, None]) & active
    ).astype(jnp.float32)
    weights = member / (4.0 * layer_counts.astype(jnp.float32))[:, None]
    resist_layers = layer_counts.shape[0]
    coarse_x = tile_x // 2
    coarse_y = tile_y // 2

    pieces = transport_halo(field, velocity, slabs)
    place = jnp.stack([group_index, row_index, column_index, active.astype(jnp.int32)])
    advanced, partial_cond = transport_call(
        place, weights, field, velocity, porosity, saturation, *pieces,
        grid=(slabs * layers, rows * tile_x, columns * tile_y),
    )
    conductivity = grp_sum(partial_cond, slabs)

    grid_x = coarse_x * rows
    grid_y = coarse_y * columns
    depth = SWEEPS
    potential = lax.dynamic_slice_in_dim(init_potential, group_index, 1, 0)
    poles = lax.dynamic_slice_in_dim(electrodes, group_index, 1, 0)

    both = with_halo(jnp.concatenate([conductivity, potential[0]], axis=0), (("gx", 1), ("gy", 2)), depth)
    cond_wide = jnp.pad(both[:resist_layers], ((1, 1), (0, 0), (0, 0)))
    potential = both[None, resist_layers:]
    wide_x = coarse_x + 2 * depth
    wide_y = coarse_y + 2 * depth
    gx_ids = row_index * coarse_x - depth + jnp.arange(wide_x, dtype=jnp.int32)
    gy_ids = column_index * coarse_y - depth + jnp.arange(wide_y, dtype=jnp.int32)
    flat_ids = (
        jnp.arange(resist_layers, dtype=jnp.int32)[:, None, None] * (grid_x * grid_y)
        + gx_ids[None, :, None] * grid_y
        + gy_ids[None, None, :]
    )
    source_terms = AMPLITUDE * (
        (flat_ids[None] == poles[:, 0, None, None, None]).astype(jnp.float32)
        - (flat_ids[None] == poles[:, 1, None, None, None]).astype(jnp.float32)
    )
    on_grid = (
        ((gx_ids >= 0) & (gx_ids < grid_x))[:, None] & ((gy_ids >= 0) & (gy_ids < grid_y))[None, :]
    )

    for sweep_index in range(SWEEPS):
        m = sweep_index + 1
        nx, ny = wide_x - 2 * m, wide_y - 2 * m
        center_c = cond_wide[1:-1, m : m + nx, m : m + ny]
        faces = []
        diagonal = jnp.zeros_like(center_c)
        for d in range(3):
            if d == 0:
                lo = cond_wide[0:-2, m : m + nx, m : m + ny]
                hi = cond_wide[2:, m : m + nx, m : m + ny]
            elif d == 1:
                lo = cond_wide[1:-1, m - 1 : m - 1 + nx, m : m + ny]
                hi = cond_wide[1:-1, m + 1 : m + 1 + nx, m : m + ny]
            else:
                lo = cond_wide[1:-1, m : m + nx, m - 1 : m - 1 + ny]
                hi = cond_wide[1:-1, m : m + nx, m + 1 : m + 1 + ny]
            face_below = 0.5 * (center_c + lo)
            face_above = 0.5 * (center_c + hi)
            faces.append((face_below, face_above))
            diagonal = diagonal + face_below + face_above
        pot_z = jnp.pad(potential, ((0, 0), (1, 1), (0, 0), (0, 0)))
        pot_c = potential[:, :, 1:-1, 1:-1]
        coupled = jnp.zeros_like(pot_c)
        for d in range(3):
            if d == 0:
                lo = pot_z[:, 0:-2, 1:-1, 1:-1]
                hi = pot_z[:, 2:, 1:-1, 1:-1]
            elif d == 1:
                lo = potential[:, :, 0:-2, 1:-1]
                hi = potential[:, :, 2:, 1:-1]
            else:
                lo = potential[:, :, 1:-1, 0:-2]
                hi = potential[:, :, 1:-1, 2:]
            coupled = coupled + faces[d][0] * lo + faces[d][1] * hi
        applied = diagonal * pot_c - coupled
        rhs = source_terms[:, :, m : m + nx, m : m + ny]
        updated = pot_c + OMEGA * (rhs - applied) / diagonal
        potential = jnp.where(on_grid[m : m + nx, m : m + ny], updated, 0.0)

    return (advanced, conductivity, potential)


def solution(mesh):
    in_specs = (
        P("grp", None, "gx", "gy"),
        P(None, "grp", None, "gx", "gy"),
        P("grp", None, "gx", "gy"),
        P("grp", None, "gx", "gy"),
        P(),
        P(),
        P(None, None, "gx", "gy"),
    )
    out_specs = (P("grp", None, "gx", "gy"), P(None, "gx", "gy"), P("grp", None, "gx", "gy"))
    return jax.shard_map(
        on_device, mesh=mesh, in_specs=in_specs, out_specs=out_specs, check_vma=False
    )
```

```python
import functools

import jax
import jax.numpy as jnp
from jax.experimental import pallas as pl
from jax.experimental.pallas import tpu as pltpu
from jax import lax
from jax.sharding import PartitionSpec as P

SWEEPS = 3


KAPPA = 0.06
OMEGA = 0.8
AMPLITUDE = 40.0
ARCHIE = 20.0


def with_halo(shard, sides, width, top=None):
    for axis, dim in sides:
        devices, length = (lax.axis_size(axis), shard.shape[dim])
        last_member = devices if (axis != "grp" or top is None) else top
        up = [(i, i + 1) for i in range(last_member - 1)]
        down = [(j, i) for i, j in up]
        last = lax.slice_in_dim(shard, length - width, length, axis=dim)
        initial = lax.slice_in_dim(shard, 0, width, axis=dim)
        before = lax.ppermute(last, axis, up)
        after = lax.ppermute(initial, axis, down)
        shard = jnp.concatenate([before, shard, after], axis=dim)
    return shard


def faces_kernel(c_ref, v_ref, zs_up, zs_dn, xr, yc_ref, yu_ref):
    nzx, ny = c_ref.shape
    nz = xr.shape[1]
    nx = nzx // nz
    f32 = jnp.float32
    zs_up[0:2] = c_ref[nzx - 2 * nx : nzx].reshape(2, nx, ny)
    zs_dn[0:2] = c_ref[0 : 2 * nx].reshape(2, nx, ny)
    for d in range(3):
        zs_up[2 + d] = v_ref[d, nzx - nx : nzx].astype(f32)
        zs_dn[2 + d] = v_ref[d, 0:nx].astype(f32)
    for z in range(nz):
        base = z * nx
        xr[0, z : z + 1] = c_ref[base + nx - 2 : base + nx - 1]
        xr[1, z : z + 1] = c_ref[base + nx - 1 : base + nx]
        xr[5, z : z + 1] = c_ref[base : base + 1]
        xr[6, z : z + 1] = c_ref[base + 1 : base + 2]
        for d in range(3):
            top = v_ref[d, base + nx - 16 : base + nx].astype(f32)
            bottom = v_ref[d, base : base + 16].astype(f32)
            xr[2 + d, z : z + 1] = top[15:16]
            xr[7 + d, z : z + 1] = bottom[0:1]
    lane = lax.broadcasted_iota(jnp.int32, (8, ny), 1)
    row = lax.broadcasted_iota(jnp.int32, (8, ny), 0)
    pick_c = (
        ((row == 0) & (lane == ny - 2))
        | ((row == 1) & (lane == ny - 1))
        | ((row == 2) & (lane == 0))
        | ((row == 3) & (lane == 1))
    )
    pick_u = ((row == 0) & (lane == ny - 1)) | ((row == 1) & (lane == 0))
    nt = (((1,), (1,)), ((), ()))
    yc_ref[...] = lax.dot_general(
        pick_c.astype(f32), c_ref[...], nt, precision=lax.Precision.HIGHEST,
        preferred_element_type=f32,
    )
    for d in range(3):
        yu_ref[d] = lax.dot_general(
            pick_u.astype(jnp.bfloat16), v_ref[d], nt, preferred_element_type=f32
        )


def faces_call(c, velocity):
    nz, nx, ny = c.shape
    f32 = jnp.float32
    vmem = pl.BlockSpec(memory_space=pltpu.VMEM)
    return pl.pallas_call(
        faces_kernel,
        out_shape=(
            jax.ShapeDtypeStruct((5, nx, ny), f32),
            jax.ShapeDtypeStruct((5, nx, ny), f32),
            jax.ShapeDtypeStruct((10, nz, ny), f32),
            jax.ShapeDtypeStruct((8, nz * nx), f32),
            jax.ShapeDtypeStruct((3, 8, nz * nx), f32),
        ),
        in_specs=[vmem, vmem],
        out_specs=(vmem,) * 5,
        compiler_params=pltpu.CompilerParams(vmem_limit_bytes=32 * 1024 * 1024),
        cost_estimate=pl.CostEstimate(
            flops=2 * 32 * nz * nx * ny, transcendentals=0, bytes_accessed=10 * nz * nx * ny
        ),
    )(c.reshape(nz * nx, ny), velocity.reshape(3, nz * nx, ny))


def transport_halo(c, u, slabs):
    f32 = jnp.float32
    nz, nx, ny = c.shape
    zs_up, zs_dn, xr, ycols, ucols = faces_call(c, u)
    ycols = ycols.reshape(8, nz, nx)
    ucols = ucols.reshape(3, 8, nz, nx)

    def chain(axis, members):
        up = [(i, i + 1) for i in range(members - 1)]
        return up, [(j, i) for i, j in up]

    up, down = chain("grp", slabs)
    below = lax.ppermute(zs_up, "grp", up)
    above = lax.ppermute(zs_dn, "grp", down)
    zlo_c, zlo_u = below[:2], below[2:]
    zhi_c, zhi_u = above[:2], above[2:]

    def zext_c(rows, picked):
        return jnp.concatenate([zlo_c[:, rows], jnp.swapaxes(picked, 0, 1), zhi_c[:, rows]], 0)

    def zext_u(row, picked):
        core = jnp.concatenate([zlo_u[:, None, row], picked, zhi_u[:, None, row]], 1)
        return jnp.pad(core, ((0, 0), (1, 1), (0, 0)))

    rows = lax.axis_size("gx")
    up, down = chain("gx", rows)
    send_up = jnp.concatenate(
        [zext_c(slice(nx - 2, nx), xr[0:2]), jnp.swapaxes(zext_u(nx - 1, xr[2:5]), 0, 1)], 1
    )
    send_dn = jnp.concatenate(
        [zext_c(slice(0, 2), xr[5:7]), jnp.swapaxes(zext_u(0, xr[7:10]), 0, 1)], 1
    )
    bx = lax.ppermute(send_up, "gx", up)
    ax = lax.ppermute(send_dn, "gx", down)

    def xz_c(lanes, picked):
        core = jnp.concatenate([zlo_c[..., lanes], jnp.moveaxis(picked, 0, 2), zhi_c[..., lanes]], 0)
        return jnp.concatenate([bx[:, 0:2, lanes], core, ax[:, 0:2, lanes]], 1)

    def xz_u(lane, picked):
        core = jnp.pad(
            jnp.concatenate([zlo_u[:, None, :, lane], picked, zhi_u[:, None, :, lane]], 1),
            ((0, 0), (1, 1), (0, 0)),
        )
        lo = jnp.swapaxes(bx[:, 2:5, lane], 0, 1)[:, :, None]
        hi = jnp.swapaxes(ax[:, 2:5, lane], 0, 1)[:, :, None]
        zero = jnp.zeros_like(lo)
        return jnp.moveaxis(jnp.concatenate([zero, lo, core, hi, zero], 2), 0, 2)

    columns = lax.axis_size("gy")
    up, down = chain("gy", columns)
    by = lax.ppermute(
        jnp.concatenate([xz_c(slice(ny - 2, ny), ycols[0:2]), xz_u(ny - 1, ucols[:, 0])], 2), "gy", up
    )
    ay = lax.ppermute(
        jnp.concatenate([xz_c(slice(0, 2), ycols[2:4]), xz_u(0, ucols[:, 1])], 2), "gy", down
    )

    xc = jnp.concatenate([ax[:, 0:2], jnp.zeros((nz + 4, 4, ny), f32), bx[:, 0:2]], 1)
    xu_hi = jnp.swapaxes(ax[1:-1, 2:5], 0, 1)[:, :, None]
    xu_lo = jnp.swapaxes(bx[1:-1, 2:5], 0, 1)[:, :, None]
    xu = jnp.concatenate([xu_hi, jnp.zeros((3, nz + 2, 6, ny), f32), xu_lo], 2)
    speeds_y = jnp.stack([by[..., 2:5], ay[..., 2:5]], 3).reshape(nz + 4, nx + 4, 6)
    fill = jnp.zeros((nz + 4, nx + 4, 118), f32)
    yt = jnp.concatenate([ay[..., 0:2], speeds_y, fill, by[..., 0:2]], 2)
    yt = jnp.pad(yt, ((0, 0), (6, 6), (0, 0)))
    return zlo_c, zhi_c, zlo_u, zhi_u, xc, xu, yt


def roll(values, shift, axis):
    return pltpu.roll(values, shift % values.shape[axis], axis)


def stencil(c, below, above, speeds):
    running = -6.0 * KAPPA * c
    for d in range(3):
        b, a, s = below[d], above[d], speeds[d]
        running = running + KAPPA * (b + a) - (
            jnp.maximum(s, 0.0) * (c - b) + jnp.minimum(s, 0.0) * (a - c)
        )
    return running


def transport_kernel(
    grid, place, weights, c_ref, v_ref, poro_ref, sat_ref, zlo_c, zhi_c, zlo_u, zhi_u,
    xc, xu, yt, adv_ref, part_ref, F, U, S, SG, H,
):
    nz, nx, ny = c_ref.shape
    wx, wy = F.shape[1], F.shape[2]
    f32 = jnp.float32
    pool_y = (
        lax.broadcasted_iota(jnp.int32, (ny, ny // 2), 0) // 2
        == lax.broadcasted_iota(jnp.int32, (ny, ny // 2), 1)
    ).astype(f32)
    F[0:2, 8 : 8 + nx, 0:ny] = zlo_c[...]
    F[nz + 2 : nz + 4, 8 : 8 + nx, 0:ny] = zhi_c[...]

    def put_c(z, carry):
        F[z + 2, 8 : 8 + nx, 0:ny] = c_ref[z]
        return carry

    lax.fori_loop(0, nz, put_c, 0)
    F[:, 0:8, 0:ny] = xc[...]
    F[:, wx - 8 : wx, 0:ny] = xc[...]
    F[:, :, ny:wy] = yt[...]
    for d in range(3):
        U[d, 0, 8 : 8 + nx, 0:ny] = zlo_u[d]
        U[d, nz + 1, 8 : 8 + nx, 0:ny] = zhi_u[d]

        def put_u(z, carry, d=d):
            U[d, z + 1, 8 : 8 + nx, 0:ny] = v_ref[d, 0, z].astype(f32)
            return carry

        lax.fori_loop(0, nz, put_u, 0)
        U[d, :, 0:8, 0:ny] = xu[d]
        U[d, :, wx - 8 : wx, 0:ny] = xu[d]
        U[d, :, :, ny:wy] = roll(yt[1 : nz + 3], -(3 + 2 * d), 2)

    total_z, total_x, total_y = grid
    gz0 = place[0] * nz - 1
    gx = place[1] * nx - 8 + lax.broadcasted_iota(jnp.int32, (wx, wy), 0)
    lane = lax.broadcasted_iota(jnp.int32, (wx, wy), 1)
    gy = place[2] * ny + jnp.where(lane < ny + (wy - ny) // 2, lane, lane - wy)
    plane = (gx >= 0) & (gx < total_x) & (gy >= 0) & (gy < total_y)

    def first(k, carry):
        c0 = F[k + 1]
        below = (F[k], roll(c0, 1, 0), roll(c0, 1, 1))
        above = (F[k + 2], roll(c0, -1, 0), roll(c0, -1, 1))
        speeds = (U[0, k], U[1, k], U[2, k])
        section = c0 + stencil(c0, below, above, speeds)
        z = gz0 + k
        keep = plane & (z >= 0) & (z < total_z)
        S[k] = jnp.where(keep, section, 0.0)
        return carry

    lax.fori_loop(0, nz + 2, first, 0)

    live = place[3] > 0

    def core(values):
        return values[8 : 8 + nx, 0:ny]

    def second(j, carry):
        s_mid = S[j + 1]
        s0 = core(s_mid)
        below = (core(S[j]), core(roll(s_mid, 1, 0)), core(roll(s_mid, 1, 1)))
        above = (core(S[j + 2]), core(roll(s_mid, -1, 0)), core(roll(s_mid, -1, 1)))
        speeds = tuple(v_ref[d, 0, j].astype(f32) for d in range(3))
        c0 = c_ref[j]
        adv = 0.5 * (c0 + s0 + stencil(s0, below, above, speeds))
        adv = jnp.where(live, adv, 0.0)
        adv_ref[0, j] = adv
        p = poro_ref[0, j].astype(f32)
        w = sat_ref[0, j].astype(f32)
        SG[pl.ds(pl.multiple_of(j * nx, nx), nx)] = ARCHIE * jnp.exp(adv) * p * p * w * w
        return carry

    lax.fori_loop(0, nz, second, 0)
    H[...] = jnp.dot(SG[...], pool_y, precision=lax.Precision.HIGHEST, preferred_element_type=f32)
    half_rows = nz * nx // 2
    coarse = H[pl.ds(0, half_rows, stride=2)] + H[pl.ds(1, half_rows, stride=2)]
    cx = nx // 2
    resist_layers = part_ref.shape[0]
    for e in range(resist_layers):
        total = jnp.zeros((cx, ny // 2), f32)
        for z in range(nz):
            total = total + weights[e, z] * coarse[z * cx : (z + 1) * cx]
        part_ref[e] = total


def transport_call(place, weights, c, velocity, porosity, saturation, *pieces, grid):
    nz, nx, ny = c.shape
    wx, wy = nx + 16, ny + 128
    resist_layers = weights.shape[0]
    vmem = pl.BlockSpec(memory_space=pltpu.VMEM)
    smem = pl.BlockSpec(memory_space=pltpu.SMEM)
    cells = nz * nx * ny
    return pl.pallas_call(
        functools.partial(transport_kernel, grid),
        out_shape=(
            jax.ShapeDtypeStruct((1, nz, nx, ny), jnp.float32),
            jax.ShapeDtypeStruct((resist_layers, nx // 2, ny // 2), jnp.float32),
        ),
        in_specs=[smem, smem] + [vmem] * 11,
        out_specs=(vmem, vmem),
        scratch_shapes=[
            pltpu.VMEM((nz + 4, wx, wy), jnp.float32),
            pltpu.VMEM((3, nz + 2, wx, wy), jnp.float32),
            pltpu.VMEM((nz + 2, wx, wy), jnp.float32),
            pltpu.VMEM((nz * nx, ny), jnp.float32),
            pltpu.VMEM((nz * nx, ny // 2), jnp.float32),
        ],
        compiler_params=pltpu.CompilerParams(vmem_limit_bytes=60 * 1024 * 1024),
        cost_estimate=pl.CostEstimate(
            flops=200 * cells, transcendentals=cells, bytes_accessed=40 * cells
        ),
    )(place, weights, c, velocity, porosity, saturation, *pieces)


def neighbours(padded, direction_index):
    leading = [slice(None)] * (padded.ndim - 3)
    middle = [slice(1, -1)] * 3
    below_slices = list(middle)
    below_slices[direction_index] = slice(0, -2)
    above_slices = list(middle)
    above_slices[direction_index] = slice(2, None)
    return (padded[tuple(leading + below_slices)], padded[tuple(leading + above_slices)])


def tendency(padded, speeds):
    center = padded[1:-1, 1:-1, 1:-1]
    running = -6.0 * KAPPA * center
    for direction_index in range(3):
        below_cells, above_cells = neighbours(padded, direction_index)
        speed_comp = speeds[direction_index]
        running = (
            running
            + KAPPA * (below_cells + above_cells)
            - (
                jnp.maximum(speed_comp, 0.0) * (center - below_cells)
                + jnp.minimum(speed_comp, 0.0) * (above_cells - center)
            )
        )
    return running


def inside(start, count, total):
    ids = start + jnp.arange(count, dtype=jnp.int32)
    return (ids >= 0) & (ids < total)


def plane_halo(values, depth):
    rows, columns = lax.axis_size("gx"), lax.axis_size("gy")
    d = depth

    def line(n, step):
        return [(i, i + step) for i in range(n) if 0 <= i + step < n]

    def flat(i, j):
        return i * columns + j

    def diagonal(di, dj):
        return [
            (flat(i, j), flat(i + di, j + dj))
            for i in range(rows)
            for j in range(columns)
            if 0 <= i + di < rows and 0 <= j + dj < columns
        ]

    both = ("gx", "gy")
    lo_x = lax.ppermute(values[:, -d:, :], "gx", line(rows, 1))
    hi_x = lax.ppermute(values[:, :d, :], "gx", line(rows, -1))
    lo_y = lax.ppermute(values[:, :, -d:], "gy", line(columns, 1))
    hi_y = lax.ppermute(values[:, :, :d], "gy", line(columns, -1))
    lo_lo = lax.ppermute(values[:, -d:, -d:], both, diagonal(1, 1))
    lo_hi = lax.ppermute(values[:, -d:, :d], both, diagonal(1, -1))
    hi_lo = lax.ppermute(values[:, :d, -d:], both, diagonal(-1, 1))
    hi_hi = lax.ppermute(values[:, :d, :d], both, diagonal(-1, -1))
    top = jnp.concatenate([lo_lo, lo_x, lo_hi], 2)
    middle = jnp.concatenate([lo_y, values, hi_y], 2)
    bottom = jnp.concatenate([hi_lo, hi_x, hi_hi], 2)
    return jnp.concatenate([top, middle, bottom], 1)


def sweeps_kernel(cond_ref, pot_ref, rhs_ref, mask_ref, out_ref, P):
    c = cond_ref[...]
    center = c[1:-1]
    faces = []
    diagonal = jnp.zeros_like(center)
    for d in range(3):
        if d == 0:
            lo, hi = c[:-2], c[2:]
        else:
            lo, hi = roll(center, 1, d), roll(center, -1, d)
        face_below = 0.5 * (center + lo)
        face_above = 0.5 * (center + hi)
        faces.append((face_below, face_above))
        diagonal = diagonal + face_below + face_above
    keep = mask_ref[...] > 0.0
    rhs = rhs_ref[...]
    P[...] = pot_ref[...]
    for sweep_index in range(SWEEPS):
        p = P[...]
        pc = p[1:-1]
        coupled = jnp.zeros_like(pc)
        for d in range(3):
            if d == 0:
                lo, hi = p[:-2], p[2:]
            else:
                lo, hi = roll(pc, 1, d), roll(pc, -1, d)
            coupled = coupled + faces[d][0] * lo + faces[d][1] * hi
        applied = diagonal * pc - coupled
        updated = pc + OMEGA * (rhs - applied) / diagonal
        P[1:-1] = jnp.where(keep, updated, 0.0)
    out_ref[...] = P[1:-1]


def sweeps_call(cond_wide, potential, source_terms, on_grid):
    zl, wx, wy = potential.shape[1:]
    px, py = -wx % 8, -wy % 128
    f32 = jnp.float32
    cond = jnp.pad(cond_wide, ((0, 0), (0, px), (0, py)))
    pot = jnp.pad(potential[0], ((1, 1), (0, px), (0, py)))
    rhs = jnp.pad(source_terms, ((0, 0), (0, px), (0, py)))
    mask = jnp.pad(on_grid.astype(f32), ((0, px), (0, py)))
    vmem = pl.BlockSpec(memory_space=pltpu.VMEM)
    out = pl.pallas_call(
        sweeps_kernel,
        out_shape=jax.ShapeDtypeStruct((zl, wx + px, wy + py), f32),
        in_specs=[vmem] * 4,
        out_specs=vmem,
        scratch_shapes=[pltpu.VMEM((zl + 2, wx + px, wy + py), f32)],
        cost_estimate=pl.CostEstimate(
            flops=40 * SWEEPS * zl * wx * wy, transcendentals=0, bytes_accessed=16 * zl * wx * wy
        ),
    )(cond, pot, rhs, mask)
    return out[:, SWEEPS : wx - SWEEPS, SWEEPS : wy - SWEEPS]


def grp_sum(partial, slabs):
    groups = lax.axis_size("grp")
    me = lax.axis_index("grp")
    received = {}
    for shift in range(1, groups):
        pairs = [(g, (g + shift) % groups) for g in range(slabs)]
        received[shift] = lax.ppermute(partial, "grp", pairs)
    total = None
    for owner in range(slabs):
        share = partial
        for shift in range(1, groups):
            share = jnp.where((me - shift) % groups == owner, received[shift], share)
        total = share if total is None else total + share
    return total


def on_device(conc, velocity, porosity, saturation, layer_counts, electrodes, init_potential):
    group_index = lax.axis_index("grp")
    row_index = lax.axis_index("gx")
    column_index = lax.axis_index("gy")
    groups = lax.axis_size("grp")
    rows = lax.axis_size("gx")
    columns = lax.axis_size("gy")
    active = group_index < 3
    field = conc[0]
    layers, tile_x, tile_y = field.shape
    slabs = 3
    speeds = velocity[:, 0]

    ends = jnp.cumsum(layer_counts)
    starts = ends - layer_counts
    layer_ids = group_index * layers + jnp.arange(layers, dtype=jnp.int32)
    member = (
        (layer_ids[None, :] >= starts[:, None]) & (layer_ids[None, :] < ends[:, None]) & active
    ).astype(jnp.float32)
    weights = member / (4.0 * layer_counts.astype(jnp.float32))[:, None]
    resist_layers = layer_counts.shape[0]
    coarse_x = tile_x // 2
    coarse_y = tile_y // 2

    pieces = transport_halo(field, velocity, slabs)
    place = jnp.stack([group_index, row_index, column_index, active.astype(jnp.int32)])
    advanced, partial_cond = transport_call(
        place, weights, field, velocity, porosity, saturation, *pieces,
        grid=(slabs * layers, rows * tile_x, columns * tile_y),
    )
    conductivity = grp_sum(partial_cond, slabs)

    grid_x = coarse_x * rows
    grid_y = coarse_y * columns
    depth = SWEEPS
    potential = lax.dynamic_slice_in_dim(init_potential, group_index, 1, 0)
    poles = lax.dynamic_slice_in_dim(electrodes, group_index, 1, 0)

    both = with_halo(jnp.concatenate([conductivity, potential[0]], axis=0), (("gx", 1), ("gy", 2)), depth)
    cond_wide = jnp.pad(both[:resist_layers], ((1, 1), (0, 0), (0, 0)))
    potential = both[None, resist_layers:]
    wide_x = coarse_x + 2 * depth
    wide_y = coarse_y + 2 * depth
    gx_ids = row_index * coarse_x - depth + jnp.arange(wide_x, dtype=jnp.int32)
    gy_ids = column_index * coarse_y - depth + jnp.arange(wide_y, dtype=jnp.int32)
    flat_ids = (
        jnp.arange(resist_layers, dtype=jnp.int32)[:, None, None] * (grid_x * grid_y)
        + gx_ids[None, :, None] * grid_y
        + gy_ids[None, None, :]
    )
    source_terms = AMPLITUDE * (
        (flat_ids[None] == poles[:, 0, None, None, None]).astype(jnp.float32)
        - (flat_ids[None] == poles[:, 1, None, None, None]).astype(jnp.float32)
    )
    on_grid = (
        ((gx_ids >= 0) & (gx_ids < grid_x))[:, None] & ((gy_ids >= 0) & (gy_ids < grid_y))[None, :]
    )

    potential = sweeps_call(cond_wide, potential, source_terms[0], on_grid)[None]

    return (advanced, conductivity, potential)


def solution(mesh):
    in_specs = (
        P("grp", None, "gx", "gy"),
        P(None, "grp", None, "gx", "gy"),
        P("grp", None, "gx", "gy"),
        P("grp", None, "gx", "gy"),
        P(),
        P(),
        P(None, None, "gx", "gy"),
    )
    out_specs = (P("grp", None, "gx", "gy"), P(None, "gx", "gy"), P("grp", None, "gx", "gy"))
    return jax.shard_map(
        on_device, mesh=mesh, in_specs=in_specs, out_specs=out_specs, check_vma=False
    )
```

```python
import functools

import jax
import jax.numpy as jnp
from jax.experimental import pallas as pl
from jax.experimental.pallas import tpu as pltpu
from jax import lax
from jax.sharding import PartitionSpec as P

SWEEPS = 3


KAPPA = 0.06
OMEGA = 0.8
AMPLITUDE = 40.0
ARCHIE = 20.0


def with_halo(shard, sides, width, top=None):
    for axis, dim in sides:
        devices, length = (lax.axis_size(axis), shard.shape[dim])
        last_member = devices if (axis != "grp" or top is None) else top
        up = [(i, i + 1) for i in range(last_member - 1)]
        down = [(j, i) for i, j in up]
        last = lax.slice_in_dim(shard, length - width, length, axis=dim)
        initial = lax.slice_in_dim(shard, 0, width, axis=dim)
        before = lax.ppermute(last, axis, up)
        after = lax.ppermute(initial, axis, down)
        shard = jnp.concatenate([before, shard, after], axis=dim)
    return shard


def faces_kernel(c_ref, v_ref, zs_up, zs_dn, xr, yc_ref, yu_ref):
    nzx, ny = c_ref.shape
    nz = xr.shape[1]
    nx = nzx // nz
    f32 = jnp.float32
    zs_up[0:2] = c_ref[nzx - 2 * nx : nzx].reshape(2, nx, ny)
    zs_dn[0:2] = c_ref[0 : 2 * nx].reshape(2, nx, ny)
    for d in range(3):
        zs_up[2 + d] = v_ref[d, nzx - nx : nzx].astype(f32)
        zs_dn[2 + d] = v_ref[d, 0:nx].astype(f32)
    for z in range(nz):
        base = z * nx
        xr[0, z : z + 1] = c_ref[base + nx - 2 : base + nx - 1]
        xr[1, z : z + 1] = c_ref[base + nx - 1 : base + nx]
        xr[5, z : z + 1] = c_ref[base : base + 1]
        xr[6, z : z + 1] = c_ref[base + 1 : base + 2]
        for d in range(3):
            top = v_ref[d, base + nx - 16 : base + nx].astype(f32)
            bottom = v_ref[d, base : base + 16].astype(f32)
            xr[2 + d, z : z + 1] = top[15:16]
            xr[7 + d, z : z + 1] = bottom[0:1]
    lane = lax.broadcasted_iota(jnp.int32, (8, ny), 1)
    row = lax.broadcasted_iota(jnp.int32, (8, ny), 0)
    pick_c = (
        ((row == 0) & (lane == ny - 2))
        | ((row == 1) & (lane == ny - 1))
        | ((row == 2) & (lane == 0))
        | ((row == 3) & (lane == 1))
    )
    pick_u = ((row == 0) & (lane == ny - 1)) | ((row == 1) & (lane == 0))
    nt = (((1,), (1,)), ((), ()))
    yc_ref[...] = lax.dot_general(
        pick_c.astype(f32), c_ref[...], nt, precision=lax.Precision.HIGHEST,
        preferred_element_type=f32,
    )
    for d in range(3):
        yu_ref[d] = lax.dot_general(
            pick_u.astype(jnp.bfloat16), v_ref[d], nt, preferred_element_type=f32
        )


def faces_call(c, velocity):
    nz, nx, ny = c.shape
    f32 = jnp.float32
    vmem = pl.BlockSpec(memory_space=pltpu.VMEM)
    return pl.pallas_call(
        faces_kernel,
        out_shape=(
            jax.ShapeDtypeStruct((5, nx, ny), f32),
            jax.ShapeDtypeStruct((5, nx, ny), f32),
            jax.ShapeDtypeStruct((10, nz, ny), f32),
            jax.ShapeDtypeStruct((8, nz * nx), f32),
            jax.ShapeDtypeStruct((3, 8, nz * nx), f32),
        ),
        in_specs=[vmem, vmem],
        out_specs=(vmem,) * 5,
        compiler_params=pltpu.CompilerParams(vmem_limit_bytes=32 * 1024 * 1024),
        cost_estimate=pl.CostEstimate(
            flops=2 * 32 * nz * nx * ny, transcendentals=0, bytes_accessed=10 * nz * nx * ny
        ),
    )(c.reshape(nz * nx, ny), velocity.reshape(3, nz * nx, ny))


def transport_halo(c, u, slabs):
    f32 = jnp.float32
    nz, nx, ny = c.shape
    zs_up, zs_dn, xr, ycols, ucols = faces_call(c, u)
    ycols = ycols.reshape(8, nz, nx)
    ucols = ucols.reshape(3, 8, nz, nx)

    def chain(axis, members):
        up = [(i, i + 1) for i in range(members - 1)]
        return up, [(j, i) for i, j in up]

    up, down = chain("grp", slabs)
    below = lax.ppermute(zs_up, "grp", up)
    above = lax.ppermute(zs_dn, "grp", down)
    zlo_c, zlo_u = below[:2], below[2:]
    zhi_c, zhi_u = above[:2], above[2:]

    def zext_c(rows, picked):
        return jnp.concatenate([zlo_c[:, rows], jnp.swapaxes(picked, 0, 1), zhi_c[:, rows]], 0)

    def zext_u(row, picked):
        core = jnp.concatenate([zlo_u[:, None, row], picked, zhi_u[:, None, row]], 1)
        return jnp.pad(core, ((0, 0), (1, 1), (0, 0)))

    rows = lax.axis_size("gx")
    up, down = chain("gx", rows)
    send_up = jnp.concatenate(
        [zext_c(slice(nx - 2, nx), xr[0:2]), jnp.swapaxes(zext_u(nx - 1, xr[2:5]), 0, 1)], 1
    )
    send_dn = jnp.concatenate(
        [zext_c(slice(0, 2), xr[5:7]), jnp.swapaxes(zext_u(0, xr[7:10]), 0, 1)], 1
    )
    bx = lax.ppermute(send_up, "gx", up)
    ax = lax.ppermute(send_dn, "gx", down)

    def xz_c(lanes, picked):
        core = jnp.concatenate([zlo_c[..., lanes], jnp.moveaxis(picked, 0, 2), zhi_c[..., lanes]], 0)
        return jnp.concatenate([bx[:, 0:2, lanes], core, ax[:, 0:2, lanes]], 1)

    def xz_u(lane, picked):
        core = jnp.pad(
            jnp.concatenate([zlo_u[:, None, :, lane], picked, zhi_u[:, None, :, lane]], 1),
            ((0, 0), (1, 1), (0, 0)),
        )
        lo = jnp.swapaxes(bx[:, 2:5, lane], 0, 1)[:, :, None]
        hi = jnp.swapaxes(ax[:, 2:5, lane], 0, 1)[:, :, None]
        zero = jnp.zeros_like(lo)
        return jnp.moveaxis(jnp.concatenate([zero, lo, core, hi, zero], 2), 0, 2)

    columns = lax.axis_size("gy")
    up, down = chain("gy", columns)
    by = lax.ppermute(
        jnp.concatenate([xz_c(slice(ny - 2, ny), ycols[0:2]), xz_u(ny - 1, ucols[:, 0])], 2), "gy", up
    )
    ay = lax.ppermute(
        jnp.concatenate([xz_c(slice(0, 2), ycols[2:4]), xz_u(0, ucols[:, 1])], 2), "gy", down
    )

    xc = jnp.concatenate([ax[:, 0:2], jnp.zeros((nz + 4, 4, ny), f32), bx[:, 0:2]], 1)
    xu_hi = jnp.swapaxes(ax[1:-1, 2:5], 0, 1)[:, :, None]
    xu_lo = jnp.swapaxes(bx[1:-1, 2:5], 0, 1)[:, :, None]
    xu = jnp.concatenate([xu_hi, jnp.zeros((3, nz + 2, 6, ny), f32), xu_lo], 2)
    speeds_y = jnp.stack([by[..., 2:5], ay[..., 2:5]], 3).reshape(nz + 4, nx + 4, 6)
    fill = jnp.zeros((nz + 4, nx + 4, 118), f32)
    yt = jnp.concatenate([ay[..., 0:2], speeds_y, fill, by[..., 0:2]], 2)
    return zlo_c, zhi_c, zlo_u, zhi_u, xc, xu, yt


def roll(values, shift, axis):
    return pltpu.roll(values, shift % values.shape[axis], axis)


def stencil(c, below, above, speeds):
    running = -6.0 * KAPPA * c
    for d in range(3):
        b, a, s = below[d], above[d], speeds[d]
        running = running + KAPPA * (b + a) - (
            jnp.maximum(s, 0.0) * (c - b) + jnp.minimum(s, 0.0) * (a - c)
        )
    return running


def transport_kernel(
    grid, place, weights, c_ref, v_ref, poro_ref, sat_ref, zlo_c, zhi_c, zlo_u, zhi_u,
    xc, xu, yt, adv_ref, part_ref, F, U, S, SG, H,
):
    nz, nx, ny = c_ref.shape
    wx, wy = F.shape[1], F.shape[2]
    f32 = jnp.float32
    pool_y = (
        lax.broadcasted_iota(jnp.int32, (ny, ny // 2), 0) // 2
        == lax.broadcasted_iota(jnp.int32, (ny, ny // 2), 1)
    ).astype(f32)
    F[0:2, 8 : 8 + nx, 0:ny] = zlo_c[...]
    F[nz + 2 : nz + 4, 8 : 8 + nx, 0:ny] = zhi_c[...]

    def put_c(z, carry):
        F[z + 2, 8 : 8 + nx, 0:ny] = c_ref[z]
        return carry

    lax.fori_loop(0, nz, put_c, 0)
    F[:, 0:8, 0:ny] = xc[...]
    F[:, wx - 8 : wx, 0:ny] = xc[...]
    F[:, 6 : 6 + nx + 4, ny:wy] = yt[...]
    for d in range(3):
        U[d, 0, 8 : 8 + nx, 0:ny] = zlo_u[d]
        U[d, nz + 1, 8 : 8 + nx, 0:ny] = zhi_u[d]

        def put_u(z, carry, d=d):
            U[d, z + 1, 8 : 8 + nx, 0:ny] = v_ref[d, 0, z].astype(f32)
            return carry

        lax.fori_loop(0, nz, put_u, 0)
        U[d, :, 0:8, 0:ny] = xu[d]
        U[d, :, wx - 8 : wx, 0:ny] = xu[d]
        U[d, :, 6 : 6 + nx + 4, ny:wy] = roll(yt[1 : nz + 3], -(3 + 2 * d), 2)

    total_z, total_x, total_y = grid
    gz0 = place[0] * nz - 1
    gx = place[1] * nx - 8 + lax.broadcasted_iota(jnp.int32, (wx, wy), 0)
    lane = lax.broadcasted_iota(jnp.int32, (wx, wy), 1)
    gy = place[2] * ny + jnp.where(lane < ny + (wy - ny) // 2, lane, lane - wy)
    plane = (gx >= 0) & (gx < total_x) & (gy >= 0) & (gy < total_y)

    def first(k, carry):
        c0 = F[k + 1]
        below = (F[k], roll(c0, 1, 0), roll(c0, 1, 1))
        above = (F[k + 2], roll(c0, -1, 0), roll(c0, -1, 1))
        speeds = (U[0, k], U[1, k], U[2, k])
        section = c0 + stencil(c0, below, above, speeds)
        z = gz0 + k
        keep = plane & (z >= 0) & (z < total_z)
        S[k] = jnp.where(keep, section, 0.0)
        return carry

    lax.fori_loop(0, nz + 2, first, 0)

    live = place[3] > 0

    def core(values):
        return values[8 : 8 + nx, 0:ny]

    def second(j, carry):
        s_mid = S[j + 1]
        s0 = core(s_mid)
        below = (core(S[j]), core(roll(s_mid, 1, 0)), core(roll(s_mid, 1, 1)))
        above = (core(S[j + 2]), core(roll(s_mid, -1, 0)), core(roll(s_mid, -1, 1)))
        speeds = tuple(v_ref[d, 0, j].astype(f32) for d in range(3))
        c0 = c_ref[j]
        adv = 0.5 * (c0 + s0 + stencil(s0, below, above, speeds))
        adv = jnp.where(live, adv, 0.0)
        adv_ref[0, j] = adv
        p = poro_ref[0, j].astype(f32)
        w = sat_ref[0, j].astype(f32)
        SG[pl.ds(pl.multiple_of(j * nx, nx), nx)] = ARCHIE * jnp.exp(adv) * p * p * w * w
        return carry

    lax.fori_loop(0, nz, second, 0)
    H[...] = jnp.dot(SG[...], pool_y, precision=lax.Precision.HIGHEST, preferred_element_type=f32)
    half_rows = nz * nx // 2
    coarse = H[pl.ds(0, half_rows, stride=2)] + H[pl.ds(1, half_rows, stride=2)]
    cx = nx // 2
    resist_layers = part_ref.shape[0]
    for e in range(resist_layers):
        total = jnp.zeros((cx, ny // 2), f32)
        for z in range(nz):
            total = total + weights[e, z] * coarse[z * cx : (z + 1) * cx]
        part_ref[e] = total


def transport_call(place, weights, c, velocity, porosity, saturation, *pieces, grid):
    nz, nx, ny = c.shape
    wx, wy = nx + 16, ny + 128
    resist_layers = weights.shape[0]
    vmem = pl.BlockSpec(memory_space=pltpu.VMEM)
    smem = pl.BlockSpec(memory_space=pltpu.SMEM)
    cells = nz * nx * ny
    return pl.pallas_call(
        functools.partial(transport_kernel, grid),
        out_shape=(
            jax.ShapeDtypeStruct((1, nz, nx, ny), jnp.float32),
            jax.ShapeDtypeStruct((resist_layers, nx // 2, ny // 2), jnp.float32),
        ),
        in_specs=[smem, smem] + [vmem] * 11,
        out_specs=(vmem, vmem),
        scratch_shapes=[
            pltpu.VMEM((nz + 4, wx, wy), jnp.float32),
            pltpu.VMEM((3, nz + 2, wx, wy), jnp.float32),
            pltpu.VMEM((nz + 2, wx, wy), jnp.float32),
            pltpu.VMEM((nz * nx, ny), jnp.float32),
            pltpu.VMEM((nz * nx, ny // 2), jnp.float32),
        ],
        compiler_params=pltpu.CompilerParams(vmem_limit_bytes=60 * 1024 * 1024),
        cost_estimate=pl.CostEstimate(
            flops=200 * cells, transcendentals=cells, bytes_accessed=40 * cells
        ),
    )(place, weights, c, velocity, porosity, saturation, *pieces)


def neighbours(padded, direction_index):
    leading = [slice(None)] * (padded.ndim - 3)
    middle = [slice(1, -1)] * 3
    below_slices = list(middle)
    below_slices[direction_index] = slice(0, -2)
    above_slices = list(middle)
    above_slices[direction_index] = slice(2, None)
    return (padded[tuple(leading + below_slices)], padded[tuple(leading + above_slices)])


def tendency(padded, speeds):
    center = padded[1:-1, 1:-1, 1:-1]
    running = -6.0 * KAPPA * center
    for direction_index in range(3):
        below_cells, above_cells = neighbours(padded, direction_index)
        speed_comp = speeds[direction_index]
        running = (
            running
            + KAPPA * (below_cells + above_cells)
            - (
                jnp.maximum(speed_comp, 0.0) * (center - below_cells)
                + jnp.minimum(speed_comp, 0.0) * (above_cells - center)
            )
        )
    return running


def inside(start, count, total):
    ids = start + jnp.arange(count, dtype=jnp.int32)
    return (ids >= 0) & (ids < total)


def plane_halo(values, depth):
    rows, columns = lax.axis_size("gx"), lax.axis_size("gy")
    d = depth

    def line(n, step):
        return [(i, i + step) for i in range(n) if 0 <= i + step < n]

    def flat(i, j):
        return i * columns + j

    def diagonal(di, dj):
        return [
            (flat(i, j), flat(i + di, j + dj))
            for i in range(rows)
            for j in range(columns)
            if 0 <= i + di < rows and 0 <= j + dj < columns
        ]

    both = ("gx", "gy")
    lo_x = lax.ppermute(values[:, -d:, :], "gx", line(rows, 1))
    hi_x = lax.ppermute(values[:, :d, :], "gx", line(rows, -1))
    lo_y = lax.ppermute(values[:, :, -d:], "gy", line(columns, 1))
    hi_y = lax.ppermute(values[:, :, :d], "gy", line(columns, -1))
    lo_lo = lax.ppermute(values[:, -d:, -d:], both, diagonal(1, 1))
    lo_hi = lax.ppermute(values[:, -d:, :d], both, diagonal(1, -1))
    hi_lo = lax.ppermute(values[:, :d, -d:], both, diagonal(-1, 1))
    hi_hi = lax.ppermute(values[:, :d, :d], both, diagonal(-1, -1))
    top = jnp.concatenate([lo_lo, lo_x, lo_hi], 2)
    middle = jnp.concatenate([lo_y, values, hi_y], 2)
    bottom = jnp.concatenate([hi_lo, hi_x, hi_hi], 2)
    return jnp.concatenate([top, middle, bottom], 1)


def grp_sum(partial, slabs):
    groups = lax.axis_size("grp")
    me = lax.axis_index("grp")
    received = {}
    for shift in range(1, groups):
        pairs = [(g, (g + shift) % groups) for g in range(slabs)]
        received[shift] = lax.ppermute(partial, "grp", pairs)
    total = None
    for owner in range(slabs):
        share = partial
        for shift in range(1, groups):
            share = jnp.where((me - shift) % groups == owner, received[shift], share)
        total = share if total is None else total + share
    return total


def on_device(conc, velocity, porosity, saturation, layer_counts, electrodes, init_potential):
    group_index = lax.axis_index("grp")
    row_index = lax.axis_index("gx")
    column_index = lax.axis_index("gy")
    groups = lax.axis_size("grp")
    rows = lax.axis_size("gx")
    columns = lax.axis_size("gy")
    active = group_index < 3
    field = conc[0]
    layers, tile_x, tile_y = field.shape
    slabs = 3
    speeds = velocity[:, 0]

    ends = jnp.cumsum(layer_counts)
    starts = ends - layer_counts
    layer_ids = group_index * layers + jnp.arange(layers, dtype=jnp.int32)
    member = (
        (layer_ids[None, :] >= starts[:, None]) & (layer_ids[None, :] < ends[:, None]) & active
    ).astype(jnp.float32)
    weights = member / (4.0 * layer_counts.astype(jnp.float32))[:, None]
    resist_layers = layer_counts.shape[0]
    coarse_x = tile_x // 2
    coarse_y = tile_y // 2

    pieces = transport_halo(field, velocity, slabs)
    place = jnp.stack([group_index, row_index, column_index, active.astype(jnp.int32)])
    advanced, partial_cond = transport_call(
        place, weights, field, velocity, porosity, saturation, *pieces,
        grid=(slabs * layers, rows * tile_x, columns * tile_y),
    )
    conductivity = grp_sum(partial_cond, slabs)

    grid_x = coarse_x * rows
    grid_y = coarse_y * columns
    depth = SWEEPS
    potential = lax.dynamic_slice_in_dim(init_potential, group_index, 1, 0)
    poles = lax.dynamic_slice_in_dim(electrodes, group_index, 1, 0)

    both = with_halo(jnp.concatenate([conductivity, potential[0]], axis=0), (("gx", 1), ("gy", 2)), depth)
    cond_wide = jnp.pad(both[:resist_layers], ((1, 1), (0, 0), (0, 0)))
    potential = both[None, resist_layers:]
    wide_x = coarse_x + 2 * depth
    wide_y = coarse_y + 2 * depth
    gx_ids = row_index * coarse_x - depth + jnp.arange(wide_x, dtype=jnp.int32)
    gy_ids = column_index * coarse_y - depth + jnp.arange(wide_y, dtype=jnp.int32)
    flat_ids = (
        jnp.arange(resist_layers, dtype=jnp.int32)[:, None, None] * (grid_x * grid_y)
        + gx_ids[None, :, None] * grid_y
        + gy_ids[None, None, :]
    )
    source_terms = AMPLITUDE * (
        (flat_ids[None] == poles[:, 0, None, None, None]).astype(jnp.float32)
        - (flat_ids[None] == poles[:, 1, None, None, None]).astype(jnp.float32)
    )
    on_grid = (
        ((gx_ids >= 0) & (gx_ids < grid_x))[:, None] & ((gy_ids >= 0) & (gy_ids < grid_y))[None, :]
    )

    for sweep_index in range(SWEEPS):
        m = sweep_index + 1
        nx, ny = wide_x - 2 * m, wide_y - 2 * m
        center_c = cond_wide[1:-1, m : m + nx, m : m + ny]
        faces = []
        diagonal = jnp.zeros_like(center_c)
        for d in range(3):
            if d == 0:
                lo = cond_wide[0:-2, m : m + nx, m : m + ny]
                hi = cond_wide[2:, m : m + nx, m : m + ny]
            elif d == 1:
                lo = cond_wide[1:-1, m - 1 : m - 1 + nx, m : m + ny]
                hi = cond_wide[1:-1, m + 1 : m + 1 + nx, m : m + ny]
            else:
                lo = cond_wide[1:-1, m : m + nx, m - 1 : m - 1 + ny]
                hi = cond_wide[1:-1, m : m + nx, m + 1 : m + 1 + ny]
            face_below = 0.5 * (center_c + lo)
            face_above = 0.5 * (center_c + hi)
            faces.append((face_below, face_above))
            diagonal = diagonal + face_below + face_above
        pot_z = jnp.pad(potential, ((0, 0), (1, 1), (0, 0), (0, 0)))
        pot_c = potential[:, :, 1:-1, 1:-1]
        coupled = jnp.zeros_like(pot_c)
        for d in range(3):
            if d == 0:
                lo = pot_z[:, 0:-2, 1:-1, 1:-1]
                hi = pot_z[:, 2:, 1:-1, 1:-1]
            elif d == 1:
                lo = potential[:, :, 0:-2, 1:-1]
                hi = potential[:, :, 2:, 1:-1]
            else:
                lo = potential[:, :, 1:-1, 0:-2]
                hi = potential[:, :, 1:-1, 2:]
            coupled = coupled + faces[d][0] * lo + faces[d][1] * hi
        applied = diagonal * pot_c - coupled
        rhs = source_terms[:, :, m : m + nx, m : m + ny]
        updated = pot_c + OMEGA * (rhs - applied) / diagonal
        potential = jnp.where(on_grid[m : m + nx, m : m + ny], updated, 0.0)

    return (advanced, conductivity, potential)


def solution(mesh):
    in_specs = (
        P("grp", None, "gx", "gy"),
        P(None, "grp", None, "gx", "gy"),
        P("grp", None, "gx", "gy"),
        P("grp", None, "gx", "gy"),
        P(),
        P(),
        P(None, None, "gx", "gy"),
    )
    out_specs = (P("grp", None, "gx", "gy"), P(None, "gx", "gy"), P("grp", None, "gx", "gy"))
    return jax.shard_map(
        on_device, mesh=mesh, in_specs=in_specs, out_specs=out_specs, check_vma=False
    )
```

```python
import functools

import jax
import jax.numpy as jnp
from jax.experimental import pallas as pl
from jax.experimental.pallas import tpu as pltpu
from jax import lax
from jax.sharding import PartitionSpec as P

SWEEPS = 3


KAPPA = 0.06
OMEGA = 0.8
AMPLITUDE = 40.0
ARCHIE = 20.0


def with_halo(shard, sides, width, top=None):
    for axis, dim in sides:
        devices, length = (lax.axis_size(axis), shard.shape[dim])
        last_member = devices if (axis != "grp" or top is None) else top
        up = [(i, i + 1) for i in range(last_member - 1)]
        down = [(j, i) for i, j in up]
        last = lax.slice_in_dim(shard, length - width, length, axis=dim)
        initial = lax.slice_in_dim(shard, 0, width, axis=dim)
        before = lax.ppermute(last, axis, up)
        after = lax.ppermute(initial, axis, down)
        shard = jnp.concatenate([before, shard, after], axis=dim)
    return shard


def faces_kernel(c_ref, v_ref, zs_up, zs_dn, xr, yc_ref, yu_ref):
    nzx, ny = c_ref.shape
    nz = xr.shape[1]
    nx = nzx // nz
    f32 = jnp.float32
    zs_up[0:2] = c_ref[nzx - 2 * nx : nzx].reshape(2, nx, ny)
    zs_dn[0:2] = c_ref[0 : 2 * nx].reshape(2, nx, ny)
    for d in range(3):
        zs_up[2 + d] = v_ref[d, nzx - nx : nzx].astype(f32)
        zs_dn[2 + d] = v_ref[d, 0:nx].astype(f32)
    for z in range(nz):
        base = z * nx
        xr[0, z : z + 1] = c_ref[base + nx - 2 : base + nx - 1]
        xr[1, z : z + 1] = c_ref[base + nx - 1 : base + nx]
        xr[5, z : z + 1] = c_ref[base : base + 1]
        xr[6, z : z + 1] = c_ref[base + 1 : base + 2]
        for d in range(3):
            top = v_ref[d, base + nx - 16 : base + nx].astype(f32)
            bottom = v_ref[d, base : base + 16].astype(f32)
            xr[2 + d, z : z + 1] = top[15:16]
            xr[7 + d, z : z + 1] = bottom[0:1]
    lane = lax.broadcasted_iota(jnp.int32, (8, ny), 1)
    row = lax.broadcasted_iota(jnp.int32, (8, ny), 0)
    pick_c = (
        ((row == 0) & (lane == ny - 2))
        | ((row == 1) & (lane == ny - 1))
        | ((row == 2) & (lane == 0))
        | ((row == 3) & (lane == 1))
    )
    pick_u = ((row == 0) & (lane == ny - 1)) | ((row == 1) & (lane == 0))
    nt = (((1,), (1,)), ((), ()))
    yc_ref[...] = lax.dot_general(
        pick_c.astype(f32), c_ref[...], nt, precision=lax.Precision.HIGHEST,
        preferred_element_type=f32,
    )
    for d in range(3):
        yu_ref[d] = lax.dot_general(
            pick_u.astype(jnp.bfloat16), v_ref[d], nt, preferred_element_type=f32
        )


def faces_call(c, velocity):
    nz, nx, ny = c.shape
    f32 = jnp.float32
    vmem = pl.BlockSpec(memory_space=pltpu.VMEM)
    return pl.pallas_call(
        faces_kernel,
        out_shape=(
            jax.ShapeDtypeStruct((5, nx, ny), f32),
            jax.ShapeDtypeStruct((5, nx, ny), f32),
            jax.ShapeDtypeStruct((10, nz, ny), f32),
            jax.ShapeDtypeStruct((8, nz * nx), f32),
            jax.ShapeDtypeStruct((3, 8, nz * nx), f32),
        ),
        in_specs=[vmem, vmem],
        out_specs=(vmem,) * 5,
        compiler_params=pltpu.CompilerParams(vmem_limit_bytes=32 * 1024 * 1024),
        cost_estimate=pl.CostEstimate(
            flops=2 * 32 * nz * nx * ny, transcendentals=0, bytes_accessed=10 * nz * nx * ny
        ),
    )(c.reshape(nz * nx, ny), velocity.reshape(3, nz * nx, ny))


def transport_halo(c, u, slabs):
    f32 = jnp.float32
    nz, nx, ny = c.shape
    zs_up, zs_dn, xr, ycols, ucols = faces_call(c, u)
    ycols = ycols.reshape(8, nz, nx)
    ucols = ucols.reshape(3, 8, nz, nx)

    def chain(axis, members):
        up = [(i, i + 1) for i in range(members - 1)]
        return up, [(j, i) for i, j in up]

    up, down = chain("grp", slabs)
    below = lax.ppermute(zs_up, "grp", up)
    above = lax.ppermute(zs_dn, "grp", down)
    zlo_c, zlo_u = below[:2], below[2:]
    zhi_c, zhi_u = above[:2], above[2:]

    def zext_c(rows, picked):
        return jnp.concatenate([zlo_c[:, rows], jnp.swapaxes(picked, 0, 1), zhi_c[:, rows]], 0)

    def zext_u(row, picked):
        core = jnp.concatenate([zlo_u[:, None, row], picked, zhi_u[:, None, row]], 1)
        return jnp.pad(core, ((0, 0), (1, 1), (0, 0)))

    rows = lax.axis_size("gx")
    up, down = chain("gx", rows)
    send_up = jnp.concatenate(
        [zext_c(slice(nx - 2, nx), xr[0:2]), jnp.swapaxes(zext_u(nx - 1, xr[2:5]), 0, 1)], 1
    )
    send_dn = jnp.concatenate(
        [zext_c(slice(0, 2), xr[5:7]), jnp.swapaxes(zext_u(0, xr[7:10]), 0, 1)], 1
    )
    bx = lax.ppermute(send_up, "gx", up)
    ax = lax.ppermute(send_dn, "gx", down)

    def xz_c(lanes, picked):
        core = jnp.concatenate([zlo_c[..., lanes], jnp.moveaxis(picked, 0, 2), zhi_c[..., lanes]], 0)
        return jnp.concatenate([bx[:, 0:2, lanes], core, ax[:, 0:2, lanes]], 1)

    def xz_u(lane, picked):
        core = jnp.pad(
            jnp.concatenate([zlo_u[:, None, :, lane], picked, zhi_u[:, None, :, lane]], 1),
            ((0, 0), (1, 1), (0, 0)),
        )
        lo = jnp.swapaxes(bx[:, 2:5, lane], 0, 1)[:, :, None]
        hi = jnp.swapaxes(ax[:, 2:5, lane], 0, 1)[:, :, None]
        zero = jnp.zeros_like(lo)
        return jnp.moveaxis(jnp.concatenate([zero, lo, core, hi, zero], 2), 0, 2)

    columns = lax.axis_size("gy")
    up, down = chain("gy", columns)
    by = lax.ppermute(
        jnp.concatenate([xz_c(slice(ny - 2, ny), ycols[0:2]), xz_u(ny - 1, ucols[:, 0])], 2), "gy", up
    )
    ay = lax.ppermute(
        jnp.concatenate([xz_c(slice(0, 2), ycols[2:4]), xz_u(0, ucols[:, 1])], 2), "gy", down
    )

    xc = jnp.concatenate([ax[:, 0:2], jnp.zeros((nz + 4, 4, ny), f32), bx[:, 0:2]], 1)
    xu_hi = jnp.swapaxes(ax[1:-1, 2:5], 0, 1)[:, :, None]
    xu_lo = jnp.swapaxes(bx[1:-1, 2:5], 0, 1)[:, :, None]
    xu = jnp.concatenate([xu_hi, xu_lo], 2)
    speeds_y = jnp.stack([by[..., 2:5], ay[..., 2:5]], 3).reshape(nz + 4, nx + 4, 6)
    fill = jnp.zeros((nz + 4, nx + 4, 118), f32)
    yt = jnp.concatenate([ay[..., 0:2], speeds_y, fill, by[..., 0:2]], 2)
    return zlo_c, zhi_c, zlo_u, zhi_u, xc, xu, yt


def roll(values, shift, axis):
    return pltpu.roll(values, shift % values.shape[axis], axis)


def stencil(c, below, above, speeds):
    running = -6.0 * KAPPA * c
    for d in range(3):
        b, a, s = below[d], above[d], speeds[d]
        running = running + KAPPA * (b + a) - (
            jnp.maximum(s, 0.0) * (c - b) + jnp.minimum(s, 0.0) * (a - c)
        )
    return running


def transport_kernel(
    grid, place, weights, c_ref, v_ref, poro_ref, sat_ref, zlo_c, zhi_c, zlo_u, zhi_u,
    xc, xu, yt, adv_ref, part_ref, F, U, S, SG, H,
):
    nz, nx, ny = c_ref.shape
    wx, wy = F.shape[1], F.shape[2]
    f32 = jnp.float32
    pool_y = (
        lax.broadcasted_iota(jnp.int32, (ny, ny // 2), 0) // 2
        == lax.broadcasted_iota(jnp.int32, (ny, ny // 2), 1)
    ).astype(f32)
    F[0:2, 8 : 8 + nx, 0:ny] = zlo_c[...]
    F[nz + 2 : nz + 4, 8 : 8 + nx, 0:ny] = zhi_c[...]

    def put_c(z, carry):
        F[z + 2, 8 : 8 + nx, 0:ny] = c_ref[z]
        return carry

    lax.fori_loop(0, nz, put_c, 0)
    F[:, 0:8, 0:ny] = xc[...]
    F[:, wx - 8 : wx, 0:ny] = xc[...]
    F[:, 6 : 6 + nx + 4, ny:wy] = yt[...]
    for d in range(3):
        U[d, 0, 8 : 8 + nx, 0:ny] = zlo_u[d]
        U[d, nz + 1, 8 : 8 + nx, 0:ny] = zhi_u[d]

        def put_u(z, carry, d=d):
            U[d, z + 1, 8 : 8 + nx, 0:ny] = v_ref[d, 0, z].astype(f32)
            return carry

        lax.fori_loop(0, nz, put_u, 0)
        U[d, :, 7:8, 0:ny] = xu[d, :, 1:2]
        U[d, :, wx - 8 : wx - 7, 0:ny] = xu[d, :, 0:1]
        U[d, :, 6 : 6 + nx + 4, ny:wy] = roll(yt[1 : nz + 3], -(3 + 2 * d), 2)

    total_z, total_x, total_y = grid
    gz0 = place[0] * nz - 1
    gx = place[1] * nx - 8 + lax.broadcasted_iota(jnp.int32, (wx, wy), 0)
    lane = lax.broadcasted_iota(jnp.int32, (wx, wy), 1)
    gy = place[2] * ny + jnp.where(lane < ny + (wy - ny) // 2, lane, lane - wy)
    plane = (gx >= 0) & (gx < total_x) & (gy >= 0) & (gy < total_y)

    def first(k, carry):
        c0 = F[k + 1]
        below = (F[k], roll(c0, 1, 0), roll(c0, 1, 1))
        above = (F[k + 2], roll(c0, -1, 0), roll(c0, -1, 1))
        speeds = (U[0, k], U[1, k], U[2, k])
        section = c0 + stencil(c0, below, above, speeds)
        z = gz0 + k
        keep = plane & (z >= 0) & (z < total_z)
        S[k] = jnp.where(keep, section, 0.0)
        return carry

    lax.fori_loop(0, nz + 2, first, 0)

    live = place[3] > 0

    def core(values):
        return values[8 : 8 + nx, 0:ny]

    def second(j, carry):
        s_mid = S[j + 1]
        s0 = core(s_mid)
        below = (core(S[j]), core(roll(s_mid, 1, 0)), core(roll(s_mid, 1, 1)))
        above = (core(S[j + 2]), core(roll(s_mid, -1, 0)), core(roll(s_mid, -1, 1)))
        speeds = tuple(v_ref[d, 0, j].astype(f32) for d in range(3))
        c0 = c_ref[j]
        adv = 0.5 * (c0 + s0 + stencil(s0, below, above, speeds))
        adv = jnp.where(live, adv, 0.0)
        adv_ref[0, j] = adv
        p = poro_ref[0, j].astype(f32)
        w = sat_ref[0, j].astype(f32)
        SG[pl.ds(pl.multiple_of(j * nx, nx), nx)] = ARCHIE * jnp.exp(adv) * p * p * w * w
        return carry

    lax.fori_loop(0, nz, second, 0)
    H[...] = jnp.dot(SG[...], pool_y, precision=lax.Precision.HIGHEST, preferred_element_type=f32)
    half_rows = nz * nx // 2
    coarse = H[pl.ds(0, half_rows, stride=2)] + H[pl.ds(1, half_rows, stride=2)]
    cx = nx // 2
    resist_layers = part_ref.shape[0]
    for e in range(resist_layers):
        total = jnp.zeros((cx, ny // 2), f32)
        for z in range(nz):
            total = total + weights[e, z] * coarse[z * cx : (z + 1) * cx]
        part_ref[e] = total


def transport_call(place, weights, c, velocity, porosity, saturation, *pieces, grid):
    nz, nx, ny = c.shape
    wx, wy = nx + 16, ny + 128
    resist_layers = weights.shape[0]
    vmem = pl.BlockSpec(memory_space=pltpu.VMEM)
    smem = pl.BlockSpec(memory_space=pltpu.SMEM)
    cells = nz * nx * ny
    return pl.pallas_call(
        functools.partial(transport_kernel, grid),
        out_shape=(
            jax.ShapeDtypeStruct((1, nz, nx, ny), jnp.float32),
            jax.ShapeDtypeStruct((resist_layers, nx // 2, ny // 2), jnp.float32),
        ),
        in_specs=[smem, smem] + [vmem] * 11,
        out_specs=(vmem, vmem),
        scratch_shapes=[
            pltpu.VMEM((nz + 4, wx, wy), jnp.float32),
            pltpu.VMEM((3, nz + 2, wx, wy), jnp.float32),
            pltpu.VMEM((nz + 2, wx, wy), jnp.float32),
            pltpu.VMEM((nz * nx, ny), jnp.float32),
            pltpu.VMEM((nz * nx, ny // 2), jnp.float32),
        ],
        compiler_params=pltpu.CompilerParams(vmem_limit_bytes=60 * 1024 * 1024),
        cost_estimate=pl.CostEstimate(
            flops=200 * cells, transcendentals=cells, bytes_accessed=40 * cells
        ),
    )(place, weights, c, velocity, porosity, saturation, *pieces)


def neighbours(padded, direction_index):
    leading = [slice(None)] * (padded.ndim - 3)
    middle = [slice(1, -1)] * 3
    below_slices = list(middle)
    below_slices[direction_index] = slice(0, -2)
    above_slices = list(middle)
    above_slices[direction_index] = slice(2, None)
    return (padded[tuple(leading + below_slices)], padded[tuple(leading + above_slices)])


def tendency(padded, speeds):
    center = padded[1:-1, 1:-1, 1:-1]
    running = -6.0 * KAPPA * center
    for direction_index in range(3):
        below_cells, above_cells = neighbours(padded, direction_index)
        speed_comp = speeds[direction_index]
        running = (
            running
            + KAPPA * (below_cells + above_cells)
            - (
                jnp.maximum(speed_comp, 0.0) * (center - below_cells)
                + jnp.minimum(speed_comp, 0.0) * (above_cells - center)
            )
        )
    return running


def inside(start, count, total):
    ids = start + jnp.arange(count, dtype=jnp.int32)
    return (ids >= 0) & (ids < total)


def plane_halo(values, depth):
    rows, columns = lax.axis_size("gx"), lax.axis_size("gy")
    d = depth

    def line(n, step):
        return [(i, i + step) for i in range(n) if 0 <= i + step < n]

    def flat(i, j):
        return i * columns + j

    def diagonal(di, dj):
        return [
            (flat(i, j), flat(i + di, j + dj))
            for i in range(rows)
            for j in range(columns)
            if 0 <= i + di < rows and 0 <= j + dj < columns
        ]

    both = ("gx", "gy")
    lo_x = lax.ppermute(values[:, -d:, :], "gx", line(rows, 1))
    hi_x = lax.ppermute(values[:, :d, :], "gx", line(rows, -1))
    lo_y = lax.ppermute(values[:, :, -d:], "gy", line(columns, 1))
    hi_y = lax.ppermute(values[:, :, :d], "gy", line(columns, -1))
    lo_lo = lax.ppermute(values[:, -d:, -d:], both, diagonal(1, 1))
    lo_hi = lax.ppermute(values[:, -d:, :d], both, diagonal(1, -1))
    hi_lo = lax.ppermute(values[:, :d, -d:], both, diagonal(-1, 1))
    hi_hi = lax.ppermute(values[:, :d, :d], both, diagonal(-1, -1))
    top = jnp.concatenate([lo_lo, lo_x, lo_hi], 2)
    middle = jnp.concatenate([lo_y, values, hi_y], 2)
    bottom = jnp.concatenate([hi_lo, hi_x, hi_hi], 2)
    return jnp.concatenate([top, middle, bottom], 1)


def grp_sum(partial, slabs):
    groups = lax.axis_size("grp")
    me = lax.axis_index("grp")
    received = {}
    for shift in range(1, groups):
        pairs = [(g, (g + shift) % groups) for g in range(slabs)]
        received[shift] = lax.ppermute(partial, "grp", pairs)
    total = None
    for owner in range(slabs):
        share = partial
        for shift in range(1, groups):
            share = jnp.where((me - shift) % groups == owner, received[shift], share)
        total = share if total is None else total + share
    return total


def on_device(conc, velocity, porosity, saturation, layer_counts, electrodes, init_potential):
    group_index = lax.axis_index("grp")
    row_index = lax.axis_index("gx")
    column_index = lax.axis_index("gy")
    groups = lax.axis_size("grp")
    rows = lax.axis_size("gx")
    columns = lax.axis_size("gy")
    active = group_index < 3
    field = conc[0]
    layers, tile_x, tile_y = field.shape
    slabs = 3
    speeds = velocity[:, 0]

    ends = jnp.cumsum(layer_counts)
    starts = ends - layer_counts
    layer_ids = group_index * layers + jnp.arange(layers, dtype=jnp.int32)
    member = (
        (layer_ids[None, :] >= starts[:, None]) & (layer_ids[None, :] < ends[:, None]) & active
    ).astype(jnp.float32)
    weights = member / (4.0 * layer_counts.astype(jnp.float32))[:, None]
    resist_layers = layer_counts.shape[0]
    coarse_x = tile_x // 2
    coarse_y = tile_y // 2

    pieces = transport_halo(field, velocity, slabs)
    place = jnp.stack([group_index, row_index, column_index, active.astype(jnp.int32)])
    advanced, partial_cond = transport_call(
        place, weights, field, velocity, porosity, saturation, *pieces,
        grid=(slabs * layers, rows * tile_x, columns * tile_y),
    )
    conductivity = grp_sum(partial_cond, slabs)

    grid_x = coarse_x * rows
    grid_y = coarse_y * columns
    depth = SWEEPS
    potential = lax.dynamic_slice_in_dim(init_potential, group_index, 1, 0)
    poles = lax.dynamic_slice_in_dim(electrodes, group_index, 1, 0)

    both = with_halo(jnp.concatenate([conductivity, potential[0]], axis=0), (("gx", 1), ("gy", 2)), depth)
    cond_wide = jnp.pad(both[:resist_layers], ((1, 1), (0, 0), (0, 0)))
    potential = both[None, resist_layers:]
    wide_x = coarse_x + 2 * depth
    wide_y = coarse_y + 2 * depth
    gx_ids = row_index * coarse_x - depth + jnp.arange(wide_x, dtype=jnp.int32)
    gy_ids = column_index * coarse_y - depth + jnp.arange(wide_y, dtype=jnp.int32)
    flat_ids = (
        jnp.arange(resist_layers, dtype=jnp.int32)[:, None, None] * (grid_x * grid_y)
        + gx_ids[None, :, None] * grid_y
        + gy_ids[None, None, :]
    )
    source_terms = AMPLITUDE * (
        (flat_ids[None] == poles[:, 0, None, None, None]).astype(jnp.float32)
        - (flat_ids[None] == poles[:, 1, None, None, None]).astype(jnp.float32)
    )
    on_grid = (
        ((gx_ids >= 0) & (gx_ids < grid_x))[:, None] & ((gy_ids >= 0) & (gy_ids < grid_y))[None, :]
    )

    for sweep_index in range(SWEEPS):
        m = sweep_index + 1
        nx, ny = wide_x - 2 * m, wide_y - 2 * m
        center_c = cond_wide[1:-1, m : m + nx, m : m + ny]
        faces = []
        diagonal = jnp.zeros_like(center_c)
        for d in range(3):
            if d == 0:
                lo = cond_wide[0:-2, m : m + nx, m : m + ny]
                hi = cond_wide[2:, m : m + nx, m : m + ny]
            elif d == 1:
                lo = cond_wide[1:-1, m - 1 : m - 1 + nx, m : m + ny]
                hi = cond_wide[1:-1, m + 1 : m + 1 + nx, m : m + ny]
            else:
                lo = cond_wide[1:-1, m : m + nx, m - 1 : m - 1 + ny]
                hi = cond_wide[1:-1, m : m + nx, m + 1 : m + 1 + ny]
            face_below = 0.5 * (center_c + lo)
            face_above = 0.5 * (center_c + hi)
            faces.append((face_below, face_above))
            diagonal = diagonal + face_below + face_above
        pot_z = jnp.pad(potential, ((0, 0), (1, 1), (0, 0), (0, 0)))
        pot_c = potential[:, :, 1:-1, 1:-1]
        coupled = jnp.zeros_like(pot_c)
        for d in range(3):
            if d == 0:
                lo = pot_z[:, 0:-2, 1:-1, 1:-1]
                hi = pot_z[:, 2:, 1:-1, 1:-1]
            elif d == 1:
                lo = potential[:, :, 0:-2, 1:-1]
                hi = potential[:, :, 2:, 1:-1]
            else:
                lo = potential[:, :, 1:-1, 0:-2]
                hi = potential[:, :, 1:-1, 2:]
            coupled = coupled + faces[d][0] * lo + faces[d][1] * hi
        applied = diagonal * pot_c - coupled
        rhs = source_terms[:, :, m : m + nx, m : m + ny]
        updated = pot_c + OMEGA * (rhs - applied) / diagonal
        potential = jnp.where(on_grid[m : m + nx, m : m + ny], updated, 0.0)

    return (advanced, conductivity, potential)


def solution(mesh):
    in_specs = (
        P("grp", None, "gx", "gy"),
        P(None, "grp", None, "gx", "gy"),
        P("grp", None, "gx", "gy"),
        P("grp", None, "gx", "gy"),
        P(),
        P(),
        P(None, None, "gx", "gy"),
    )
    out_specs = (P("grp", None, "gx", "gy"), P(None, "gx", "gy"), P("grp", None, "gx", "gy"))
    return jax.shard_map(
        on_device, mesh=mesh, in_specs=in_specs, out_specs=out_specs, check_vma=False
    )
```

```python
import functools

import jax
import jax.numpy as jnp
from jax.experimental import pallas as pl
from jax.experimental.pallas import tpu as pltpu
from jax import lax
from jax.sharding import PartitionSpec as P

SWEEPS = 3


KAPPA = 0.06
OMEGA = 0.8
AMPLITUDE = 40.0
ARCHIE = 20.0


def with_halo(shard, sides, width, top=None):
    for axis, dim in sides:
        devices, length = (lax.axis_size(axis), shard.shape[dim])
        last_member = devices if (axis != "grp" or top is None) else top
        up = [(i, i + 1) for i in range(last_member - 1)]
        down = [(j, i) for i, j in up]
        last = lax.slice_in_dim(shard, length - width, length, axis=dim)
        initial = lax.slice_in_dim(shard, 0, width, axis=dim)
        before = lax.ppermute(last, axis, up)
        after = lax.ppermute(initial, axis, down)
        shard = jnp.concatenate([before, shard, after], axis=dim)
    return shard


def faces_kernel(c_ref, v_ref, zs_up, zs_dn, xr, yc_ref, yu_ref):
    nzx, ny = c_ref.shape
    nz = xr.shape[1]
    nx = nzx // nz
    f32 = jnp.float32
    zs_up[0:2] = c_ref[nzx - 2 * nx : nzx].reshape(2, nx, ny)
    zs_dn[0:2] = c_ref[0 : 2 * nx].reshape(2, nx, ny)
    for d in range(3):
        zs_up[2 + d] = v_ref[d, nzx - nx : nzx].astype(f32)
        zs_dn[2 + d] = v_ref[d, 0:nx].astype(f32)
    for z in range(nz):
        base = z * nx
        xr[0, z : z + 1] = c_ref[base + nx - 2 : base + nx - 1]
        xr[1, z : z + 1] = c_ref[base + nx - 1 : base + nx]
        xr[5, z : z + 1] = c_ref[base : base + 1]
        xr[6, z : z + 1] = c_ref[base + 1 : base + 2]
        for d in range(3):
            top = v_ref[d, base + nx - 16 : base + nx].astype(f32)
            bottom = v_ref[d, base : base + 16].astype(f32)
            xr[2 + d, z : z + 1] = top[15:16]
            xr[7 + d, z : z + 1] = bottom[0:1]
    lane = lax.broadcasted_iota(jnp.int32, (8, ny), 1)
    row = lax.broadcasted_iota(jnp.int32, (8, ny), 0)
    pick_c = (
        ((row == 0) & (lane == ny - 2))
        | ((row == 1) & (lane == ny - 1))
        | ((row == 2) & (lane == 0))
        | ((row == 3) & (lane == 1))
    )
    pick_u = ((row == 0) & (lane == ny - 1)) | ((row == 1) & (lane == 0))
    nt = (((1,), (1,)), ((), ()))
    yc_ref[...] = lax.dot_general(
        pick_c.astype(f32), c_ref[...], nt, precision=lax.Precision.HIGHEST,
        preferred_element_type=f32,
    )
    for d in range(3):
        yu_ref[d] = lax.dot_general(
            pick_u.astype(jnp.bfloat16), v_ref[d], nt, preferred_element_type=f32
        )


def faces_call(c, velocity):
    nz, nx, ny = c.shape
    f32 = jnp.float32
    vmem = pl.BlockSpec(memory_space=pltpu.VMEM)
    return pl.pallas_call(
        faces_kernel,
        out_shape=(
            jax.ShapeDtypeStruct((5, nx, ny), f32),
            jax.ShapeDtypeStruct((5, nx, ny), f32),
            jax.ShapeDtypeStruct((10, nz, ny), f32),
            jax.ShapeDtypeStruct((8, nz * nx), f32),
            jax.ShapeDtypeStruct((3, 8, nz * nx), f32),
        ),
        in_specs=[vmem, vmem],
        out_specs=(vmem,) * 5,
        compiler_params=pltpu.CompilerParams(vmem_limit_bytes=32 * 1024 * 1024),
        cost_estimate=pl.CostEstimate(
            flops=2 * 32 * nz * nx * ny, transcendentals=0, bytes_accessed=10 * nz * nx * ny
        ),
    )(c.reshape(nz * nx, ny), velocity.reshape(3, nz * nx, ny))


def transport_halo(c, u, slabs):
    f32 = jnp.float32
    nz, nx, ny = c.shape
    zs_up, zs_dn, xr, ycols, ucols = faces_call(c, u)
    ycols = ycols.reshape(8, nz, nx)
    ucols = ucols.reshape(3, 8, nz, nx)

    def chain(axis, members):
        up = [(i, i + 1) for i in range(members - 1)]
        return up, [(j, i) for i, j in up]

    up, down = chain("grp", slabs)
    below = lax.ppermute(zs_up, "grp", up)
    above = lax.ppermute(zs_dn, "grp", down)
    zlo_c, zlo_u = below[:2], below[2:]
    zhi_c, zhi_u = above[:2], above[2:]

    def zext_c(rows, picked):
        return jnp.concatenate([zlo_c[:, rows], jnp.swapaxes(picked, 0, 1), zhi_c[:, rows]], 0)

    def zext_u(row, picked):
        core = jnp.concatenate([zlo_u[:, None, row], picked, zhi_u[:, None, row]], 1)
        return jnp.pad(core, ((0, 0), (1, 1), (0, 0)))

    rows = lax.axis_size("gx")
    up, down = chain("gx", rows)
    send_up = jnp.concatenate(
        [zext_c(slice(nx - 2, nx), xr[0:2]), jnp.swapaxes(zext_u(nx - 1, xr[2:5]), 0, 1)], 1
    )
    send_dn = jnp.concatenate(
        [zext_c(slice(0, 2), xr[5:7]), jnp.swapaxes(zext_u(0, xr[7:10]), 0, 1)], 1
    )
    bx = lax.ppermute(send_up, "gx", up)
    ax = lax.ppermute(send_dn, "gx", down)

    def xz_c(lanes, picked):
        core = jnp.concatenate([zlo_c[..., lanes], jnp.moveaxis(picked, 0, 2), zhi_c[..., lanes]], 0)
        return jnp.concatenate([bx[:, 0:2, lanes], core, ax[:, 0:2, lanes]], 1)

    def xz_u(lane, picked):
        core = jnp.pad(
            jnp.concatenate([zlo_u[:, None, :, lane], picked, zhi_u[:, None, :, lane]], 1),
            ((0, 0), (1, 1), (0, 0)),
        )
        lo = jnp.swapaxes(bx[:, 2:5, lane], 0, 1)[:, :, None]
        hi = jnp.swapaxes(ax[:, 2:5, lane], 0, 1)[:, :, None]
        zero = jnp.zeros_like(lo)
        return jnp.moveaxis(jnp.concatenate([zero, lo, core, hi, zero], 2), 0, 2)

    columns = lax.axis_size("gy")
    up, down = chain("gy", columns)
    by = lax.ppermute(
        jnp.concatenate([xz_c(slice(ny - 2, ny), ycols[0:2]), xz_u(ny - 1, ucols[:, 0])], 2), "gy", up
    )
    ay = lax.ppermute(
        jnp.concatenate([xz_c(slice(0, 2), ycols[2:4]), xz_u(0, ucols[:, 1])], 2), "gy", down
    )

    xc = jnp.concatenate([ax[:, 0:2], bx[:, 0:2]], 1)
    xu_hi = jnp.swapaxes(ax[1:-1, 2:5], 0, 1)[:, :, None]
    xu_lo = jnp.swapaxes(bx[1:-1, 2:5], 0, 1)[:, :, None]
    xu = jnp.concatenate([xu_hi, xu_lo], 2)
    speeds_y = jnp.stack([by[..., 2:5], ay[..., 2:5]], 3).reshape(nz + 4, nx + 4, 6)
    fill = jnp.zeros((nz + 4, nx + 4, 118), f32)
    yt = jnp.concatenate([ay[..., 0:2], speeds_y, fill, by[..., 0:2]], 2)
    return zlo_c, zhi_c, zlo_u, zhi_u, xc, xu, yt


def roll(values, shift, axis):
    return pltpu.roll(values, shift % values.shape[axis], axis)


def stencil(c, below, above, speeds):
    running = -6.0 * KAPPA * c
    for d in range(3):
        b, a, s = below[d], above[d], speeds[d]
        running = running + KAPPA * (b + a) - (
            jnp.maximum(s, 0.0) * (c - b) + jnp.minimum(s, 0.0) * (a - c)
        )
    return running


def transport_kernel(
    grid, place, weights, c_ref, v_ref, poro_ref, sat_ref, zlo_c, zhi_c, zlo_u, zhi_u,
    xc, xu, yt, adv_ref, part_ref, F, U, S, SG, H,
):
    nz, nx, ny = c_ref.shape
    wx, wy = F.shape[1], F.shape[2]
    f32 = jnp.float32
    pool_y = (
        lax.broadcasted_iota(jnp.int32, (ny, ny // 2), 0) // 2
        == lax.broadcasted_iota(jnp.int32, (ny, ny // 2), 1)
    ).astype(f32)
    F[0:2, 8 : 8 + nx, 0:ny] = zlo_c[...]
    F[nz + 2 : nz + 4, 8 : 8 + nx, 0:ny] = zhi_c[...]

    def put_c(z, carry):
        F[z + 2, 8 : 8 + nx, 0:ny] = c_ref[z]
        return carry

    lax.fori_loop(0, nz, put_c, 0)
    F[:, 6:8, 0:ny] = xc[:, 2:4]
    F[:, wx - 8 : wx - 6, 0:ny] = xc[:, 0:2]
    F[:, 6 : 6 + nx + 4, ny:wy] = yt[...]
    for d in range(3):
        U[d, 0, 8 : 8 + nx, 0:ny] = zlo_u[d]
        U[d, nz + 1, 8 : 8 + nx, 0:ny] = zhi_u[d]

        def put_u(z, carry, d=d):
            U[d, z + 1, 8 : 8 + nx, 0:ny] = v_ref[d, 0, z].astype(f32)
            return carry

        lax.fori_loop(0, nz, put_u, 0)
        U[d, :, 7:8, 0:ny] = xu[d, :, 1:2]
        U[d, :, wx - 8 : wx - 7, 0:ny] = xu[d, :, 0:1]
        U[d, :, 6 : 6 + nx + 4, ny:wy] = roll(yt[1 : nz + 3], -(3 + 2 * d), 2)

    total_z, total_x, total_y = grid
    gz0 = place[0] * nz - 1
    gx = place[1] * nx - 8 + lax.broadcasted_iota(jnp.int32, (wx, wy), 0)
    lane = lax.broadcasted_iota(jnp.int32, (wx, wy), 1)
    gy = place[2] * ny + jnp.where(lane < ny + (wy - ny) // 2, lane, lane - wy)
    plane = (gx >= 0) & (gx < total_x) & (gy >= 0) & (gy < total_y)

    def first(k, carry):
        c0 = F[k + 1]
        below = (F[k], roll(c0, 1, 0), roll(c0, 1, 1))
        above = (F[k + 2], roll(c0, -1, 0), roll(c0, -1, 1))
        speeds = (U[0, k], U[1, k], U[2, k])
        section = c0 + stencil(c0, below, above, speeds)
        z = gz0 + k
        keep = plane & (z >= 0) & (z < total_z)
        S[k] = jnp.where(keep, section, 0.0)
        return carry

    lax.fori_loop(0, nz + 2, first, 0)

    live = place[3] > 0

    def core(values):
        return values[8 : 8 + nx, 0:ny]

    def second(j, carry):
        s_mid = S[j + 1]
        s0 = core(s_mid)
        below = (core(S[j]), core(roll(s_mid, 1, 0)), core(roll(s_mid, 1, 1)))
        above = (core(S[j + 2]), core(roll(s_mid, -1, 0)), core(roll(s_mid, -1, 1)))
        speeds = tuple(v_ref[d, 0, j].astype(f32) for d in range(3))
        c0 = c_ref[j]
        adv = 0.5 * (c0 + s0 + stencil(s0, below, above, speeds))
        adv = jnp.where(live, adv, 0.0)
        adv_ref[0, j] = adv
        p = poro_ref[0, j].astype(f32)
        w = sat_ref[0, j].astype(f32)
        SG[pl.ds(pl.multiple_of(j * nx, nx), nx)] = ARCHIE * jnp.exp(adv) * p * p * w * w
        return carry

    lax.fori_loop(0, nz, second, 0)
    H[...] = jnp.dot(SG[...], pool_y, precision=lax.Precision.HIGHEST, preferred_element_type=f32)
    half_rows = nz * nx // 2
    coarse = H[pl.ds(0, half_rows, stride=2)] + H[pl.ds(1, half_rows, stride=2)]
    cx = nx // 2
    resist_layers = part_ref.shape[0]
    for e in range(resist_layers):
        total = jnp.zeros((cx, ny // 2), f32)
        for z in range(nz):
            total = total + weights[e, z] * coarse[z * cx : (z + 1) * cx]
        part_ref[e] = total


def transport_call(place, weights, c, velocity, porosity, saturation, *pieces, grid):
    nz, nx, ny = c.shape
    wx, wy = nx + 16, ny + 128
    resist_layers = weights.shape[0]
    vmem = pl.BlockSpec(memory_space=pltpu.VMEM)
    smem = pl.BlockSpec(memory_space=pltpu.SMEM)
    cells = nz * nx * ny
    return pl.pallas_call(
        functools.partial(transport_kernel, grid),
        out_shape=(
            jax.ShapeDtypeStruct((1, nz, nx, ny), jnp.float32),
            jax.ShapeDtypeStruct((resist_layers, nx // 2, ny // 2), jnp.float32),
        ),
        in_specs=[smem, smem] + [vmem] * 11,
        out_specs=(vmem, vmem),
        scratch_shapes=[
            pltpu.VMEM((nz + 4, wx, wy), jnp.float32),
            pltpu.VMEM((3, nz + 2, wx, wy), jnp.float32),
            pltpu.VMEM((nz + 2, wx, wy), jnp.float32),
            pltpu.VMEM((nz * nx, ny), jnp.float32),
            pltpu.VMEM((nz * nx, ny // 2), jnp.float32),
        ],
        compiler_params=pltpu.CompilerParams(vmem_limit_bytes=60 * 1024 * 1024),
        cost_estimate=pl.CostEstimate(
            flops=200 * cells, transcendentals=cells, bytes_accessed=40 * cells
        ),
    )(place, weights, c, velocity, porosity, saturation, *pieces)


def neighbours(padded, direction_index):
    leading = [slice(None)] * (padded.ndim - 3)
    middle = [slice(1, -1)] * 3
    below_slices = list(middle)
    below_slices[direction_index] = slice(0, -2)
    above_slices = list(middle)
    above_slices[direction_index] = slice(2, None)
    return (padded[tuple(leading + below_slices)], padded[tuple(leading + above_slices)])


def tendency(padded, speeds):
    center = padded[1:-1, 1:-1, 1:-1]
    running = -6.0 * KAPPA * center
    for direction_index in range(3):
        below_cells, above_cells = neighbours(padded, direction_index)
        speed_comp = speeds[direction_index]
        running = (
            running
            + KAPPA * (below_cells + above_cells)
            - (
                jnp.maximum(speed_comp, 0.0) * (center - below_cells)
                + jnp.minimum(speed_comp, 0.0) * (above_cells - center)
            )
        )
    return running


def inside(start, count, total):
    ids = start + jnp.arange(count, dtype=jnp.int32)
    return (ids >= 0) & (ids < total)


def plane_halo(values, depth):
    rows, columns = lax.axis_size("gx"), lax.axis_size("gy")
    d = depth

    def line(n, step):
        return [(i, i + step) for i in range(n) if 0 <= i + step < n]

    def flat(i, j):
        return i * columns + j

    def diagonal(di, dj):
        return [
            (flat(i, j), flat(i + di, j + dj))
            for i in range(rows)
            for j in range(columns)
            if 0 <= i + di < rows and 0 <= j + dj < columns
        ]

    both = ("gx", "gy")
    lo_x = lax.ppermute(values[:, -d:, :], "gx", line(rows, 1))
    hi_x = lax.ppermute(values[:, :d, :], "gx", line(rows, -1))
    lo_y = lax.ppermute(values[:, :, -d:], "gy", line(columns, 1))
    hi_y = lax.ppermute(values[:, :, :d], "gy", line(columns, -1))
    lo_lo = lax.ppermute(values[:, -d:, -d:], both, diagonal(1, 1))
    lo_hi = lax.ppermute(values[:, -d:, :d], both, diagonal(1, -1))
    hi_lo = lax.ppermute(values[:, :d, -d:], both, diagonal(-1, 1))
    hi_hi = lax.ppermute(values[:, :d, :d], both, diagonal(-1, -1))
    top = jnp.concatenate([lo_lo, lo_x, lo_hi], 2)
    middle = jnp.concatenate([lo_y, values, hi_y], 2)
    bottom = jnp.concatenate([hi_lo, hi_x, hi_hi], 2)
    return jnp.concatenate([top, middle, bottom], 1)


def grp_sum(partial, slabs):
    groups = lax.axis_size("grp")
    me = lax.axis_index("grp")
    received = {}
    for shift in range(1, groups):
        pairs = [(g, (g + shift) % groups) for g in range(slabs)]
        received[shift] = lax.ppermute(partial, "grp", pairs)
    total = None
    for owner in range(slabs):
        share = partial
        for shift in range(1, groups):
            share = jnp.where((me - shift) % groups == owner, received[shift], share)
        total = share if total is None else total + share
    return total


def on_device(conc, velocity, porosity, saturation, layer_counts, electrodes, init_potential):
    group_index = lax.axis_index("grp")
    row_index = lax.axis_index("gx")
    column_index = lax.axis_index("gy")
    groups = lax.axis_size("grp")
    rows = lax.axis_size("gx")
    columns = lax.axis_size("gy")
    active = group_index < 3
    field = conc[0]
    layers, tile_x, tile_y = field.shape
    slabs = 3
    speeds = velocity[:, 0]

    ends = jnp.cumsum(layer_counts)
    starts = ends - layer_counts
    layer_ids = group_index * layers + jnp.arange(layers, dtype=jnp.int32)
    member = (
        (layer_ids[None, :] >= starts[:, None]) & (layer_ids[None, :] < ends[:, None]) & active
    ).astype(jnp.float32)
    weights = member / (4.0 * layer_counts.astype(jnp.float32))[:, None]
    resist_layers = layer_counts.shape[0]
    coarse_x = tile_x // 2
    coarse_y = tile_y // 2

    pieces = transport_halo(field, velocity, slabs)
    place = jnp.stack([group_index, row_index, column_index, active.astype(jnp.int32)])
    advanced, partial_cond = transport_call(
        place, weights, field, velocity, porosity, saturation, *pieces,
        grid=(slabs * layers, rows * tile_x, columns * tile_y),
    )
    conductivity = grp_sum(partial_cond, slabs)

    grid_x = coarse_x * rows
    grid_y = coarse_y * columns
    depth = SWEEPS
    potential = lax.dynamic_slice_in_dim(init_potential, group_index, 1, 0)
    poles = lax.dynamic_slice_in_dim(electrodes, group_index, 1, 0)

    both = with_halo(jnp.concatenate([conductivity, potential[0]], axis=0), (("gx", 1), ("gy", 2)), depth)
    cond_wide = jnp.pad(both[:resist_layers], ((1, 1), (0, 0), (0, 0)))
    potential = both[None, resist_layers:]
    wide_x = coarse_x + 2 * depth
    wide_y = coarse_y + 2 * depth
    gx_ids = row_index * coarse_x - depth + jnp.arange(wide_x, dtype=jnp.int32)
    gy_ids = column_index * coarse_y - depth + jnp.arange(wide_y, dtype=jnp.int32)
    flat_ids = (
        jnp.arange(resist_layers, dtype=jnp.int32)[:, None, None] * (grid_x * grid_y)
        + gx_ids[None, :, None] * grid_y
        + gy_ids[None, None, :]
    )
    source_terms = AMPLITUDE * (
        (flat_ids[None] == poles[:, 0, None, None, None]).astype(jnp.float32)
        - (flat_ids[None] == poles[:, 1, None, None, None]).astype(jnp.float32)
    )
    on_grid = (
        ((gx_ids >= 0) & (gx_ids < grid_x))[:, None] & ((gy_ids >= 0) & (gy_ids < grid_y))[None, :]
    )

    for sweep_index in range(SWEEPS):
        m = sweep_index + 1
        nx, ny = wide_x - 2 * m, wide_y - 2 * m
        center_c = cond_wide[1:-1, m : m + nx, m : m + ny]
        faces = []
        diagonal = jnp.zeros_like(center_c)
        for d in range(3):
            if d == 0:
                lo = cond_wide[0:-2, m : m + nx, m : m + ny]
                hi = cond_wide[2:, m : m + nx, m : m + ny]
            elif d == 1:
                lo = cond_wide[1:-1, m - 1 : m - 1 + nx, m : m + ny]
                hi = cond_wide[1:-1, m + 1 : m + 1 + nx, m : m + ny]
            else:
                lo = cond_wide[1:-1, m : m + nx, m - 1 : m - 1 + ny]
                hi = cond_wide[1:-1, m : m + nx, m + 1 : m + 1 + ny]
            face_below = 0.5 * (center_c + lo)
            face_above = 0.5 * (center_c + hi)
            faces.append((face_below, face_above))
            diagonal = diagonal + face_below + face_above
        pot_z = jnp.pad(potential, ((0, 0), (1, 1), (0, 0), (0, 0)))
        pot_c = potential[:, :, 1:-1, 1:-1]
        coupled = jnp.zeros_like(pot_c)
        for d in range(3):
            if d == 0:
                lo = pot_z[:, 0:-2, 1:-1, 1:-1]
                hi = pot_z[:, 2:, 1:-1, 1:-1]
            elif d == 1:
                lo = potential[:, :, 0:-2, 1:-1]
                hi = potential[:, :, 2:, 1:-1]
            else:
                lo = potential[:, :, 1:-1, 0:-2]
                hi = potential[:, :, 1:-1, 2:]
            coupled = coupled + faces[d][0] * lo + faces[d][1] * hi
        applied = diagonal * pot_c - coupled
        rhs = source_terms[:, :, m : m + nx, m : m + ny]
        updated = pot_c + OMEGA * (rhs - applied) / diagonal
        potential = jnp.where(on_grid[m : m + nx, m : m + ny], updated, 0.0)

    return (advanced, conductivity, potential)


def solution(mesh):
    in_specs = (
        P("grp", None, "gx", "gy"),
        P(None, "grp", None, "gx", "gy"),
        P("grp", None, "gx", "gy"),
        P("grp", None, "gx", "gy"),
        P(),
        P(),
        P(None, None, "gx", "gy"),
    )
    out_specs = (P("grp", None, "gx", "gy"), P(None, "gx", "gy"), P("grp", None, "gx", "gy"))
    return jax.shard_map(
        on_device, mesh=mesh, in_specs=in_specs, out_specs=out_specs, check_vma=False
    )
```
